32 devices in a mesh: groups: 2 (over x), tm: 16 (over z, y, core).
Axes of the slice: x: 2, y: 2, z: 4, core: 2. Of those that a mesh axis runs over, the one named last changes fastest.
Arguments:
- observed: float32 [32, 128], P(('groups', 'tm')), parts along dimension 0, may hold values from -6 to 6
- obs_masks: int32 [32, 128], P(('groups', 'tm')), parts along dimension 0, may hold values 0 or 1
- decay_rates: float32 [256], P('groups'), parts along dimension 0, may hold values from 0.05 to 0.5
- noise_var: float32 [256], P('groups'), parts along dimension 0, may hold values from 0.05 to 0.5
- spatial_cov: float32 [256, 128], P('groups'), parts along dimension 0, may hold values from -1 to 4, as said below
Outputs:
- smooth_mean: float32 [32, 256], P(('groups', 'tm')), parts along dimension 0
- smooth_cov: float32 [32, 256, 256], P(('groups', 'tm')), parts along dimension 0
The draws below stay inside these ranges and needn't reach their ends.
There are 2 independent parts, one for each index of `groups`. The reference program is written for one: setup_inputs(seed, part) draws one part's arguments, and reference() takes and returns one part's arrays. A program takes and returns all parts, laid end to end along the dimension named above; each array names one. Nothing has to cross between parts.
Inputs may be any that keep to these rules, and one draw needn't show every extreme that they name: spatial_cov is symmetric, and each diagonal entry is positive and larger than the sum of the magnitudes of the other entries of its row.
All inputs are finite; a program needn't handle non-finite values. No bound on the sum of `obs_masks` on one device may be relied on, other than what follows from the above.
Results may differ from the reference program's by a relative error of at most 0.0003.
Values sent between devices are 32-bit elements; how exact they have to be, the bound alone decides.
No kernel may reach another device: no remote copies, remote signals or barrier semaphores. Data moves between devices by JAX's collectives and lax.ppermute only.
A program may use at most 128 MiB of HBM per device.

```python
import math
import jax
import jax.numpy as jnp
from jax import lax

POINTS = 128
STEPS = 16


def draw_spatial_cov(key, part):
    key_off = jax.random.fold_in(key, 11)
    key_diag = jax.random.fold_in(key, 23)
    uniform_draw = jax.random.uniform(key_off, (POINTS, POINTS), jnp.float32, -1.0, 1.0)
    symmetric = (uniform_draw + uniform_draw.T) * (0.45 / POINTS)
    diagonal_part = 1.0 + jax.random.uniform(key_diag, (POINTS,), jnp.float32)
    identity_mat = jnp.eye(POINTS, dtype=jnp.float32)
    return symmetric * (1.0 - identity_mat) + identity_mat * diagonal_part[None, :]


def place_ends(result, key, low, largest):
    extent = result.shape
    index_at = [jax.random.randint(jax.random.fold_in(key, axis), (), 0, extent[axis]) for axis in range(len(extent))]
    result = result.at[tuple(index_at)].set(low)
    longest = extent.index(max(extent))
    index_at[longest] = (index_at[longest] + 1) % extent[longest]
    return result.at[tuple(index_at)].set(largest)


def shard_levels(key, shape, shards, smallest, largest):
    gain = 1.0
    for position, blocks in shards:
        heights = jax.random.uniform(jax.random.fold_in(jax.random.fold_in(key, 6), position), (blocks,), jnp.float32, smallest / len(shards), largest / len(shards))
        gain = gain * jnp.repeat(jnp.exp(heights), shape[position] // blocks).reshape((-1,) + (1,) * (len(shape) - 1 - position))
    return gain


def noise(rng, extent, scale, bound, shards=(), kind=jnp.bfloat16):
    factor_of = shard_levels(rng, extent, shards, -0.22, 0.18) if shards else 1.0
    drawn = jax.random.normal(rng, extent, jnp.float32) * scale * factor_of
    return jnp.minimum(jnp.maximum(drawn, -bound), bound).astype(kind)


def setup_inputs(seed: int = 0, part: int = 0) -> dict:
    keys = jax.random.split(jax.random.key(seed), 6)
    part_splits = jax.random.split(jax.random.fold_in(keys[5], part), 6)
    return {
        "observed": noise(part_splits[0], (STEPS, POINTS), 1.0, 6.0, ((0, 16),), jnp.float32),
        "obs_masks": place_ends((jax.random.randint(part_splits[1], (STEPS, POINTS), 0, 4) < 3).astype(jnp.int32), jax.random.fold_in(part_splits[1], 1), 0, 1),
        "decay_rates": jnp.clip(jnp.exp(jax.random.uniform(part_splits[2], (POINTS,), jnp.float32, math.log(0.05), math.log(0.5))), 0.05, 0.5),
        "noise_var": jnp.clip(jnp.exp(jax.random.uniform(part_splits[3], (POINTS,), jnp.float32, math.log(0.05), math.log(0.5))), 0.05, 0.5),
        "spatial_cov": draw_spatial_cov(jax.random.fold_in(jax.random.fold_in(keys[5], part), 71), part),
    }


HIGHEST = lax.Precision.HIGHEST
JITTER = 0.001

def matmul_hi(left, right):
    return jnp.matmul(left, right, precision=HIGHEST)

def swap_last(matrix):
    return jnp.swapaxes(matrix, -1, -2)

def apply_trans(transit, matrix):
    points = transit.shape[1]
    upper_half = matrix[..., :points, :]
    lower_half = matrix[..., points:, :]
    return jnp.concatenate([transit[0][:, None] * upper_half + transit[1][:, None] * lower_half, transit[2][:, None] * upper_half + transit[3][:, None] * lower_half], axis=-2)

def apply_trans_t(transit, matrix):
    points = transit.shape[1]
    upper_half = matrix[..., :points, :]
    lower_half = matrix[..., points:, :]
    return jnp.concatenate([transit[0][:, None] * upper_half + transit[2][:, None] * lower_half, transit[1][:, None] * upper_half + transit[3][:, None] * lower_half], axis=-2)

def spd_inverse(matrix):
    factor = jnp.linalg.cholesky(matrix)
    identity_mat = jnp.broadcast_to(jnp.eye(matrix.shape[-1], dtype=jnp.float32), matrix.shape)
    low_inverse = lax.linalg.triangular_solve(factor, identity_mat, left_side=True, lower=True)
    return matmul_hi(swap_last(low_inverse), low_inverse)

def build_model(decay_rates, spatial_cov):
    decay_one = jnp.exp(-decay_rates)
    transit = jnp.stack([decay_one * (1.0 + decay_rates), decay_one * decay_rates, -decay_one * decay_rates, decay_one * (1.0 - decay_rates)])
    decay_two = jnp.exp(-2.0 * decay_rates)
    var_ff = 1.0 - decay_two * (1.0 + 2.0 * decay_rates + 2.0 * decay_rates * decay_rates)
    cov_fg = 2.0 * decay_rates * decay_rates * decay_two
    var_gg = 1.0 - decay_two * (1.0 - 2.0 * decay_rates + 2.0 * decay_rates * decay_rates)
    fac_ff = jnp.sqrt(var_ff)
    fac_gf = cov_fg / fac_ff
    fac_gg = jnp.sqrt(var_gg - fac_gf * fac_gf)

    def scaled(left, right):
        return left[:, None] * spatial_cov * right[None, :]
    zero_block = jnp.zeros_like(spatial_cov)
    process = jnp.block([[scaled(fac_ff, fac_ff), scaled(fac_ff, fac_gf)], [scaled(fac_gf, fac_ff), scaled(fac_gf, fac_gf) + scaled(fac_gg, fac_gg)]])
    process = process + JITTER * jnp.eye(2 * spatial_cov.shape[0], dtype=jnp.float32)
    prior = jnp.block([[spatial_cov, zero_block], [zero_block, spatial_cov]])
    return (transit, process, prior)

def make_elements(observed, obs_masks, first_flag, model_parts, noise_var):
    transit, process, prior = model_parts
    width = 2 * observed.shape[-1]
    obs_prec = obs_masks.astype(jnp.float32) / noise_var
    prec_root = jnp.sqrt(jnp.concatenate([obs_prec, jnp.zeros_like(obs_prec)], axis=-1))
    obs_full = jnp.concatenate([observed, jnp.zeros_like(observed)], axis=-1)
    identity_mat = jnp.eye(width, dtype=jnp.float32)
    cov_pred = jnp.where(first_flag[:, None, None], prior, process)
    normal = identity_mat + prec_root[:, :, None] * cov_pred * prec_root[:, None, :]
    weight = prec_root[:, :, None] * spd_inverse(normal) * prec_root[:, None, :]
    cov_weight = matmul_hi(cov_pred, weight)
    cov_filt = cov_pred - matmul_hi(cov_weight, cov_pred)
    weight_obs = matmul_hi(weight, obs_full[..., None])
    mean_filt = matmul_hi(cov_pred, weight_obs)[..., 0]
    trans_a = swap_last(apply_trans_t(transit, swap_last(identity_mat - cov_weight)))
    half_info = apply_trans_t(transit, weight)
    info_j = apply_trans_t(transit, swap_last(half_info))
    info_eta = apply_trans_t(transit, weight_obs)[..., 0]
    keep_mask = 1.0 - first_flag.astype(jnp.float32)
    flags = jnp.ones(observed.shape[0], dtype=jnp.float32)
    return (trans_a * keep_mask[:, None, None], mean_filt, cov_filt, info_j * keep_mask[:, None, None], info_eta * keep_mask[:, None], flags)

def cov_gain(cov_early, flag_early, info_later):
    identity_mat = jnp.eye(cov_early.shape[-1], dtype=jnp.float32)
    safe_cov = jnp.where(flag_early > 0, cov_early, identity_mat)
    factor = jnp.linalg.cholesky(safe_cov)
    middle = identity_mat + matmul_hi(swap_last(factor), matmul_hi(info_later, factor))
    return matmul_hi(matmul_hi(factor, spd_inverse(middle)), swap_last(factor))

def combine_full(earlier, later_el):
    trans_e, mean_e, cov_e, info_e, eta_e, flag_e = earlier
    trans_l, mean_l, cov_l, info_l, eta_l, flag_l = later_el
    identity_mat = jnp.eye(cov_e.shape[-1], dtype=jnp.float32)
    gain_cov = cov_gain(cov_e, flag_e, info_l)
    solve_x = identity_mat - matmul_hi(gain_cov, info_l)
    x_trans = matmul_hi(solve_x, trans_e)
    trans_new = matmul_hi(trans_l, x_trans)
    shifted = mean_e + matmul_hi(cov_e, eta_l)
    mean_new = matmul_hi(trans_l, matmul_hi(solve_x, shifted)) + mean_l
    cov_new = matmul_hi(matmul_hi(trans_l, gain_cov), swap_last(trans_l)) + cov_l
    eta_new = matmul_hi(swap_last(x_trans), eta_l - matmul_hi(info_l, mean_e)) + eta_e
    info_new = matmul_hi(swap_last(x_trans), matmul_hi(info_l, trans_e)) + info_e
    joined = (trans_new, mean_new, cov_new, info_new, eta_new, jnp.maximum(flag_e, flag_l))
    return jax.tree.map(lambda leaf_e, leaf_l, leaf_j: jnp.where(flag_l > 0, jnp.where(flag_e > 0, leaf_j, leaf_l), leaf_e), earlier, later_el, joined)

def smoother_elements(means, covs, last_flag, transit, process):
    forward_cov = apply_trans(transit, covs)
    predicted = apply_trans(transit, swap_last(forward_cov)) + process
    factor = jnp.linalg.cholesky(predicted)
    half_solve = lax.linalg.triangular_solve(factor, forward_cov, left_side=True, lower=True)
    gain_t = lax.linalg.triangular_solve(factor, half_solve, left_side=True, lower=True, transpose_a=True)
    gains = swap_last(gain_t) * (1.0 - last_flag.astype(jnp.float32))[:, None, None]
    forward_mean = apply_trans(transit, means[..., None])
    shift_means = means - matmul_hi(gains, forward_mean)[..., 0]
    shift_covs = covs - matmul_hi(gains, forward_cov)
    return (gains, shift_means, shift_covs)

def smooth_join(lower_el, higher_el):
    gain_a, mean_a, cov_a = lower_el
    gain_b, mean_b, cov_b = higher_el
    return (matmul_hi(gain_a, gain_b), matmul_hi(gain_a, mean_b) + mean_a, matmul_hi(matmul_hi(gain_a, cov_b), swap_last(gain_a)) + cov_a)

def reference(observed, obs_masks, decay_rates, noise_var, spatial_cov):
    model_parts = build_model(decay_rates, spatial_cov)
    transit, process, prior = model_parts
    steps_total = observed.shape[0]
    positions = jnp.arange(steps_total)
    elements = make_elements(observed, obs_masks, positions == 0, model_parts, noise_var)
    first_el = jax.tree.map(lambda leaf: leaf[0], elements)
    rest_els = jax.tree.map(lambda leaf: leaf[1:], elements)

    def forward(running, element):
        joined = combine_full(running, element)
        return (joined, (joined[1], joined[2]))
    _, (means_tail, covs_tail) = lax.scan(forward, first_el, rest_els)
    means = jnp.concatenate([first_el[1][None], means_tail], axis=0)
    covs = jnp.concatenate([first_el[2][None], covs_tail], axis=0)
    smooth = smoother_elements(means, covs, positions == steps_total - 1, transit, process)
    last_el = jax.tree.map(lambda leaf: leaf[-1], smooth)
    front_els = jax.tree.map(lambda leaf: leaf[:-1], smooth)

    def backward(running, element):
        joined = smooth_join(element, running)
        return (joined, (joined[1], joined[2]))
    _, (mean_front, cov_front) = lax.scan(backward, last_el, front_els, reverse=True)
    smooth_mean = jnp.concatenate([mean_front, last_el[1][None]], axis=0)
    smooth_cov = jnp.concatenate([cov_front, last_el[2][None]], axis=0)
    return (smooth_mean, smooth_cov)
```

```python
import jax
import jax.numpy as jnp
from jax import lax
from jax.sharding import PartitionSpec as P

HIGHEST = lax.Precision.HIGHEST
JITTER = 0.001


def matmul_hi(left, right):
    return jnp.matmul(left, right, precision=HIGHEST)


def swap_last(matrix):
    return jnp.swapaxes(matrix, -1, -2)


def apply_trans(transit, matrix):
    points = transit.shape[1]
    upper_half = matrix[..., :points, :]
    lower_half = matrix[..., points:, :]
    return jnp.concatenate(
        [
            transit[0][:, None] * upper_half + transit[1][:, None] * lower_half,
            transit[2][:, None] * upper_half + transit[3][:, None] * lower_half,
        ],
        axis=-2,
    )


def build_model(decay_rates, spatial_cov):
    decay_one = jnp.exp(-decay_rates)
    transit = jnp.stack(
        [
            decay_one * (1.0 + decay_rates),
            decay_one * decay_rates,
            -decay_one * decay_rates,
            decay_one * (1.0 - decay_rates),
        ]
    )
    decay_two = jnp.exp(-2.0 * decay_rates)
    var_ff = 1.0 - decay_two * (1.0 + 2.0 * decay_rates + 2.0 * decay_rates * decay_rates)
    cov_fg = 2.0 * decay_rates * decay_rates * decay_two
    var_gg = 1.0 - decay_two * (1.0 - 2.0 * decay_rates + 2.0 * decay_rates * decay_rates)
    fac_ff = jnp.sqrt(var_ff)
    fac_gf = cov_fg / fac_ff
    fac_gg = jnp.sqrt(var_gg - fac_gf * fac_gf)

    def scaled(left, right):
        return left[:, None] * spatial_cov * right[None, :]

    zero_block = jnp.zeros_like(spatial_cov)
    process = jnp.block(
        [
            [scaled(fac_ff, fac_ff), scaled(fac_ff, fac_gf)],
            [scaled(fac_gf, fac_ff), scaled(fac_gf, fac_gf) + scaled(fac_gg, fac_gg)],
        ]
    )
    process = process + JITTER * jnp.eye(2 * spatial_cov.shape[0], dtype=jnp.float32)
    prior = jnp.block([[spatial_cov, zero_block], [zero_block, spatial_cov]])
    return (transit, process, prior)


def predict(transit, process, mean, cov):
    forward_cov = apply_trans(transit, cov)
    cov_pred = apply_trans(transit, swap_last(forward_cov)) + process
    mean_pred = apply_trans(transit, mean[:, None])[:, 0]
    return mean_pred, cov_pred


def kalman_update(mean_pred, cov_pred, obs, root):
    points = obs.shape[-1]
    normal = jnp.eye(points, dtype=jnp.float32) + root[:, None] * cov_pred[:points, :points] * root[None, :]
    factor = jnp.linalg.cholesky(normal)
    innovation = root * (obs - mean_pred[:points])
    rhs = jnp.concatenate([root[:, None] * cov_pred[:points, :], innovation[:, None]], axis=1)
    half = lax.linalg.triangular_solve(factor, rhs, left_side=True, lower=True)
    gain_half = half[:, :-1]
    cov_new = cov_pred - matmul_hi(swap_last(gain_half), gain_half)
    mean_new = mean_pred + matmul_hi(swap_last(gain_half), half[:, -1])
    return mean_new, cov_new


def smoother_elements(means, covs, last_flag, transit, process):
    forward_cov = apply_trans(transit, covs)
    predicted = apply_trans(transit, swap_last(forward_cov)) + process
    factor = jnp.linalg.cholesky(predicted)
    half_solve = lax.linalg.triangular_solve(factor, forward_cov, left_side=True, lower=True)
    gain_t = lax.linalg.triangular_solve(
        factor, half_solve, left_side=True, lower=True, transpose_a=True
    )
    gains = swap_last(gain_t) * (1.0 - last_flag.astype(jnp.float32))[:, None, None]
    forward_mean = apply_trans(transit, means[..., None])
    shift_means = means - matmul_hi(gains, forward_mean)[..., 0]
    shift_covs = covs - matmul_hi(gains, forward_cov)
    return (gains, shift_means, shift_covs)


def smooth_join(lower_el, higher_el):
    gain_a, mean_a, cov_a = lower_el
    gain_b, mean_b, cov_b = higher_el
    return (
        matmul_hi(gain_a, gain_b),
        matmul_hi(gain_a, mean_b[..., None])[..., 0] + mean_a,
        matmul_hi(matmul_hi(gain_a, cov_b), swap_last(gain_a)) + cov_a,
    )


def shards(observed, obs_masks, decay_rates, noise_var, spatial_cov):
    transit, process, prior = build_model(decay_rates, spatial_cov)
    local_steps, points = observed.shape
    width = 2 * points
    position = lax.axis_index("tm")
    tm_count = lax.axis_size("tm")
    total_steps = tm_count * local_steps

    root_local = jnp.sqrt(obs_masks.astype(jnp.float32) / noise_var)
    packed = jnp.stack([observed, root_local], axis=1)
    gathered = lax.all_gather(packed, "tm", tiled=True)
    obs_all = gathered[:, 0]
    root_all = gathered[:, 1]

    mean_first, cov_first = kalman_update(
        jnp.zeros((width,), jnp.float32), prior, obs_all[0], root_all[0]
    )
    last_local = position * local_steps + (local_steps - 1)

    def filter_step(step, mean, cov):
        mean_pred, cov_pred = predict(transit, process, mean, cov)
        obs_now = lax.dynamic_index_in_dim(obs_all, step, keepdims=False)
        root_now = lax.dynamic_index_in_dim(root_all, step, keepdims=False)
        return kalman_update(mean_pred, cov_pred, obs_now, root_now)

    if local_steps == 1:

        def body(step, carry):
            return filter_step(step, carry[0], carry[1])

        mean_last, cov_last = lax.fori_loop(1, last_local + 1, body, (mean_first, cov_first))
        means = mean_last[None]
        covs = cov_last[None]
    else:
        mean_buf = jnp.zeros((local_steps, width), jnp.float32).at[0].set(mean_first)
        cov_buf = jnp.zeros((local_steps, width, width), jnp.float32).at[0].set(cov_first)

        def body(step, carry):
            mean, cov, mean_buf, cov_buf = carry
            mean, cov = filter_step(step, mean, cov)
            slot = step % local_steps
            mean_buf = lax.dynamic_update_index_in_dim(mean_buf, mean, slot, 0)
            cov_buf = lax.dynamic_update_index_in_dim(cov_buf, cov, slot, 0)
            return (mean, cov, mean_buf, cov_buf)

        _, _, means, covs = lax.fori_loop(
            1, last_local + 1, body, (mean_first, cov_first, mean_buf, cov_buf)
        )

    global_step = position * local_steps + jnp.arange(local_steps)
    last_flag = global_step == total_steps - 1
    if local_steps == 1:

        def compute_elements(operand):
            return smoother_elements(operand[0], operand[1], last_flag, transit, process)

        def final_elements(operand):
            return (jnp.zeros_like(operand[1]), operand[0], operand[1])

        smooth = lax.cond(position == tm_count - 1, final_elements, compute_elements, (means, covs))
    else:
        smooth = smoother_elements(means, covs, last_flag, transit, process)

    if local_steps > 1:
        last_el = jax.tree.map(lambda leaf: leaf[-1], smooth)
        front_els = jax.tree.map(lambda leaf: leaf[:-1], smooth)

        def backward(running, element):
            joined = smooth_join(element, running)
            return (joined, joined)

        _, head_els = lax.scan(backward, last_el, front_els, reverse=True)
        suffixes = jax.tree.map(
            lambda head_leaf, last_leaf: jnp.concatenate([head_leaf, last_leaf[None]], axis=0),
            head_els,
            last_el,
        )
        block_total = jax.tree.map(lambda leaf: leaf[0], suffixes)
    else:
        block_total = jax.tree.map(lambda leaf: leaf[0], smooth)

    running = block_total
    shift = 1
    while shift < tm_count:
        pairs = [(source, source - shift) for source in range(shift, tm_count)]
        received = lax.ppermute(running, "tm", pairs)
        running = smooth_join(running, received)
        shift *= 2

    if local_steps == 1:
        return (running[1][None], running[2][None])
    pairs = [(source, source - 1) for source in range(1, tm_count)]
    after_mine = lax.ppermute(running, "tm", pairs)
    gains, shift_means, shift_covs = suffixes
    smooth_mean = matmul_hi(gains, after_mine[1][:, None])[..., 0] + shift_means
    smooth_cov = matmul_hi(matmul_hi(gains, after_mine[2]), swap_last(gains)) + shift_covs
    return (smooth_mean, smooth_cov)


def solution(mesh):
    placed = (
        P(("groups", "tm"), None),
        P(("groups", "tm"), None),
        P("groups"),
        P("groups"),
        P("groups", None),
    )
    return jax.shard_map(
        shards,
        mesh=mesh,
        in_specs=placed,
        out_specs=(P(("groups", "tm"), None), P(("groups", "tm"), None, None)),
        check_vma=False,
    )
```

```python
import jax
import jax.numpy as jnp
from jax import lax
from jax.experimental import pallas as pl
from jax.experimental.pallas import tpu as pltpu
from jax.sharding import PartitionSpec as P

HIGHEST = lax.Precision.HIGHEST
JITTER = 0.001
PANEL = 32


def _sweep_kernel(a_ref, o_ref):
    n = a_ref.shape[0]
    o_ref[...] = a_ref[...]
    sub = lax.broadcasted_iota(jnp.int32, (PANEL, n), 0)
    lane = lax.broadcasted_iota(jnp.int32, (PANEL, n), 1)
    sub_col = lax.broadcasted_iota(jnp.int32, (PANEL, 1), 0)
    lane_full = lax.broadcasted_iota(jnp.int32, (n, n), 1)
    for blk in range(n // PANEL):
        base = blk * PANEL
        orig = o_ref[base:base + PANEL, :]
        panel = orig
        for t in range(PANEL):
            is_row = sub == t
            is_col = lane == base + t
            colv = jnp.sum(jnp.where(is_col, panel, 0.0), axis=1, keepdims=True)
            rowv = jnp.sum(jnp.where(is_row, panel, 0.0), axis=0, keepdims=True)
            pivot = jnp.sum(jnp.where(sub_col == t, colv, 0.0), axis=0, keepdims=True)
            inv = 1.0 / pivot
            scaled_row = rowv * inv
            panel = jnp.where(
                is_row,
                jnp.where(is_col, -inv, scaled_row),
                jnp.where(is_col, colv * inv, panel - colv * scaled_row),
            )
        full = o_ref[...]
        update = lax.dot_general(
            orig, panel, (((0,), (0,)), ((), ())), precision=HIGHEST,
            preferred_element_type=jnp.float32,
        )
        in_block = (lane_full >= base) & (lane_full < base + PANEL)
        o_ref[...] = jnp.where(in_block, 0.0, full) - update
        o_ref[base:base + PANEL, :] = panel


def neg_inverse(matrix):
    size = matrix.shape[-1]
    return pl.pallas_call(
        _sweep_kernel,
        out_shape=jax.ShapeDtypeStruct((size, size), jnp.float32),
        in_specs=[pl.BlockSpec(memory_space=pltpu.VMEM)],
        out_specs=pl.BlockSpec(memory_space=pltpu.VMEM),
    )(matrix)


def matmul_hi(left, right):
    return jnp.matmul(left, right, precision=HIGHEST)


def swap_last(matrix):
    return jnp.swapaxes(matrix, -1, -2)


def apply_trans(transit, matrix):
    points = transit.shape[1]
    upper_half = matrix[..., :points, :]
    lower_half = matrix[..., points:, :]
    return jnp.concatenate(
        [
            transit[0][:, None] * upper_half + transit[1][:, None] * lower_half,
            transit[2][:, None] * upper_half + transit[3][:, None] * lower_half,
        ],
        axis=-2,
    )


def build_model(decay_rates, spatial_cov):
    decay_one = jnp.exp(-decay_rates)
    transit = jnp.stack(
        [
            decay_one * (1.0 + decay_rates),
            decay_one * decay_rates,
            -decay_one * decay_rates,
            decay_one * (1.0 - decay_rates),
        ]
    )
    decay_two = jnp.exp(-2.0 * decay_rates)
    var_ff = 1.0 - decay_two * (1.0 + 2.0 * decay_rates + 2.0 * decay_rates * decay_rates)
    cov_fg = 2.0 * decay_rates * decay_rates * decay_two
    var_gg = 1.0 - decay_two * (1.0 - 2.0 * decay_rates + 2.0 * decay_rates * decay_rates)
    fac_ff = jnp.sqrt(var_ff)
    fac_gf = cov_fg / fac_ff
    fac_gg = jnp.sqrt(var_gg - fac_gf * fac_gf)

    def scaled(left, right):
        return left[:, None] * spatial_cov * right[None, :]

    zero_block = jnp.zeros_like(spatial_cov)
    process = jnp.block(
        [
            [scaled(fac_ff, fac_ff), scaled(fac_ff, fac_gf)],
            [scaled(fac_gf, fac_ff), scaled(fac_gf, fac_gf) + scaled(fac_gg, fac_gg)],
        ]
    )
    process = process + JITTER * jnp.eye(2 * spatial_cov.shape[0], dtype=jnp.float32)
    prior = jnp.block([[spatial_cov, zero_block], [zero_block, spatial_cov]])
    return (transit, process, prior)


def predict(transit, process, mean, cov):
    forward_cov = apply_trans(transit, cov)
    cov_pred = apply_trans(transit, swap_last(forward_cov)) + process
    mean_pred = apply_trans(transit, mean[:, None])[:, 0]
    return mean_pred, cov_pred


def kalman_update(mean_pred, cov_pred, obs, root):
    points = obs.shape[-1]
    normal = jnp.eye(points, dtype=jnp.float32) + root[:, None] * cov_pred[:points, :points] * root[None, :]
    neg_inv = neg_inverse(normal)
    innovation = root * (obs - mean_pred[:points])
    scaled = root[:, None] * cov_pred[:points, :]
    rhs = jnp.concatenate([scaled, innovation[:, None]], axis=1)
    solved = matmul_hi(neg_inv, rhs)
    correction = matmul_hi(swap_last(scaled), solved)
    cov_new = cov_pred + correction[:, :-1]
    mean_new = mean_pred - correction[:, -1]
    return mean_new, cov_new


def smoother_elements(means, covs, last_flag, transit, process):
    forward_cov = apply_trans(transit, covs)
    predicted = apply_trans(transit, swap_last(forward_cov)) + process
    neg_inv = jax.vmap(neg_inverse)(predicted)
    gains = -matmul_hi(swap_last(forward_cov), neg_inv)
    gains = gains * (1.0 - last_flag.astype(jnp.float32))[:, None, None]
    forward_mean = apply_trans(transit, means[..., None])
    shift_means = means - matmul_hi(gains, forward_mean)[..., 0]
    shift_covs = covs - matmul_hi(gains, forward_cov)
    return (gains, shift_means, shift_covs)


def smooth_join(lower_el, higher_el):
    gain_a, mean_a, cov_a = lower_el
    gain_b, mean_b, cov_b = higher_el
    return (
        matmul_hi(gain_a, gain_b),
        matmul_hi(gain_a, mean_b[..., None])[..., 0] + mean_a,
        matmul_hi(matmul_hi(gain_a, cov_b), swap_last(gain_a)) + cov_a,
    )


def shards(observed, obs_masks, decay_rates, noise_var, spatial_cov):
    transit, process, prior = build_model(decay_rates, spatial_cov)
    local_steps, points = observed.shape
    width = 2 * points
    position = lax.axis_index("tm")
    tm_count = lax.axis_size("tm")
    total_steps = tm_count * local_steps

    root_local = jnp.sqrt(obs_masks.astype(jnp.float32) / noise_var)
    packed = jnp.stack([observed, root_local], axis=1)
    gathered = lax.all_gather(packed, "tm", tiled=True)
    obs_all = gathered[:, 0]
    root_all = gathered[:, 1]

    mean_first, cov_first = kalman_update(
        jnp.zeros((width,), jnp.float32), prior, obs_all[0], root_all[0]
    )
    last_local = position * local_steps + (local_steps - 1)

    def filter_step(step, mean, cov):
        mean_pred, cov_pred = predict(transit, process, mean, cov)
        obs_now = lax.dynamic_index_in_dim(obs_all, step, keepdims=False)
        root_now = lax.dynamic_index_in_dim(root_all, step, keepdims=False)
        return kalman_update(mean_pred, cov_pred, obs_now, root_now)

    if local_steps == 1:

        def body(step, carry):
            return filter_step(step, carry[0], carry[1])

        mean_last, cov_last = lax.fori_loop(1, last_local + 1, body, (mean_first, cov_first))
        means = mean_last[None]
        covs = cov_last[None]
    else:
        mean_buf = jnp.zeros((local_steps, width), jnp.float32).at[0].set(mean_first)
        cov_buf = jnp.zeros((local_steps, width, width), jnp.float32).at[0].set(cov_first)

        def body(step, carry):
            mean, cov, mean_buf, cov_buf = carry
            mean, cov = filter_step(step, mean, cov)
            slot = step % local_steps
            mean_buf = lax.dynamic_update_index_in_dim(mean_buf, mean, slot, 0)
            cov_buf = lax.dynamic_update_index_in_dim(cov_buf, cov, slot, 0)
            return (mean, cov, mean_buf, cov_buf)

        _, _, means, covs = lax.fori_loop(
            1, last_local + 1, body, (mean_first, cov_first, mean_buf, cov_buf)
        )

    global_step = position * local_steps + jnp.arange(local_steps)
    last_flag = global_step == total_steps - 1
    if local_steps == 1:

        def compute_elements(operand):
            return smoother_elements(operand[0], operand[1], last_flag, transit, process)

        def final_elements(operand):
            return (jnp.zeros_like(operand[1]), operand[0], operand[1])

        smooth = lax.cond(position == tm_count - 1, final_elements, compute_elements, (means, covs))
    else:
        smooth = smoother_elements(means, covs, last_flag, transit, process)

    if local_steps > 1:
        last_el = jax.tree.map(lambda leaf: leaf[-1], smooth)
        front_els = jax.tree.map(lambda leaf: leaf[:-1], smooth)

        def backward(running, element):
            joined = smooth_join(element, running)
            return (joined, joined)

        _, head_els = lax.scan(backward, last_el, front_els, reverse=True)
        suffixes = jax.tree.map(
            lambda head_leaf, last_leaf: jnp.concatenate([head_leaf, last_leaf[None]], axis=0),
            head_els,
            last_el,
        )
        block_total = jax.tree.map(lambda leaf: leaf[0], suffixes)
    else:
        block_total = jax.tree.map(lambda leaf: leaf[0], smooth)

    running = block_total
    shift = 1
    while shift < tm_count:
        pairs = [(source, source - shift) for source in range(shift, tm_count)]
        received = lax.ppermute(running, "tm", pairs)
        running = smooth_join(running, received)
        shift *= 2

    if local_steps == 1:
        return (running[1][None], running[2][None])
    pairs = [(source, source - 1) for source in range(1, tm_count)]
    after_mine = lax.ppermute(running, "tm", pairs)
    gains, shift_means, shift_covs = suffixes
    smooth_mean = matmul_hi(gains, after_mine[1][:, None])[..., 0] + shift_means
    smooth_cov = matmul_hi(matmul_hi(gains, after_mine[2]), swap_last(gains)) + shift_covs
    return (smooth_mean, smooth_cov)


def solution(mesh):
    placed = (
        P(("groups", "tm"), None),
        P(("groups", "tm"), None),
        P("groups"),
        P("groups"),
        P("groups", None),
    )
    return jax.shard_map(
        shards,
        mesh=mesh,
        in_specs=placed,
        out_specs=(P(("groups", "tm"), None), P(("groups", "tm"), None, None)),
        check_vma=False,
    )
```

```python
import jax
import jax.numpy as jnp
from jax import lax
from jax.experimental import pallas as pl
from jax.experimental.pallas import tpu as pltpu
from jax.sharding import PartitionSpec as P

HIGHEST = lax.Precision.HIGHEST
JITTER = 0.001
PANEL = 32


def _sweep_kernel(a_ref, o_ref):
    o_ref[...] = a_ref[...]
    _sweep_in_place(o_ref)


def _sweep_in_place(o_ref):
    n = o_ref.shape[0]
    sub = lax.broadcasted_iota(jnp.int32, (PANEL, n), 0)
    lane = lax.broadcasted_iota(jnp.int32, (PANEL, n), 1)
    sub_col = lax.broadcasted_iota(jnp.int32, (PANEL, 1), 0)
    lane_full = lax.broadcasted_iota(jnp.int32, (n, n), 1)
    for blk in range(n // PANEL):
        base = blk * PANEL
        orig = o_ref[base:base + PANEL, :]
        panel = orig
        for t in range(PANEL):
            is_row = sub == t
            is_col = lane == base + t
            colv = jnp.sum(jnp.where(is_col, panel, 0.0), axis=1, keepdims=True)
            rowv = jnp.sum(jnp.where(is_row, panel, 0.0), axis=0, keepdims=True)
            pivot = jnp.sum(jnp.where(sub_col == t, colv, 0.0), axis=0, keepdims=True)
            inv = 1.0 / pivot
            scaled_row = rowv * inv
            panel = jnp.where(
                is_row,
                jnp.where(is_col, -inv, scaled_row),
                jnp.where(is_col, colv * inv, panel - colv * scaled_row),
            )
        full = o_ref[...]
        update = lax.dot_general(
            orig, panel, (((0,), (0,)), ((), ())), precision=HIGHEST,
            preferred_element_type=jnp.float32,
        )
        in_block = (lane_full >= base) & (lane_full < base + PANEL)
        o_ref[...] = jnp.where(in_block, 0.0, full) - update
        o_ref[base:base + PANEL, :] = panel


def neg_inverse(matrix):
    size = matrix.shape[-1]
    return pl.pallas_call(
        _sweep_kernel,
        out_shape=jax.ShapeDtypeStruct((size, size), jnp.float32),
        in_specs=[pl.BlockSpec(memory_space=pltpu.VMEM)],
        out_specs=pl.BlockSpec(memory_space=pltpu.VMEM),
    )(matrix)


def _filter_kernel(
    count_ref, obs_ref, root_row_ref, root_col_ref, trans_row_ref, trans_col_ref, process_ref,
    prior_ref, mean_ref, cov_ref, pred_ref, normal_ref,
):
    points = obs_ref.shape[1]
    eye = (
        lax.broadcasted_iota(jnp.int32, (points, points), 0)
        == lax.broadcasted_iota(jnp.int32, (points, points), 1)
    ).astype(jnp.float32)
    cov_ref[...] = prior_ref[...]
    a_col, b_col, c_col, d_col = (trans_col_ref[i] for i in range(4))
    a_row, b_row, c_row, d_row = (trans_row_ref[i:i + 1, :] for i in range(4))

    def step(t, mean):
        first = t == 0
        top = cov_ref[:points, :]
        bottom = cov_ref[points:, :]
        for rows, left_w, right_w in ((slice(0, points), a_col, b_col), (slice(points, None), c_col, d_col)):
            forward = left_w * top + right_w * bottom
            f_left = forward[:, :points]
            f_right = forward[:, points:]
            pred_ref[rows, :points] = f_left * a_row + f_right * b_row
            pred_ref[rows, points:] = f_left * c_row + f_right * d_row
        cov_pred = jnp.where(first, prior_ref[...], pred_ref[...] + process_ref[...])
        m_top = mean[:, :points]
        m_bottom = mean[:, points:]
        mean_fwd = jnp.concatenate(
            [a_row * m_top + b_row * m_bottom, c_row * m_top + d_row * m_bottom], axis=1
        )
        mean_pred = jnp.where(first, 0.0, mean_fwd)
        r_col = root_col_ref[t]
        r_row = root_row_ref[pl.ds(t, 1), :]
        obs_row = obs_ref[pl.ds(t, 1), :]
        normal_ref[...] = eye + r_col * cov_pred[:points, :points] * r_row
        _sweep_in_place(normal_ref)
        scaled = r_col * cov_pred[:points, :]
        solved = jnp.dot(normal_ref[...], scaled, precision=HIGHEST, preferred_element_type=jnp.float32)
        correction = lax.dot_general(
            scaled, solved, (((0,), (0,)), ((), ())), precision=HIGHEST,
            preferred_element_type=jnp.float32,
        )
        cov_ref[...] = cov_pred + correction
        innovation = jnp.broadcast_to(r_row * (obs_row - mean_pred[:, :points]), (8, points))
        mean_shift = jnp.dot(innovation, solved, precision=HIGHEST, preferred_element_type=jnp.float32)
        return mean_pred - mean_shift[0:1, :]

    mean_ref[...] = lax.fori_loop(0, count_ref[0], step, jnp.zeros((1, 2 * points), jnp.float32))


def run_filter(count, obs_all, root_all, transit, process, prior):
    total, points = obs_all.shape
    width = 2 * points
    vmem = pl.BlockSpec(memory_space=pltpu.VMEM)
    return pl.pallas_call(
        _filter_kernel,
        out_shape=(
            jax.ShapeDtypeStruct((1, width), jnp.float32),
            jax.ShapeDtypeStruct((width, width), jnp.float32),
        ),
        in_specs=[pl.BlockSpec(memory_space=pltpu.SMEM)] + [vmem] * 7,
        out_specs=(vmem, vmem),
        scratch_shapes=[
            pltpu.VMEM((width, width), jnp.float32),
            pltpu.VMEM((points, points), jnp.float32),
        ],
    )(
        jnp.reshape(count, (1,)).astype(jnp.int32),
        obs_all,
        root_all,
        root_all[:, :, None],
        transit,
        transit[:, :, None],
        process,
        prior,
    )


def matmul_hi(left, right):
    return jnp.matmul(left, right, precision=HIGHEST)


def swap_last(matrix):
    return jnp.swapaxes(matrix, -1, -2)


def apply_trans(transit, matrix):
    points = transit.shape[1]
    upper_half = matrix[..., :points, :]
    lower_half = matrix[..., points:, :]
    return jnp.concatenate(
        [
            transit[0][:, None] * upper_half + transit[1][:, None] * lower_half,
            transit[2][:, None] * upper_half + transit[3][:, None] * lower_half,
        ],
        axis=-2,
    )


def build_model(decay_rates, spatial_cov):
    decay_one = jnp.exp(-decay_rates)
    transit = jnp.stack(
        [
            decay_one * (1.0 + decay_rates),
            decay_one * decay_rates,
            -decay_one * decay_rates,
            decay_one * (1.0 - decay_rates),
        ]
    )
    decay_two = jnp.exp(-2.0 * decay_rates)
    var_ff = 1.0 - decay_two * (1.0 + 2.0 * decay_rates + 2.0 * decay_rates * decay_rates)
    cov_fg = 2.0 * decay_rates * decay_rates * decay_two
    var_gg = 1.0 - decay_two * (1.0 - 2.0 * decay_rates + 2.0 * decay_rates * decay_rates)
    fac_ff = jnp.sqrt(var_ff)
    fac_gf = cov_fg / fac_ff
    fac_gg = jnp.sqrt(var_gg - fac_gf * fac_gf)

    def scaled(left, right):
        return left[:, None] * spatial_cov * right[None, :]

    zero_block = jnp.zeros_like(spatial_cov)
    process = jnp.block(
        [
            [scaled(fac_ff, fac_ff), scaled(fac_ff, fac_gf)],
            [scaled(fac_gf, fac_ff), scaled(fac_gf, fac_gf) + scaled(fac_gg, fac_gg)],
        ]
    )
    process = process + JITTER * jnp.eye(2 * spatial_cov.shape[0], dtype=jnp.float32)
    prior = jnp.block([[spatial_cov, zero_block], [zero_block, spatial_cov]])
    return (transit, process, prior)


def predict(transit, process, mean, cov):
    forward_cov = apply_trans(transit, cov)
    cov_pred = apply_trans(transit, swap_last(forward_cov)) + process
    mean_pred = apply_trans(transit, mean[:, None])[:, 0]
    return mean_pred, cov_pred


def kalman_update(mean_pred, cov_pred, obs, root):
    points = obs.shape[-1]
    normal = jnp.eye(points, dtype=jnp.float32) + root[:, None] * cov_pred[:points, :points] * root[None, :]
    neg_inv = neg_inverse(normal)
    innovation = root * (obs - mean_pred[:points])
    scaled = root[:, None] * cov_pred[:points, :]
    rhs = jnp.concatenate([scaled, innovation[:, None]], axis=1)
    solved = matmul_hi(neg_inv, rhs)
    correction = matmul_hi(swap_last(scaled), solved)
    cov_new = cov_pred + correction[:, :-1]
    mean_new = mean_pred - correction[:, -1]
    return mean_new, cov_new


def smoother_elements(means, covs, last_flag, transit, process):
    forward_cov = apply_trans(transit, covs)
    predicted = apply_trans(transit, swap_last(forward_cov)) + process
    neg_inv = jax.vmap(neg_inverse)(predicted)
    gains = -matmul_hi(swap_last(forward_cov), neg_inv)
    gains = gains * (1.0 - last_flag.astype(jnp.float32))[:, None, None]
    forward_mean = apply_trans(transit, means[..., None])
    shift_means = means - matmul_hi(gains, forward_mean)[..., 0]
    shift_covs = covs - matmul_hi(gains, forward_cov)
    return (gains, shift_means, shift_covs)


def smooth_join(lower_el, higher_el):
    gain_a, mean_a, cov_a = lower_el
    gain_b, mean_b, cov_b = higher_el
    return (
        matmul_hi(gain_a, gain_b),
        matmul_hi(gain_a, mean_b[..., None])[..., 0] + mean_a,
        matmul_hi(matmul_hi(gain_a, cov_b), swap_last(gain_a)) + cov_a,
    )


def shards(observed, obs_masks, decay_rates, noise_var, spatial_cov):
    transit, process, prior = build_model(decay_rates, spatial_cov)
    local_steps, points = observed.shape
    width = 2 * points
    position = lax.axis_index("tm")
    tm_count = lax.axis_size("tm")
    total_steps = tm_count * local_steps

    root_local = jnp.sqrt(obs_masks.astype(jnp.float32) / noise_var)
    packed = jnp.stack([observed, root_local], axis=1)
    gathered = lax.all_gather(packed, "tm", tiled=True)
    obs_all = gathered[:, 0]
    root_all = gathered[:, 1]

    last_local = position * local_steps + (local_steps - 1)

    def filter_step(step, mean, cov):
        mean_pred, cov_pred = predict(transit, process, mean, cov)
        obs_now = lax.dynamic_index_in_dim(obs_all, step, keepdims=False)
        root_now = lax.dynamic_index_in_dim(root_all, step, keepdims=False)
        return kalman_update(mean_pred, cov_pred, obs_now, root_now)

    if local_steps == 1:
        mean_last, cov_last = run_filter(position + 1, obs_all, root_all, transit, process, prior)
        means = mean_last
        covs = cov_last[None]
    else:
        mean_first, cov_first = kalman_update(
            jnp.zeros((width,), jnp.float32), prior, obs_all[0], root_all[0]
        )
        mean_buf = jnp.zeros((local_steps, width), jnp.float32).at[0].set(mean_first)
        cov_buf = jnp.zeros((local_steps, width, width), jnp.float32).at[0].set(cov_first)

        def body(step, carry):
            mean, cov, mean_buf, cov_buf = carry
            mean, cov = filter_step(step, mean, cov)
            slot = step % local_steps
            mean_buf = lax.dynamic_update_index_in_dim(mean_buf, mean, slot, 0)
            cov_buf = lax.dynamic_update_index_in_dim(cov_buf, cov, slot, 0)
            return (mean, cov, mean_buf, cov_buf)

        _, _, means, covs = lax.fori_loop(
            1, last_local + 1, body, (mean_first, cov_first, mean_buf, cov_buf)
        )

    global_step = position * local_steps + jnp.arange(local_steps)
    last_flag = global_step == total_steps - 1
    if local_steps == 1:

        def compute_elements(operand):
            return smoother_elements(operand[0], operand[1], last_flag, transit, process)

        def final_elements(operand):
            return (jnp.zeros_like(operand[1]), operand[0], operand[1])

        smooth = lax.cond(position == tm_count - 1, final_elements, compute_elements, (means, covs))
    else:
        smooth = smoother_elements(means, covs, last_flag, transit, process)

    if local_steps > 1:
        last_el = jax.tree.map(lambda leaf: leaf[-1], smooth)
        front_els = jax.tree.map(lambda leaf: leaf[:-1], smooth)

        def backward(running, element):
            joined = smooth_join(element, running)
            return (joined, joined)

        _, head_els = lax.scan(backward, last_el, front_els, reverse=True)
        suffixes = jax.tree.map(
            lambda head_leaf, last_leaf: jnp.concatenate([head_leaf, last_leaf[None]], axis=0),
            head_els,
            last_el,
        )
        block_total = jax.tree.map(lambda leaf: leaf[0], suffixes)
    else:
        block_total = jax.tree.map(lambda leaf: leaf[0], smooth)

    running = block_total
    shift = 1
    while shift < tm_count:
        pairs = [(source, source - shift) for source in range(shift, tm_count)]
        received = lax.ppermute(running, "tm", pairs)
        running = smooth_join(running, received)
        shift *= 2

    if local_steps == 1:
        return (running[1][None], running[2][None])
    pairs = [(source, source - 1) for source in range(1, tm_count)]
    after_mine = lax.ppermute(running, "tm", pairs)
    gains, shift_means, shift_covs = suffixes
    smooth_mean = matmul_hi(gains, after_mine[1][:, None])[..., 0] + shift_means
    smooth_cov = matmul_hi(matmul_hi(gains, after_mine[2]), swap_last(gains)) + shift_covs
    return (smooth_mean, smooth_cov)


def solution(mesh):
    placed = (
        P(("groups", "tm"), None),
        P(("groups", "tm"), None),
        P("groups"),
        P("groups"),
        P("groups", None),
    )
    return jax.shard_map(
        shards,
        mesh=mesh,
        in_specs=placed,
        out_specs=(P(("groups", "tm"), None), P(("groups", "tm"), None, None)),
        check_vma=False,
    )
```

```python
import jax
import jax.numpy as jnp
from jax import lax
from jax.experimental import pallas as pl
from jax.experimental.pallas import tpu as pltpu
from jax.sharding import PartitionSpec as P

HIGHEST = lax.Precision.HIGHEST
JITTER = 0.001
PANEL = 32


def _sweep_kernel(a_ref, o_ref):
    o_ref[...] = a_ref[...]
    _sweep_in_place(o_ref)


def _sweep_in_place(o_ref):
    n = o_ref.shape[0]
    sub = lax.broadcasted_iota(jnp.int32, (PANEL, n), 0)
    lane = lax.broadcasted_iota(jnp.int32, (PANEL, n), 1)
    sub_col = lax.broadcasted_iota(jnp.int32, (PANEL, 1), 0)
    lane_full = lax.broadcasted_iota(jnp.int32, (n, n), 1)
    for blk in range(n // PANEL):
        base = blk * PANEL
        orig = o_ref[base:base + PANEL, :]
        panel = orig
        for t in range(0, PANEL, 2):
            row_a = sub == t
            row_b = sub == t + 1
            col_a = lane == base + t
            col_b = lane == base + t + 1
            cv_a = jnp.sum(jnp.where(col_a, panel, 0.0), axis=1, keepdims=True)
            cv_b = jnp.sum(jnp.where(col_b, panel, 0.0), axis=1, keepdims=True)
            rv_a = jnp.sum(jnp.where(row_a, panel, 0.0), axis=0, keepdims=True)
            rv_b = jnp.sum(jnp.where(row_b, panel, 0.0), axis=0, keepdims=True)
            p = jnp.sum(jnp.where(sub_col == t, cv_a, 0.0), axis=0, keepdims=True)
            q = jnp.sum(jnp.where(sub_col == t + 1, cv_a, 0.0), axis=0, keepdims=True)
            s = jnp.sum(jnp.where(sub_col == t + 1, cv_b, 0.0), axis=0, keepdims=True)
            idet = 1.0 / (p * s - q * q)
            i_pp = s * idet
            i_pq = -q * idet
            i_ss = p * idet
            nr_a = i_pp * rv_a + i_pq * rv_b
            nr_b = i_pq * rv_a + i_ss * rv_b
            nc_a = cv_a * i_pp + cv_b * i_pq
            nc_b = cv_a * i_pq + cv_b * i_ss
            rest = panel - cv_a * nr_a - cv_b * nr_b
            rest = jnp.where(col_a, nc_a, jnp.where(col_b, nc_b, rest))
            top = jnp.where(col_a, -i_pp, jnp.where(col_b, -i_pq, nr_a))
            bot = jnp.where(col_a, -i_pq, jnp.where(col_b, -i_ss, nr_b))
            panel = jnp.where(row_a, top, jnp.where(row_b, bot, rest))
        full = o_ref[...]
        update = lax.dot_general(
            orig, panel, (((0,), (0,)), ((), ())), precision=HIGHEST,
            preferred_element_type=jnp.float32,
        )
        in_block = (lane_full >= base) & (lane_full < base + PANEL)
        o_ref[...] = jnp.where(in_block, 0.0, full) - update
        o_ref[base:base + PANEL, :] = panel


def neg_inverse(matrix):
    size = matrix.shape[-1]
    return pl.pallas_call(
        _sweep_kernel,
        out_shape=jax.ShapeDtypeStruct((size, size), jnp.float32),
        in_specs=[pl.BlockSpec(memory_space=pltpu.VMEM)],
        out_specs=pl.BlockSpec(memory_space=pltpu.VMEM),
    )(matrix)


def _filter_kernel(
    count_ref, obs_ref, root_row_ref, root_col_ref, trans_row_ref, trans_col_ref, process_ref,
    prior_ref, mean_ref, cov_ref, pred_ref, normal_ref,
):
    points = obs_ref.shape[1]
    eye = (
        lax.broadcasted_iota(jnp.int32, (points, points), 0)
        == lax.broadcasted_iota(jnp.int32, (points, points), 1)
    ).astype(jnp.float32)
    cov_ref[...] = prior_ref[...]
    a_col, b_col, c_col, d_col = (trans_col_ref[i] for i in range(4))
    a_row, b_row, c_row, d_row = (trans_row_ref[i:i + 1, :] for i in range(4))

    def step(t, mean):
        first = t == 0
        top = cov_ref[:points, :]
        bottom = cov_ref[points:, :]
        for rows, left_w, right_w in ((slice(0, points), a_col, b_col), (slice(points, None), c_col, d_col)):
            forward = left_w * top + right_w * bottom
            f_left = forward[:, :points]
            f_right = forward[:, points:]
            pred_ref[rows, :points] = f_left * a_row + f_right * b_row
            pred_ref[rows, points:] = f_left * c_row + f_right * d_row
        cov_pred = jnp.where(first, prior_ref[...], pred_ref[...] + process_ref[...])
        m_top = mean[:, :points]
        m_bottom = mean[:, points:]
        mean_fwd = jnp.concatenate(
            [a_row * m_top + b_row * m_bottom, c_row * m_top + d_row * m_bottom], axis=1
        )
        mean_pred = jnp.where(first, 0.0, mean_fwd)
        r_col = root_col_ref[t]
        r_row = root_row_ref[pl.ds(t, 1), :]
        obs_row = obs_ref[pl.ds(t, 1), :]
        normal_ref[...] = eye + r_col * cov_pred[:points, :points] * r_row
        _sweep_in_place(normal_ref)
        scaled = r_col * cov_pred[:points, :]
        solved = jnp.dot(normal_ref[...], scaled, precision=HIGHEST, preferred_element_type=jnp.float32)
        correction = lax.dot_general(
            scaled, solved, (((0,), (0,)), ((), ())), precision=HIGHEST,
            preferred_element_type=jnp.float32,
        )
        cov_ref[...] = cov_pred + correction
        innovation = jnp.broadcast_to(r_row * (obs_row - mean_pred[:, :points]), (8, points))
        mean_shift = jnp.dot(innovation, solved, precision=HIGHEST, preferred_element_type=jnp.float32)
        return mean_pred - mean_shift[0:1, :]

    mean_ref[...] = lax.fori_loop(0, count_ref[0], step, jnp.zeros((1, 2 * points), jnp.float32))


def run_filter(count, obs_all, root_all, transit, process, prior):
    total, points = obs_all.shape
    width = 2 * points
    vmem = pl.BlockSpec(memory_space=pltpu.VMEM)
    return pl.pallas_call(
        _filter_kernel,
        out_shape=(
            jax.ShapeDtypeStruct((1, width), jnp.float32),
            jax.ShapeDtypeStruct((width, width), jnp.float32),
        ),
        in_specs=[pl.BlockSpec(memory_space=pltpu.SMEM)] + [vmem] * 7,
        out_specs=(vmem, vmem),
        scratch_shapes=[
            pltpu.VMEM((width, width), jnp.float32),
            pltpu.VMEM((points, points), jnp.float32),
        ],
    )(
        jnp.reshape(count, (1,)).astype(jnp.int32),
        obs_all,
        root_all,
        root_all[:, :, None],
        transit,
        transit[:, :, None],
        process,
        prior,
    )


def matmul_hi(left, right):
    return jnp.matmul(left, right, precision=HIGHEST)


def swap_last(matrix):
    return jnp.swapaxes(matrix, -1, -2)


def apply_trans(transit, matrix):
    points = transit.shape[1]
    upper_half = matrix[..., :points, :]
    lower_half = matrix[..., points:, :]
    return jnp.concatenate(
        [
            transit[0][:, None] * upper_half + transit[1][:, None] * lower_half,
            transit[2][:, None] * upper_half + transit[3][:, None] * lower_half,
        ],
        axis=-2,
    )


def build_model(decay_rates, spatial_cov):
    decay_one = jnp.exp(-decay_rates)
    transit = jnp.stack(
        [
            decay_one * (1.0 + decay_rates),
            decay_one * decay_rates,
            -decay_one * decay_rates,
            decay_one * (1.0 - decay_rates),
        ]
    )
    decay_two = jnp.exp(-2.0 * decay_rates)
    var_ff = 1.0 - decay_two * (1.0 + 2.0 * decay_rates + 2.0 * decay_rates * decay_rates)
    cov_fg = 2.0 * decay_rates * decay_rates * decay_two
    var_gg = 1.0 - decay_two * (1.0 - 2.0 * decay_rates + 2.0 * decay_rates * decay_rates)
    fac_ff = jnp.sqrt(var_ff)
    fac_gf = cov_fg / fac_ff
    fac_gg = jnp.sqrt(var_gg - fac_gf * fac_gf)

    def scaled(left, right):
        return left[:, None] * spatial_cov * right[None, :]

    zero_block = jnp.zeros_like(spatial_cov)
    process = jnp.block(
        [
            [scaled(fac_ff, fac_ff), scaled(fac_ff, fac_gf)],
            [scaled(fac_gf, fac_ff), scaled(fac_gf, fac_gf) + scaled(fac_gg, fac_gg)],
        ]
    )
    process = process + JITTER * jnp.eye(2 * spatial_cov.shape[0], dtype=jnp.float32)
    prior = jnp.block([[spatial_cov, zero_block], [zero_block, spatial_cov]])
    return (transit, process, prior)


def predict(transit, process, mean, cov):
    forward_cov = apply_trans(transit, cov)
    cov_pred = apply_trans(transit, swap_last(forward_cov)) + process
    mean_pred = apply_trans(transit, mean[:, None])[:, 0]
    return mean_pred, cov_pred


def kalman_update(mean_pred, cov_pred, obs, root):
    points = obs.shape[-1]
    normal = jnp.eye(points, dtype=jnp.float32) + root[:, None] * cov_pred[:points, :points] * root[None, :]
    neg_inv = neg_inverse(normal)
    innovation = root * (obs - mean_pred[:points])
    scaled = root[:, None] * cov_pred[:points, :]
    rhs = jnp.concatenate([scaled, innovation[:, None]], axis=1)
    solved = matmul_hi(neg_inv, rhs)
    correction = matmul_hi(swap_last(scaled), solved)
    cov_new = cov_pred + correction[:, :-1]
    mean_new = mean_pred - correction[:, -1]
    return mean_new, cov_new


def smoother_elements(means, covs, last_flag, transit, process):
    forward_cov = apply_trans(transit, covs)
    predicted = apply_trans(transit, swap_last(forward_cov)) + process
    neg_inv = jax.vmap(neg_inverse)(predicted)
    gains = -matmul_hi(swap_last(forward_cov), neg_inv)
    gains = gains * (1.0 - last_flag.astype(jnp.float32))[:, None, None]
    forward_mean = apply_trans(transit, means[..., None])
    shift_means = means - matmul_hi(gains, forward_mean)[..., 0]
    shift_covs = covs - matmul_hi(gains, forward_cov)
    return (gains, shift_means, shift_covs)


def smooth_join(lower_el, higher_el):
    gain_a, mean_a, cov_a = lower_el
    gain_b, mean_b, cov_b = higher_el
    return (
        matmul_hi(gain_a, gain_b),
        matmul_hi(gain_a, mean_b[..., None])[..., 0] + mean_a,
        matmul_hi(matmul_hi(gain_a, cov_b), swap_last(gain_a)) + cov_a,
    )


def shards(observed, obs_masks, decay_rates, noise_var, spatial_cov):
    transit, process, prior = build_model(decay_rates, spatial_cov)
    local_steps, points = observed.shape
    width = 2 * points
    position = lax.axis_index("tm")
    tm_count = lax.axis_size("tm")
    total_steps = tm_count * local_steps

    root_local = jnp.sqrt(obs_masks.astype(jnp.float32) / noise_var)
    packed = jnp.stack([observed, root_local], axis=1)
    gathered = lax.all_gather(packed, "tm", tiled=True)
    obs_all = gathered[:, 0]
    root_all = gathered[:, 1]

    last_local = position * local_steps + (local_steps - 1)

    def filter_step(step, mean, cov):
        mean_pred, cov_pred = predict(transit, process, mean, cov)
        obs_now = lax.dynamic_index_in_dim(obs_all, step, keepdims=False)
        root_now = lax.dynamic_index_in_dim(root_all, step, keepdims=False)
        return kalman_update(mean_pred, cov_pred, obs_now, root_now)

    if local_steps == 1:
        mean_last, cov_last = run_filter(position + 1, obs_all, root_all, transit, process, prior)
        means = mean_last
        covs = cov_last[None]
    else:
        mean_first, cov_first = kalman_update(
            jnp.zeros((width,), jnp.float32), prior, obs_all[0], root_all[0]
        )
        mean_buf = jnp.zeros((local_steps, width), jnp.float32).at[0].set(mean_first)
        cov_buf = jnp.zeros((local_steps, width, width), jnp.float32).at[0].set(cov_first)

        def body(step, carry):
            mean, cov, mean_buf, cov_buf = carry
            mean, cov = filter_step(step, mean, cov)
            slot = step % local_steps
            mean_buf = lax.dynamic_update_index_in_dim(mean_buf, mean, slot, 0)
            cov_buf = lax.dynamic_update_index_in_dim(cov_buf, cov, slot, 0)
            return (mean, cov, mean_buf, cov_buf)

        _, _, means, covs = lax.fori_loop(
            1, last_local + 1, body, (mean_first, cov_first, mean_buf, cov_buf)
        )

    global_step = position * local_steps + jnp.arange(local_steps)
    last_flag = global_step == total_steps - 1
    if local_steps == 1:

        def compute_elements(operand):
            return smoother_elements(operand[0], operand[1], last_flag, transit, process)

        def final_elements(operand):
            return (jnp.zeros_like(operand[1]), operand[0], operand[1])

        smooth = lax.cond(position == tm_count - 1, final_elements, compute_elements, (means, covs))
    else:
        smooth = smoother_elements(means, covs, last_flag, transit, process)

    if local_steps > 1:
        last_el = jax.tree.map(lambda leaf: leaf[-1], smooth)
        front_els = jax.tree.map(lambda leaf: leaf[:-1], smooth)

        def backward(running, element):
            joined = smooth_join(element, running)
            return (joined, joined)

        _, head_els = lax.scan(backward, last_el, front_els, reverse=True)
        suffixes = jax.tree.map(
            lambda head_leaf, last_leaf: jnp.concatenate([head_leaf, last_leaf[None]], axis=0),
            head_els,
            last_el,
        )
        block_total = jax.tree.map(lambda leaf: leaf[0], suffixes)
    else:
        block_total = jax.tree.map(lambda leaf: leaf[0], smooth)

    running = block_total
    shift = 1
    while shift < tm_count:
        pairs = [(source, source - shift) for source in range(shift, tm_count)]
        received = lax.ppermute(running, "tm", pairs)
        running = smooth_join(running, received)
        shift *= 2

    if local_steps == 1:
        return (running[1][None], running[2][None])
    pairs = [(source, source - 1) for source in range(1, tm_count)]
    after_mine = lax.ppermute(running, "tm", pairs)
    gains, shift_means, shift_covs = suffixes
    smooth_mean = matmul_hi(gains, after_mine[1][:, None])[..., 0] + shift_means
    smooth_cov = matmul_hi(matmul_hi(gains, after_mine[2]), swap_last(gains)) + shift_covs
    return (smooth_mean, smooth_cov)


def solution(mesh):
    placed = (
        P(("groups", "tm"), None),
        P(("groups", "tm"), None),
        P("groups"),
        P("groups"),
        P("groups", None),
    )
    return jax.shard_map(
        shards,
        mesh=mesh,
        in_specs=placed,
        out_specs=(P(("groups", "tm"), None), P(("groups", "tm"), None, None)),
        check_vma=False,
    )
```

```python
import jax
import jax.numpy as jnp
from jax import lax
from jax.experimental import pallas as pl
from jax.experimental.pallas import tpu as pltpu
from jax.sharding import PartitionSpec as P

HIGHEST = lax.Precision.HIGHEST
JITTER = 0.001
PANEL = 32


def _inv2(a, b, d):
    idet = 1.0 / (a * d - b * b)
    return d * idet, -b * idet, a * idet

def _inv4(m):
    a00, a01, a11 = _inv2(m[0][0], m[0][1], m[1][1])
    b = ((m[0][2], m[0][3]), (m[1][2], m[1][3]))
    x = [[a00 * b[0][j] + a01 * b[1][j] for j in range(2)], [a01 * b[0][j] + a11 * b[1][j] for j in range(2)]]
    s00 = m[2][2] - (b[0][0] * x[0][0] + b[1][0] * x[1][0])
    s01 = m[2][3] - (b[0][0] * x[0][1] + b[1][0] * x[1][1])
    s11 = m[3][3] - (b[0][1] * x[0][1] + b[1][1] * x[1][1])
    c00, c01, c11 = _inv2(s00, s01, s11)
    cm = ((c00, c01), (c01, c11))
    y = [[x[i][0] * cm[0][j] + x[i][1] * cm[1][j] for j in range(2)] for i in range(2)]
    am = ((a00, a01), (a01, a11))
    out = [[None] * 4 for _ in range(4)]
    for i in range(2):
        for j in range(2):
            out[i][j] = am[i][j] + y[i][0] * x[j][0] + y[i][1] * x[j][1]
            out[i][2 + j] = -y[i][j]
            out[2 + j][i] = -y[i][j]
            out[2 + i][2 + j] = cm[i][j]
    return out

def _sweep_kernel(a_ref, o_ref):
    o_ref[...] = a_ref[...]
    _sweep_in_place(o_ref)

def _sweep_in_place(o_ref):
    n = o_ref.shape[0]
    sub = lax.broadcasted_iota(jnp.int32, (PANEL, n), 0)
    lane = lax.broadcasted_iota(jnp.int32, (PANEL, n), 1)
    sub_col = lax.broadcasted_iota(jnp.int32, (PANEL, 1), 0)
    lane_full = lax.broadcasted_iota(jnp.int32, (n, n), 1)
    for blk in range(n // PANEL):
        base = blk * PANEL
        orig = o_ref[base:base + PANEL, :]
        panel = orig
        for t in range(0, PANEL, 4):
            rows = [sub == t + i for i in range(4)]
            cols = [lane == base + t + i for i in range(4)]
            cv = [jnp.sum(jnp.where(cols[i], panel, 0.0), axis=1, keepdims=True) for i in range(4)]
            rv = [jnp.sum(jnp.where(rows[i], panel, 0.0), axis=0, keepdims=True) for i in range(4)]
            m = [[None] * 4 for _ in range(4)]
            for i in range(4):
                for j in range(i, 4):
                    m[i][j] = jnp.sum(jnp.where(sub_col == t + i, cv[j], 0.0), axis=0, keepdims=True)
                    m[j][i] = m[i][j]
            mi = _inv4(m)
            nr = [mi[i][0] * rv[0] + mi[i][1] * rv[1] + mi[i][2] * rv[2] + mi[i][3] * rv[3] for i in range(4)]
            nc = [cv[0] * mi[0][j] + cv[1] * mi[1][j] + cv[2] * mi[2][j] + cv[3] * mi[3][j] for j in range(4)]
            rest = panel - cv[0] * nr[0] - cv[1] * nr[1] - cv[2] * nr[2] - cv[3] * nr[3]
            for j in range(4):
                rest = jnp.where(cols[j], nc[j], rest)
            for i in range(4):
                row_val = nr[i]
                for j in range(4):
                    row_val = jnp.where(cols[j], -mi[i][j], row_val)
                rest = jnp.where(rows[i], row_val, rest)
            panel = rest
        full = o_ref[...]
        update = lax.dot_general(orig, panel, (((0,), (0,)), ((), ())), precision=HIGHEST,
                                 preferred_element_type=jnp.float32)
        in_blk = (lane_full >= base) & (lane_full < base + PANEL)
        o_ref[...] = jnp.where(in_blk, 0.0, full) - update
        o_ref[base:base + PANEL, :] = panel

def neg_inverse(matrix):
    size = matrix.shape[-1]
    return pl.pallas_call(
        _sweep_kernel,
        out_shape=jax.ShapeDtypeStruct((size, size), jnp.float32),
        in_specs=[pl.BlockSpec(memory_space=pltpu.VMEM)],
        out_specs=pl.BlockSpec(memory_space=pltpu.VMEM),
    )(matrix)


def _filter_kernel(
    count_ref, obs_ref, root_row_ref, root_col_ref, trans_row_ref, trans_col_ref, process_ref,
    prior_ref, mean_ref, cov_ref, pred_ref, normal_ref,
):
    points = obs_ref.shape[1]
    eye = (
        lax.broadcasted_iota(jnp.int32, (points, points), 0)
        == lax.broadcasted_iota(jnp.int32, (points, points), 1)
    ).astype(jnp.float32)
    cov_ref[...] = prior_ref[...]
    a_col, b_col, c_col, d_col = (trans_col_ref[i] for i in range(4))
    a_row, b_row, c_row, d_row = (trans_row_ref[i:i + 1, :] for i in range(4))

    def step(t, mean):
        first = t == 0
        top = cov_ref[:points, :]
        bottom = cov_ref[points:, :]
        for rows, left_w, right_w in ((slice(0, points), a_col, b_col), (slice(points, None), c_col, d_col)):
            forward = left_w * top + right_w * bottom
            f_left = forward[:, :points]
            f_right = forward[:, points:]
            pred_ref[rows, :points] = f_left * a_row + f_right * b_row
            pred_ref[rows, points:] = f_left * c_row + f_right * d_row
        cov_pred = jnp.where(first, prior_ref[...], pred_ref[...] + process_ref[...])
        m_top = mean[:, :points]
        m_bottom = mean[:, points:]
        mean_fwd = jnp.concatenate(
            [a_row * m_top + b_row * m_bottom, c_row * m_top + d_row * m_bottom], axis=1
        )
        mean_pred = jnp.where(first, 0.0, mean_fwd)
        r_col = root_col_ref[t]
        r_row = root_row_ref[pl.ds(t, 1), :]
        obs_row = obs_ref[pl.ds(t, 1), :]
        normal_ref[...] = eye + r_col * cov_pred[:points, :points] * r_row
        _sweep_in_place(normal_ref)
        scaled = r_col * cov_pred[:points, :]
        solved = jnp.dot(normal_ref[...], scaled, precision=HIGHEST, preferred_element_type=jnp.float32)
        correction = lax.dot_general(
            scaled, solved, (((0,), (0,)), ((), ())), precision=HIGHEST,
            preferred_element_type=jnp.float32,
        )
        cov_ref[...] = cov_pred + correction
        innovation = jnp.broadcast_to(r_row * (obs_row - mean_pred[:, :points]), (8, points))
        mean_shift = jnp.dot(innovation, solved, precision=HIGHEST, preferred_element_type=jnp.float32)
        return mean_pred - mean_shift[0:1, :]

    mean_ref[...] = lax.fori_loop(0, count_ref[0], step, jnp.zeros((1, 2 * points), jnp.float32))


def run_filter(count, obs_all, root_all, transit, process, prior):
    total, points = obs_all.shape
    width = 2 * points
    vmem = pl.BlockSpec(memory_space=pltpu.VMEM)
    return pl.pallas_call(
        _filter_kernel,
        out_shape=(
            jax.ShapeDtypeStruct((1, width), jnp.float32),
            jax.ShapeDtypeStruct((width, width), jnp.float32),
        ),
        in_specs=[pl.BlockSpec(memory_space=pltpu.SMEM)] + [vmem] * 7,
        out_specs=(vmem, vmem),
        scratch_shapes=[
            pltpu.VMEM((width, width), jnp.float32),
            pltpu.VMEM((points, points), jnp.float32),
        ],
    )(
        jnp.reshape(count, (1,)).astype(jnp.int32),
        obs_all,
        root_all,
        root_all[:, :, None],
        transit,
        transit[:, :, None],
        process,
        prior,
    )


def matmul_hi(left, right):
    return jnp.matmul(left, right, precision=HIGHEST)


def swap_last(matrix):
    return jnp.swapaxes(matrix, -1, -2)


def apply_trans(transit, matrix):
    points = transit.shape[1]
    upper_half = matrix[..., :points, :]
    lower_half = matrix[..., points:, :]
    return jnp.concatenate(
        [
            transit[0][:, None] * upper_half + transit[1][:, None] * lower_half,
            transit[2][:, None] * upper_half + transit[3][:, None] * lower_half,
        ],
        axis=-2,
    )


def build_model(decay_rates, spatial_cov):
    decay_one = jnp.exp(-decay_rates)
    transit = jnp.stack(
        [
            decay_one * (1.0 + decay_rates),
            decay_one * decay_rates,
            -decay_one * decay_rates,
            decay_one * (1.0 - decay_rates),
        ]
    )
    decay_two = jnp.exp(-2.0 * decay_rates)
    var_ff = 1.0 - decay_two * (1.0 + 2.0 * decay_rates + 2.0 * decay_rates * decay_rates)
    cov_fg = 2.0 * decay_rates * decay_rates * decay_two
    var_gg = 1.0 - decay_two * (1.0 - 2.0 * decay_rates + 2.0 * decay_rates * decay_rates)
    fac_ff = jnp.sqrt(var_ff)
    fac_gf = cov_fg / fac_ff
    fac_gg = jnp.sqrt(var_gg - fac_gf * fac_gf)

    def scaled(left, right):
        return left[:, None] * spatial_cov * right[None, :]

    zero_block = jnp.zeros_like(spatial_cov)
    process = jnp.block(
        [
            [scaled(fac_ff, fac_ff), scaled(fac_ff, fac_gf)],
            [scaled(fac_gf, fac_ff), scaled(fac_gf, fac_gf) + scaled(fac_gg, fac_gg)],
        ]
    )
    process = process + JITTER * jnp.eye(2 * spatial_cov.shape[0], dtype=jnp.float32)
    prior = jnp.block([[spatial_cov, zero_block], [zero_block, spatial_cov]])
    return (transit, process, prior)


def predict(transit, process, mean, cov):
    forward_cov = apply_trans(transit, cov)
    cov_pred = apply_trans(transit, swap_last(forward_cov)) + process
    mean_pred = apply_trans(transit, mean[:, None])[:, 0]
    return mean_pred, cov_pred


def kalman_update(mean_pred, cov_pred, obs, root):
    points = obs.shape[-1]
    normal = jnp.eye(points, dtype=jnp.float32) + root[:, None] * cov_pred[:points, :points] * root[None, :]
    neg_inv = neg_inverse(normal)
    innovation = root * (obs - mean_pred[:points])
    scaled = root[:, None] * cov_pred[:points, :]
    rhs = jnp.concatenate([scaled, innovation[:, None]], axis=1)
    solved = matmul_hi(neg_inv, rhs)
    correction = matmul_hi(swap_last(scaled), solved)
    cov_new = cov_pred + correction[:, :-1]
    mean_new = mean_pred - correction[:, -1]
    return mean_new, cov_new


def smoother_elements(means, covs, last_flag, transit, process):
    forward_cov = apply_trans(transit, covs)
    predicted = apply_trans(transit, swap_last(forward_cov)) + process
    neg_inv = jax.vmap(neg_inverse)(predicted)
    gains = -matmul_hi(swap_last(forward_cov), neg_inv)
    gains = gains * (1.0 - last_flag.astype(jnp.float32))[:, None, None]
    forward_mean = apply_trans(transit, means[..., None])
    shift_means = means - matmul_hi(gains, forward_mean)[..., 0]
    shift_covs = covs - matmul_hi(gains, forward_cov)
    return (gains, shift_means, shift_covs)


def smooth_join(lower_el, higher_el):
    gain_a, mean_a, cov_a = lower_el
    gain_b, mean_b, cov_b = higher_el
    return (
        matmul_hi(gain_a, gain_b),
        matmul_hi(gain_a, mean_b[..., None])[..., 0] + mean_a,
        matmul_hi(matmul_hi(gain_a, cov_b), swap_last(gain_a)) + cov_a,
    )


def shards(observed, obs_masks, decay_rates, noise_var, spatial_cov):
    transit, process, prior = build_model(decay_rates, spatial_cov)
    local_steps, points = observed.shape
    width = 2 * points
    position = lax.axis_index("tm")
    tm_count = lax.axis_size("tm")
    total_steps = tm_count * local_steps

    root_local = jnp.sqrt(obs_masks.astype(jnp.float32) / noise_var)
    packed = jnp.stack([observed, root_local], axis=1)
    gathered = lax.all_gather(packed, "tm", tiled=True)
    obs_all = gathered[:, 0]
    root_all = gathered[:, 1]

    last_local = position * local_steps + (local_steps - 1)

    def filter_step(step, mean, cov):
        mean_pred, cov_pred = predict(transit, process, mean, cov)
        obs_now = lax.dynamic_index_in_dim(obs_all, step, keepdims=False)
        root_now = lax.dynamic_index_in_dim(root_all, step, keepdims=False)
        return kalman_update(mean_pred, cov_pred, obs_now, root_now)

    if local_steps == 1:
        mean_last, cov_last = run_filter(position + 1, obs_all, root_all, transit, process, prior)
        means = mean_last
        covs = cov_last[None]
    else:
        mean_first, cov_first = kalman_update(
            jnp.zeros((width,), jnp.float32), prior, obs_all[0], root_all[0]
        )
        mean_buf = jnp.zeros((local_steps, width), jnp.float32).at[0].set(mean_first)
        cov_buf = jnp.zeros((local_steps, width, width), jnp.float32).at[0].set(cov_first)

        def body(step, carry):
            mean, cov, mean_buf, cov_buf = carry
            mean, cov = filter_step(step, mean, cov)
            slot = step % local_steps
            mean_buf = lax.dynamic_update_index_in_dim(mean_buf, mean, slot, 0)
            cov_buf = lax.dynamic_update_index_in_dim(cov_buf, cov, slot, 0)
            return (mean, cov, mean_buf, cov_buf)

        _, _, means, covs = lax.fori_loop(
            1, last_local + 1, body, (mean_first, cov_first, mean_buf, cov_buf)
        )

    global_step = position * local_steps + jnp.arange(local_steps)
    last_flag = global_step == total_steps - 1
    if local_steps == 1:

        def compute_elements(operand):
            return smoother_elements(operand[0], operand[1], last_flag, transit, process)

        def final_elements(operand):
            return (jnp.zeros_like(operand[1]), operand[0], operand[1])

        smooth = lax.cond(position == tm_count - 1, final_elements, compute_elements, (means, covs))
    else:
        smooth = smoother_elements(means, covs, last_flag, transit, process)

    if local_steps > 1:
        last_el = jax.tree.map(lambda leaf: leaf[-1], smooth)
        front_els = jax.tree.map(lambda leaf: leaf[:-1], smooth)

        def backward(running, element):
            joined = smooth_join(element, running)
            return (joined, joined)

        _, head_els = lax.scan(backward, last_el, front_els, reverse=True)
        suffixes = jax.tree.map(
            lambda head_leaf, last_leaf: jnp.concatenate([head_leaf, last_leaf[None]], axis=0),
            head_els,
            last_el,
        )
        block_total = jax.tree.map(lambda leaf: leaf[0], suffixes)
    else:
        block_total = jax.tree.map(lambda leaf: leaf[0], smooth)

    running = block_total
    shift = 1
    while shift < tm_count:
        pairs = [(source, source - shift) for source in range(shift, tm_count)]
        received = lax.ppermute(running, "tm", pairs)
        running = smooth_join(running, received)
        shift *= 2

    if local_steps == 1:
        return (running[1][None], running[2][None])
    pairs = [(source, source - 1) for source in range(1, tm_count)]
    after_mine = lax.ppermute(running, "tm", pairs)
    gains, shift_means, shift_covs = suffixes
    smooth_mean = matmul_hi(gains, after_mine[1][:, None])[..., 0] + shift_means
    smooth_cov = matmul_hi(matmul_hi(gains, after_mine[2]), swap_last(gains)) + shift_covs
    return (smooth_mean, smooth_cov)


def solution(mesh):
    placed = (
        P(("groups", "tm"), None),
        P(("groups", "tm"), None),
        P("groups"),
        P("groups"),
        P("groups", None),
    )
    return jax.shard_map(
        shards,
        mesh=mesh,
        in_specs=placed,
        out_specs=(P(("groups", "tm"), None), P(("groups", "tm"), None, None)),
        check_vma=False,
    )
```

```python
import jax
import jax.numpy as jnp
from jax import lax
from jax.experimental import pallas as pl
from jax.experimental.pallas import tpu as pltpu
from jax.sharding import PartitionSpec as P

HIGHEST = lax.Precision.HIGHEST
JITTER = 0.001
PANEL = 32


def _inv2(a, b, d):
    idet = 1.0 / (a * d - b * b)
    return d * idet, -b * idet, a * idet

def _inv4(m):
    a00, a01, a11 = _inv2(m[0][0], m[0][1], m[1][1])
    b = ((m[0][2], m[0][3]), (m[1][2], m[1][3]))
    x = [[a00 * b[0][j] + a01 * b[1][j] for j in range(2)], [a01 * b[0][j] + a11 * b[1][j] for j in range(2)]]
    s00 = m[2][2] - (b[0][0] * x[0][0] + b[1][0] * x[1][0])
    s01 = m[2][3] - (b[0][0] * x[0][1] + b[1][0] * x[1][1])
    s11 = m[3][3] - (b[0][1] * x[0][1] + b[1][1] * x[1][1])
    c00, c01, c11 = _inv2(s00, s01, s11)
    cm = ((c00, c01), (c01, c11))
    y = [[x[i][0] * cm[0][j] + x[i][1] * cm[1][j] for j in range(2)] for i in range(2)]
    am = ((a00, a01), (a01, a11))
    out = [[None] * 4 for _ in range(4)]
    for i in range(2):
        for j in range(2):
            out[i][j] = am[i][j] + y[i][0] * x[j][0] + y[i][1] * x[j][1]
            out[i][2 + j] = -y[i][j]
            out[2 + j][i] = -y[i][j]
            out[2 + i][2 + j] = cm[i][j]
    return out

def _sweep_kernel(a_ref, o_ref):
    o_ref[...] = a_ref[...]
    _sweep_in_place(o_ref)

def _sweep_in_place(o_ref):
    n = o_ref.shape[0]
    sub = lax.broadcasted_iota(jnp.int32, (PANEL, n), 0)
    lane = lax.broadcasted_iota(jnp.int32, (PANEL, n), 1)
    sub_col = lax.broadcasted_iota(jnp.int32, (PANEL, 1), 0)
    lane_full = lax.broadcasted_iota(jnp.int32, (n, n), 1)
    for blk in range(n // PANEL):
        base = blk * PANEL
        orig = o_ref[base:base + PANEL, :]
        panel = orig
        for t in range(0, PANEL, 4):
            rows = [sub == t + i for i in range(4)]
            cols = [lane == base + t + i for i in range(4)]
            cv = [jnp.sum(jnp.where(cols[i], panel, 0.0), axis=1, keepdims=True) for i in range(4)]
            rv = [jnp.sum(jnp.where(rows[i], panel, 0.0), axis=0, keepdims=True) for i in range(4)]
            m = [[None] * 4 for _ in range(4)]
            for i in range(4):
                for j in range(i, 4):
                    m[i][j] = jnp.sum(jnp.where(sub_col == t + i, cv[j], 0.0), axis=0, keepdims=True)
                    m[j][i] = m[i][j]
            mi = _inv4(m)
            nr = [mi[i][0] * rv[0] + mi[i][1] * rv[1] + mi[i][2] * rv[2] + mi[i][3] * rv[3] for i in range(4)]
            nc = [cv[0] * mi[0][j] + cv[1] * mi[1][j] + cv[2] * mi[2][j] + cv[3] * mi[3][j] for j in range(4)]
            rest = panel - cv[0] * nr[0] - cv[1] * nr[1] - cv[2] * nr[2] - cv[3] * nr[3]
            for j in range(4):
                rest = jnp.where(cols[j], nc[j], rest)
            for i in range(4):
                row_val = nr[i]
                for j in range(4):
                    row_val = jnp.where(cols[j], -mi[i][j], row_val)
                rest = jnp.where(rows[i], row_val, rest)
            panel = rest
        full = o_ref[...]
        update = lax.dot_general(orig, panel, (((0,), (0,)), ((), ())), precision=HIGHEST,
                                 preferred_element_type=jnp.float32)
        in_blk = (lane_full >= base) & (lane_full < base + PANEL)
        o_ref[...] = jnp.where(in_blk, 0.0, full) - update
        o_ref[base:base + PANEL, :] = panel

def neg_inverse(matrix):
    size = matrix.shape[-1]
    return pl.pallas_call(
        _sweep_kernel,
        out_shape=jax.ShapeDtypeStruct((size, size), jnp.float32),
        in_specs=[pl.BlockSpec(memory_space=pltpu.VMEM)],
        out_specs=pl.BlockSpec(memory_space=pltpu.VMEM),
    )(matrix)


def _filter_kernel(
    count_ref, obs_ref, root_row_ref, root_col_ref, trans_row_ref, trans_col_ref, process_ref,
    prior_ref, mean_ref, cov_ref, pred_ref, normal_ref,
):
    points = obs_ref.shape[1]
    eye = (
        lax.broadcasted_iota(jnp.int32, (points, points), 0)
        == lax.broadcasted_iota(jnp.int32, (points, points), 1)
    ).astype(jnp.float32)
    cov_ref[...] = prior_ref[...]
    a_col, b_col, c_col, d_col = (trans_col_ref[i] for i in range(4))
    a_row, b_row, c_row, d_row = (trans_row_ref[i:i + 1, :] for i in range(4))

    def step(t, mean):
        first = t == 0
        top = cov_ref[:points, :]
        bottom = cov_ref[points:, :]
        for rows, left_w, right_w in ((slice(0, points), a_col, b_col), (slice(points, None), c_col, d_col)):
            forward = left_w * top + right_w * bottom
            f_left = forward[:, :points]
            f_right = forward[:, points:]
            pred_ref[rows, :points] = f_left * a_row + f_right * b_row
            pred_ref[rows, points:] = f_left * c_row + f_right * d_row
        cov_pred = jnp.where(first, prior_ref[...], pred_ref[...] + process_ref[...])
        m_top = mean[:, :points]
        m_bottom = mean[:, points:]
        mean_fwd = jnp.concatenate(
            [a_row * m_top + b_row * m_bottom, c_row * m_top + d_row * m_bottom], axis=1
        )
        mean_pred = jnp.where(first, 0.0, mean_fwd)
        r_col = root_col_ref[t]
        r_row = root_row_ref[pl.ds(t, 1), :]
        obs_row = obs_ref[pl.ds(t, 1), :]
        normal_ref[...] = eye + r_col * cov_pred[:points, :points] * r_row
        _sweep_in_place(normal_ref)
        scaled = r_col * cov_pred[:points, :]
        solved = jnp.dot(normal_ref[...], scaled, precision=HIGHEST, preferred_element_type=jnp.float32)
        correction = lax.dot_general(
            scaled, solved, (((0,), (0,)), ((), ())), precision=HIGHEST,
            preferred_element_type=jnp.float32,
        )
        cov_ref[...] = cov_pred + correction
        innovation = jnp.broadcast_to(r_row * (obs_row - mean_pred[:, :points]), (8, points))
        mean_shift = jnp.dot(innovation, solved, precision=HIGHEST, preferred_element_type=jnp.float32)
        return mean_pred - mean_shift[0:1, :]

    mean_ref[...] = lax.fori_loop(0, count_ref[0], step, jnp.zeros((1, 2 * points), jnp.float32))


def run_filter(count, obs_all, root_all, transit, process, prior):
    total, points = obs_all.shape
    width = 2 * points
    vmem = pl.BlockSpec(memory_space=pltpu.VMEM)
    return pl.pallas_call(
        _filter_kernel,
        out_shape=(
            jax.ShapeDtypeStruct((1, width), jnp.float32),
            jax.ShapeDtypeStruct((width, width), jnp.float32),
        ),
        in_specs=[pl.BlockSpec(memory_space=pltpu.SMEM)] + [vmem] * 7,
        out_specs=(vmem, vmem),
        scratch_shapes=[
            pltpu.VMEM((width, width), jnp.float32),
            pltpu.VMEM((points, points), jnp.float32),
        ],
    )(
        jnp.reshape(count, (1,)).astype(jnp.int32),
        obs_all,
        root_all,
        root_all[:, :, None],
        transit,
        transit[:, :, None],
        process,
        prior,
    )


def matmul_hi(left, right):
    return jnp.matmul(left, right, precision=HIGHEST)


def swap_last(matrix):
    return jnp.swapaxes(matrix, -1, -2)


def apply_trans(transit, matrix):
    points = transit.shape[1]
    upper_half = matrix[..., :points, :]
    lower_half = matrix[..., points:, :]
    return jnp.concatenate(
        [
            transit[0][:, None] * upper_half + transit[1][:, None] * lower_half,
            transit[2][:, None] * upper_half + transit[3][:, None] * lower_half,
        ],
        axis=-2,
    )


def build_model(decay_rates, spatial_cov):
    decay_one = jnp.exp(-decay_rates)
    transit = jnp.stack(
        [
            decay_one * (1.0 + decay_rates),
            decay_one * decay_rates,
            -decay_one * decay_rates,
            decay_one * (1.0 - decay_rates),
        ]
    )
    decay_two = jnp.exp(-2.0 * decay_rates)
    var_ff = 1.0 - decay_two * (1.0 + 2.0 * decay_rates + 2.0 * decay_rates * decay_rates)
    cov_fg = 2.0 * decay_rates * decay_rates * decay_two
    var_gg = 1.0 - decay_two * (1.0 - 2.0 * decay_rates + 2.0 * decay_rates * decay_rates)
    fac_ff = jnp.sqrt(var_ff)
    fac_gf = cov_fg / fac_ff
    fac_gg = jnp.sqrt(var_gg - fac_gf * fac_gf)

    def scaled(left, right):
        return left[:, None] * spatial_cov * right[None, :]

    zero_block = jnp.zeros_like(spatial_cov)
    process = jnp.block(
        [
            [scaled(fac_ff, fac_ff), scaled(fac_ff, fac_gf)],
            [scaled(fac_gf, fac_ff), scaled(fac_gf, fac_gf) + scaled(fac_gg, fac_gg)],
        ]
    )
    process = process + JITTER * jnp.eye(2 * spatial_cov.shape[0], dtype=jnp.float32)
    prior = jnp.block([[spatial_cov, zero_block], [zero_block, spatial_cov]])
    return (transit, process, prior)


def predict(transit, process, mean, cov):
    forward_cov = apply_trans(transit, cov)
    cov_pred = apply_trans(transit, swap_last(forward_cov)) + process
    mean_pred = apply_trans(transit, mean[:, None])[:, 0]
    return mean_pred, cov_pred


def kalman_update(mean_pred, cov_pred, obs, root):
    points = obs.shape[-1]
    normal = jnp.eye(points, dtype=jnp.float32) + root[:, None] * cov_pred[:points, :points] * root[None, :]
    neg_inv = neg_inverse(normal)
    innovation = root * (obs - mean_pred[:points])
    scaled = root[:, None] * cov_pred[:points, :]
    rhs = jnp.concatenate([scaled, innovation[:, None]], axis=1)
    solved = matmul_hi(neg_inv, rhs)
    correction = matmul_hi(swap_last(scaled), solved)
    cov_new = cov_pred + correction[:, :-1]
    mean_new = mean_pred - correction[:, -1]
    return mean_new, cov_new


def smoother_elements(means, covs, last_flag, transit, process):
    forward_cov = apply_trans(transit, covs)
    predicted = apply_trans(transit, swap_last(forward_cov)) + process
    neg_inv = jax.vmap(neg_inverse)(predicted)
    gains = -matmul_hi(swap_last(forward_cov), neg_inv)
    gains = gains * (1.0 - last_flag.astype(jnp.float32))[:, None, None]
    forward_mean = apply_trans(transit, means[..., None])
    shift_means = means - matmul_hi(gains, forward_mean)[..., 0]
    shift_covs = covs - matmul_hi(gains, forward_cov)
    return (gains, shift_means, shift_covs)


def smooth_join(lower_el, higher_el):
    gain_a, mean_a, cov_a = lower_el
    gain_b, mean_b, cov_b = higher_el
    return (
        matmul_hi(gain_a, gain_b),
        matmul_hi(gain_a, mean_b[..., None])[..., 0] + mean_a,
        matmul_hi(matmul_hi(gain_a, cov_b), swap_last(gain_a)) + cov_a,
    )


def send_packed(element, pairs, with_gain):
    gain, mean, cov = element
    width = mean.shape[-1]
    pieces = ([gain] if with_gain else []) + [cov, jnp.broadcast_to(mean[None], (8, width))]
    received = lax.ppermute(jnp.concatenate(pieces, axis=0), "tm", pairs)
    offset = width if with_gain else 0
    recv_gain = received[:width] if with_gain else jnp.zeros_like(gain)
    return (recv_gain, received[offset + width], received[offset:offset + width])


def shards(observed, obs_masks, decay_rates, noise_var, spatial_cov):
    transit, process, prior = build_model(decay_rates, spatial_cov)
    local_steps, points = observed.shape
    width = 2 * points
    position = lax.axis_index("tm")
    tm_count = lax.axis_size("tm")
    total_steps = tm_count * local_steps

    root_local = jnp.sqrt(obs_masks.astype(jnp.float32) / noise_var)
    packed = jnp.stack([observed, root_local], axis=1)
    gathered = lax.all_gather(packed, "tm", tiled=True)
    obs_all = gathered[:, 0]
    root_all = gathered[:, 1]

    last_local = position * local_steps + (local_steps - 1)

    def filter_step(step, mean, cov):
        mean_pred, cov_pred = predict(transit, process, mean, cov)
        obs_now = lax.dynamic_index_in_dim(obs_all, step, keepdims=False)
        root_now = lax.dynamic_index_in_dim(root_all, step, keepdims=False)
        return kalman_update(mean_pred, cov_pred, obs_now, root_now)

    if local_steps == 1:
        mean_last, cov_last = run_filter(position + 1, obs_all, root_all, transit, process, prior)
        means = mean_last
        covs = cov_last[None]
    else:
        mean_first, cov_first = kalman_update(
            jnp.zeros((width,), jnp.float32), prior, obs_all[0], root_all[0]
        )
        mean_buf = jnp.zeros((local_steps, width), jnp.float32).at[0].set(mean_first)
        cov_buf = jnp.zeros((local_steps, width, width), jnp.float32).at[0].set(cov_first)

        def body(step, carry):
            mean, cov, mean_buf, cov_buf = carry
            mean, cov = filter_step(step, mean, cov)
            slot = step % local_steps
            mean_buf = lax.dynamic_update_index_in_dim(mean_buf, mean, slot, 0)
            cov_buf = lax.dynamic_update_index_in_dim(cov_buf, cov, slot, 0)
            return (mean, cov, mean_buf, cov_buf)

        _, _, means, covs = lax.fori_loop(
            1, last_local + 1, body, (mean_first, cov_first, mean_buf, cov_buf)
        )

    global_step = position * local_steps + jnp.arange(local_steps)
    last_flag = global_step == total_steps - 1
    if local_steps == 1:

        def compute_elements(operand):
            return smoother_elements(operand[0], operand[1], last_flag, transit, process)

        def final_elements(operand):
            return (jnp.zeros_like(operand[1]), operand[0], operand[1])

        smooth = lax.cond(position == tm_count - 1, final_elements, compute_elements, (means, covs))
    else:
        smooth = smoother_elements(means, covs, last_flag, transit, process)

    if local_steps > 1:
        last_el = jax.tree.map(lambda leaf: leaf[-1], smooth)
        front_els = jax.tree.map(lambda leaf: leaf[:-1], smooth)

        def backward(running, element):
            joined = smooth_join(element, running)
            return (joined, joined)

        _, head_els = lax.scan(backward, last_el, front_els, reverse=True)
        suffixes = jax.tree.map(
            lambda head_leaf, last_leaf: jnp.concatenate([head_leaf, last_leaf[None]], axis=0),
            head_els,
            last_el,
        )
        block_total = jax.tree.map(lambda leaf: leaf[0], suffixes)
    else:
        block_total = jax.tree.map(lambda leaf: leaf[0], smooth)

    running = block_total
    shift = 1
    while shift < tm_count:
        pairs = [(source, source - shift) for source in range(shift, tm_count)]
        final_round = 2 * shift >= tm_count
        received = send_packed(running, pairs, not final_round)
        running = smooth_join(running, received)
        shift *= 2

    if local_steps == 1:
        return (running[1][None], running[2][None])
    pairs = [(source, source - 1) for source in range(1, tm_count)]
    after_mine = lax.ppermute(running, "tm", pairs)
    gains, shift_means, shift_covs = suffixes
    smooth_mean = matmul_hi(gains, after_mine[1][:, None])[..., 0] + shift_means
    smooth_cov = matmul_hi(matmul_hi(gains, after_mine[2]), swap_last(gains)) + shift_covs
    return (smooth_mean, smooth_cov)


def solution(mesh):
    placed = (
        P(("groups", "tm"), None),
        P(("groups", "tm"), None),
        P("groups"),
        P("groups"),
        P("groups", None),
    )
    return jax.shard_map(
        shards,
        mesh=mesh,
        in_specs=placed,
        out_specs=(P(("groups", "tm"), None), P(("groups", "tm"), None, None)),
        check_vma=False,
    )
```

```python
import jax
import jax.numpy as jnp
from jax import lax
from jax.experimental import pallas as pl
from jax.experimental.pallas import tpu as pltpu
from jax.sharding import PartitionSpec as P

HIGHEST = lax.Precision.HIGHEST
JITTER = 0.001
PANEL = 32


def _inv2(a, b, d):
    idet = 1.0 / (a * d - b * b)
    return d * idet, -b * idet, a * idet

def _inv4(m):
    a00, a01, a11 = _inv2(m[0][0], m[0][1], m[1][1])
    b = ((m[0][2], m[0][3]), (m[1][2], m[1][3]))
    x = [[a00 * b[0][j] + a01 * b[1][j] for j in range(2)], [a01 * b[0][j] + a11 * b[1][j] for j in range(2)]]
    s00 = m[2][2] - (b[0][0] * x[0][0] + b[1][0] * x[1][0])
    s01 = m[2][3] - (b[0][0] * x[0][1] + b[1][0] * x[1][1])
    s11 = m[3][3] - (b[0][1] * x[0][1] + b[1][1] * x[1][1])
    c00, c01, c11 = _inv2(s00, s01, s11)
    cm = ((c00, c01), (c01, c11))
    y = [[x[i][0] * cm[0][j] + x[i][1] * cm[1][j] for j in range(2)] for i in range(2)]
    am = ((a00, a01), (a01, a11))
    out = [[None] * 4 for _ in range(4)]
    for i in range(2):
        for j in range(2):
            out[i][j] = am[i][j] + y[i][0] * x[j][0] + y[i][1] * x[j][1]
            out[i][2 + j] = -y[i][j]
            out[2 + j][i] = -y[i][j]
            out[2 + i][2 + j] = cm[i][j]
    return out

def _sweep_kernel(a_ref, o_ref):
    o_ref[...] = a_ref[...]
    _sweep_in_place(o_ref)

def _sweep_in_place(o_ref):
    n = o_ref.shape[0]
    PANEL = 64 if n >= 256 else 32
    sub = lax.broadcasted_iota(jnp.int32, (PANEL, n), 0)
    lane = lax.broadcasted_iota(jnp.int32, (PANEL, n), 1)
    sub_col = lax.broadcasted_iota(jnp.int32, (PANEL, 1), 0)
    lane_full = lax.broadcasted_iota(jnp.int32, (n, n), 1)
    for blk in range(n // PANEL):
        base = blk * PANEL
        orig = o_ref[base:base + PANEL, :]
        panel = orig
        for t in range(0, PANEL, 4):
            rows = [sub == t + i for i in range(4)]
            cols = [lane == base + t + i for i in range(4)]
            cv = [jnp.sum(jnp.where(cols[i], panel, 0.0), axis=1, keepdims=True) for i in range(4)]
            rv = [jnp.sum(jnp.where(rows[i], panel, 0.0), axis=0, keepdims=True) for i in range(4)]
            m = [[None] * 4 for _ in range(4)]
            for i in range(4):
                for j in range(i, 4):
                    m[i][j] = jnp.sum(jnp.where(sub_col == t + i, cv[j], 0.0), axis=0, keepdims=True)
                    m[j][i] = m[i][j]
            mi = _inv4(m)
            nr = [mi[i][0] * rv[0] + mi[i][1] * rv[1] + mi[i][2] * rv[2] + mi[i][3] * rv[3] for i in range(4)]
            nc = [cv[0] * mi[0][j] + cv[1] * mi[1][j] + cv[2] * mi[2][j] + cv[3] * mi[3][j] for j in range(4)]
            rest = panel - cv[0] * nr[0] - cv[1] * nr[1] - cv[2] * nr[2] - cv[3] * nr[3]
            for j in range(4):
                rest = jnp.where(cols[j], nc[j], rest)
            for i in range(4):
                row_val = nr[i]
                for j in range(4):
                    row_val = jnp.where(cols[j], -mi[i][j], row_val)
                rest = jnp.where(rows[i], row_val, rest)
            panel = rest
        full = o_ref[...]
        update = lax.dot_general(orig, panel, (((0,), (0,)), ((), ())), precision=HIGHEST,
                                 preferred_element_type=jnp.float32)
        in_blk = (lane_full >= base) & (lane_full < base + PANEL)
        o_ref[...] = jnp.where(in_blk, 0.0, full) - update
        o_ref[base:base + PANEL, :] = panel

def neg_inverse(matrix):
    size = matrix.shape[-1]
    return pl.pallas_call(
        _sweep_kernel,
        out_shape=jax.ShapeDtypeStruct((size, size), jnp.float32),
        in_specs=[pl.BlockSpec(memory_space=pltpu.VMEM)],
        out_specs=pl.BlockSpec(memory_space=pltpu.VMEM),
    )(matrix)


def _filter_kernel(
    count_ref, obs_ref, root_row_ref, root_col_ref, trans_row_ref, trans_col_ref, process_ref,
    prior_ref, mean_ref, cov_ref, pred_ref, normal_ref,
):
    points = obs_ref.shape[1]
    eye = (
        lax.broadcasted_iota(jnp.int32, (points, points), 0)
        == lax.broadcasted_iota(jnp.int32, (points, points), 1)
    ).astype(jnp.float32)
    cov_ref[...] = prior_ref[...]
    a_col, b_col, c_col, d_col = (trans_col_ref[i] for i in range(4))
    a_row, b_row, c_row, d_row = (trans_row_ref[i:i + 1, :] for i in range(4))

    def step(t, mean):
        first = t == 0
        top = cov_ref[:points, :]
        bottom = cov_ref[points:, :]
        for rows, left_w, right_w in ((slice(0, points), a_col, b_col), (slice(points, None), c_col, d_col)):
            forward = left_w * top + right_w * bottom
            f_left = forward[:, :points]
            f_right = forward[:, points:]
            pred_ref[rows, :points] = f_left * a_row + f_right * b_row
            pred_ref[rows, points:] = f_left * c_row + f_right * d_row
        cov_pred = jnp.where(first, prior_ref[...], pred_ref[...] + process_ref[...])
        m_top = mean[:, :points]
        m_bottom = mean[:, points:]
        mean_fwd = jnp.concatenate(
            [a_row * m_top + b_row * m_bottom, c_row * m_top + d_row * m_bottom], axis=1
        )
        mean_pred = jnp.where(first, 0.0, mean_fwd)
        r_col = root_col_ref[t]
        r_row = root_row_ref[pl.ds(t, 1), :]
        obs_row = obs_ref[pl.ds(t, 1), :]
        normal_ref[...] = eye + r_col * cov_pred[:points, :points] * r_row
        _sweep_in_place(normal_ref)
        scaled = r_col * cov_pred[:points, :]
        solved = jnp.dot(normal_ref[...], scaled, precision=HIGHEST, preferred_element_type=jnp.float32)
        correction = lax.dot_general(
            scaled, solved, (((0,), (0,)), ((), ())), precision=HIGHEST,
            preferred_element_type=jnp.float32,
        )
        cov_ref[...] = cov_pred + correction
        innovation = jnp.broadcast_to(r_row * (obs_row - mean_pred[:, :points]), (8, points))
        mean_shift = jnp.dot(innovation, solved, precision=HIGHEST, preferred_element_type=jnp.float32)
        return mean_pred - mean_shift[0:1, :]

    mean_ref[...] = lax.fori_loop(0, count_ref[0], step, jnp.zeros((1, 2 * points), jnp.float32))


def run_filter(count, obs_all, root_all, transit, process, prior):
    total, points = obs_all.shape
    width = 2 * points
    vmem = pl.BlockSpec(memory_space=pltpu.VMEM)
    return pl.pallas_call(
        _filter_kernel,
        out_shape=(
            jax.ShapeDtypeStruct((1, width), jnp.float32),
            jax.ShapeDtypeStruct((width, width), jnp.float32),
        ),
        in_specs=[pl.BlockSpec(memory_space=pltpu.SMEM)] + [vmem] * 7,
        out_specs=(vmem, vmem),
        scratch_shapes=[
            pltpu.VMEM((width, width), jnp.float32),
            pltpu.VMEM((points, points), jnp.float32),
        ],
    )(
        jnp.reshape(count, (1,)).astype(jnp.int32),
        obs_all,
        root_all,
        root_all[:, :, None],
        transit,
        transit[:, :, None],
        process,
        prior,
    )


def matmul_hi(left, right):
    return jnp.matmul(left, right, precision=HIGHEST)


def swap_last(matrix):
    return jnp.swapaxes(matrix, -1, -2)


def apply_trans(transit, matrix):
    points = transit.shape[1]
    upper_half = matrix[..., :points, :]
    lower_half = matrix[..., points:, :]
    return jnp.concatenate(
        [
            transit[0][:, None] * upper_half + transit[1][:, None] * lower_half,
            transit[2][:, None] * upper_half + transit[3][:, None] * lower_half,
        ],
        axis=-2,
    )


def build_model(decay_rates, spatial_cov):
    decay_one = jnp.exp(-decay_rates)
    transit = jnp.stack(
        [
            decay_one * (1.0 + decay_rates),
            decay_one * decay_rates,
            -decay_one * decay_rates,
            decay_one * (1.0 - decay_rates),
        ]
    )
    decay_two = jnp.exp(-2.0 * decay_rates)
    var_ff = 1.0 - decay_two * (1.0 + 2.0 * decay_rates + 2.0 * decay_rates * decay_rates)
    cov_fg = 2.0 * decay_rates * decay_rates * decay_two
    var_gg = 1.0 - decay_two * (1.0 - 2.0 * decay_rates + 2.0 * decay_rates * decay_rates)
    fac_ff = jnp.sqrt(var_ff)
    fac_gf = cov_fg / fac_ff
    fac_gg = jnp.sqrt(var_gg - fac_gf * fac_gf)

    def scaled(left, right):
        return left[:, None] * spatial_cov * right[None, :]

    zero_block = jnp.zeros_like(spatial_cov)
    process = jnp.block(
        [
            [scaled(fac_ff, fac_ff), scaled(fac_ff, fac_gf)],
            [scaled(fac_gf, fac_ff), scaled(fac_gf, fac_gf) + scaled(fac_gg, fac_gg)],
        ]
    )
    process = process + JITTER * jnp.eye(2 * spatial_cov.shape[0], dtype=jnp.float32)
    prior = jnp.block([[spatial_cov, zero_block], [zero_block, spatial_cov]])
    return (transit, process, prior)


def predict(transit, process, mean, cov):
    forward_cov = apply_trans(transit, cov)
    cov_pred = apply_trans(transit, swap_last(forward_cov)) + process
    mean_pred = apply_trans(transit, mean[:, None])[:, 0]
    return mean_pred, cov_pred


def kalman_update(mean_pred, cov_pred, obs, root):
    points = obs.shape[-1]
    normal = jnp.eye(points, dtype=jnp.float32) + root[:, None] * cov_pred[:points, :points] * root[None, :]
    neg_inv = neg_inverse(normal)
    innovation = root * (obs - mean_pred[:points])
    scaled = root[:, None] * cov_pred[:points, :]
    rhs = jnp.concatenate([scaled, innovation[:, None]], axis=1)
    solved = matmul_hi(neg_inv, rhs)
    correction = matmul_hi(swap_last(scaled), solved)
    cov_new = cov_pred + correction[:, :-1]
    mean_new = mean_pred - correction[:, -1]
    return mean_new, cov_new


def smoother_elements(means, covs, last_flag, transit, process):
    forward_cov = apply_trans(transit, covs)
    predicted = apply_trans(transit, swap_last(forward_cov)) + process
    neg_inv = jax.vmap(neg_inverse)(predicted)
    gains = -matmul_hi(swap_last(forward_cov), neg_inv)
    gains = gains * (1.0 - last_flag.astype(jnp.float32))[:, None, None]
    forward_mean = apply_trans(transit, means[..., None])
    shift_means = means - matmul_hi(gains, forward_mean)[..., 0]
    shift_covs = covs - matmul_hi(gains, forward_cov)
    return (gains, shift_means, shift_covs)


def smooth_join(lower_el, higher_el):
    gain_a, mean_a, cov_a = lower_el
    gain_b, mean_b, cov_b = higher_el
    return (
        matmul_hi(gain_a, gain_b),
        matmul_hi(gain_a, mean_b[..., None])[..., 0] + mean_a,
        matmul_hi(matmul_hi(gain_a, cov_b), swap_last(gain_a)) + cov_a,
    )


def send_element(element, pairs):
    gain, mean, cov = element
    width = mean.shape[-1]
    packed = jnp.concatenate([cov, jnp.broadcast_to(mean[None], (8, width))], axis=0)
    recv_gain, recv_packed = lax.ppermute((gain, packed), "tm", pairs)
    return (recv_gain, recv_packed[width], recv_packed[:width])


def shards(observed, obs_masks, decay_rates, noise_var, spatial_cov):
    transit, process, prior = build_model(decay_rates, spatial_cov)
    local_steps, points = observed.shape
    width = 2 * points
    position = lax.axis_index("tm")
    tm_count = lax.axis_size("tm")
    total_steps = tm_count * local_steps

    root_local = jnp.sqrt(obs_masks.astype(jnp.float32) / noise_var)
    packed = jnp.stack([observed, root_local], axis=1)
    gathered = lax.all_gather(packed, "tm", tiled=True)
    obs_all = gathered[:, 0]
    root_all = gathered[:, 1]

    last_local = position * local_steps + (local_steps - 1)

    def filter_step(step, mean, cov):
        mean_pred, cov_pred = predict(transit, process, mean, cov)
        obs_now = lax.dynamic_index_in_dim(obs_all, step, keepdims=False)
        root_now = lax.dynamic_index_in_dim(root_all, step, keepdims=False)
        return kalman_update(mean_pred, cov_pred, obs_now, root_now)

    if local_steps == 1:
        mean_last, cov_last = run_filter(position + 1, obs_all, root_all, transit, process, prior)
        means = mean_last
        covs = cov_last[None]
    else:
        mean_first, cov_first = kalman_update(
            jnp.zeros((width,), jnp.float32), prior, obs_all[0], root_all[0]
        )
        mean_buf = jnp.zeros((local_steps, width), jnp.float32).at[0].set(mean_first)
        cov_buf = jnp.zeros((local_steps, width, width), jnp.float32).at[0].set(cov_first)

        def body(step, carry):
            mean, cov, mean_buf, cov_buf = carry
            mean, cov = filter_step(step, mean, cov)
            slot = step % local_steps
            mean_buf = lax.dynamic_update_index_in_dim(mean_buf, mean, slot, 0)
            cov_buf = lax.dynamic_update_index_in_dim(cov_buf, cov, slot, 0)
            return (mean, cov, mean_buf, cov_buf)

        _, _, means, covs = lax.fori_loop(
            1, last_local + 1, body, (mean_first, cov_first, mean_buf, cov_buf)
        )

    global_step = position * local_steps + jnp.arange(local_steps)
    last_flag = global_step == total_steps - 1
    if local_steps == 1:

        def compute_elements(operand):
            return smoother_elements(operand[0], operand[1], last_flag, transit, process)

        def final_elements(operand):
            return (jnp.zeros_like(operand[1]), operand[0], operand[1])

        smooth = lax.cond(position == tm_count - 1, final_elements, compute_elements, (means, covs))
    else:
        smooth = smoother_elements(means, covs, last_flag, transit, process)

    if local_steps > 1:
        last_el = jax.tree.map(lambda leaf: leaf[-1], smooth)
        front_els = jax.tree.map(lambda leaf: leaf[:-1], smooth)

        def backward(running, element):
            joined = smooth_join(element, running)
            return (joined, joined)

        _, head_els = lax.scan(backward, last_el, front_els, reverse=True)
        suffixes = jax.tree.map(
            lambda head_leaf, last_leaf: jnp.concatenate([head_leaf, last_leaf[None]], axis=0),
            head_els,
            last_el,
        )
        block_total = jax.tree.map(lambda leaf: leaf[0], suffixes)
    else:
        block_total = jax.tree.map(lambda leaf: leaf[0], smooth)

    running = block_total
    shift = 1
    while shift < tm_count:
        pairs = [(source, source - shift) for source in range(shift, tm_count)]
        received = send_element(running, pairs)
        running = smooth_join(running, received)
        shift *= 2

    if local_steps == 1:
        return (running[1][None], running[2][None])
    pairs = [(source, source - 1) for source in range(1, tm_count)]
    after_mine = lax.ppermute(running, "tm", pairs)
    gains, shift_means, shift_covs = suffixes
    smooth_mean = matmul_hi(gains, after_mine[1][:, None])[..., 0] + shift_means
    smooth_cov = matmul_hi(matmul_hi(gains, after_mine[2]), swap_last(gains)) + shift_covs
    return (smooth_mean, smooth_cov)


def solution(mesh):
    placed = (
        P(("groups", "tm"), None),
        P(("groups", "tm"), None),
        P("groups"),
        P("groups"),
        P("groups", None),
    )
    return jax.shard_map(
        shards,
        mesh=mesh,
        in_specs=placed,
        out_specs=(P(("groups", "tm"), None), P(("groups", "tm"), None, None)),
        check_vma=False,
    )
```

```python
import jax
import jax.numpy as jnp
from jax import lax
from jax.experimental import pallas as pl
from jax.experimental.pallas import tpu as pltpu
from jax.sharding import PartitionSpec as P

HIGHEST = lax.Precision.HIGHEST
KERNEL_PRECISION = lax.Precision.HIGH
JITTER = 0.001
PANEL = 32


def _inv2(a, b, d):
    idet = 1.0 / (a * d - b * b)
    return d * idet, -b * idet, a * idet

def _inv4(m):
    a00, a01, a11 = _inv2(m[0][0], m[0][1], m[1][1])
    b = ((m[0][2], m[0][3]), (m[1][2], m[1][3]))
    x = [[a00 * b[0][j] + a01 * b[1][j] for j in range(2)], [a01 * b[0][j] + a11 * b[1][j] for j in range(2)]]
    s00 = m[2][2] - (b[0][0] * x[0][0] + b[1][0] * x[1][0])
    s01 = m[2][3] - (b[0][0] * x[0][1] + b[1][0] * x[1][1])
    s11 = m[3][3] - (b[0][1] * x[0][1] + b[1][1] * x[1][1])
    c00, c01, c11 = _inv2(s00, s01, s11)
    cm = ((c00, c01), (c01, c11))
    y = [[x[i][0] * cm[0][j] + x[i][1] * cm[1][j] for j in range(2)] for i in range(2)]
    am = ((a00, a01), (a01, a11))
    out = [[None] * 4 for _ in range(4)]
    for i in range(2):
        for j in range(2):
            out[i][j] = am[i][j] + y[i][0] * x[j][0] + y[i][1] * x[j][1]
            out[i][2 + j] = -y[i][j]
            out[2 + j][i] = -y[i][j]
            out[2 + i][2 + j] = cm[i][j]
    return out

def _sweep_kernel(a_ref, o_ref):
    o_ref[...] = a_ref[...]
    _sweep_in_place(o_ref)

def _sweep_in_place(o_ref):
    n = o_ref.shape[0]
    PANEL = 64 if n >= 256 else 32
    precision = HIGHEST if n >= 256 else KERNEL_PRECISION
    sub = lax.broadcasted_iota(jnp.int32, (PANEL, n), 0)
    lane = lax.broadcasted_iota(jnp.int32, (PANEL, n), 1)
    sub_col = lax.broadcasted_iota(jnp.int32, (PANEL, 1), 0)
    lane_full = lax.broadcasted_iota(jnp.int32, (n, n), 1)
    for blk in range(n // PANEL):
        base = blk * PANEL
        orig = o_ref[base:base + PANEL, :]
        panel = orig
        for t in range(0, PANEL, 4):
            rows = [sub == t + i for i in range(4)]
            cols = [lane == base + t + i for i in range(4)]
            cv = [jnp.sum(jnp.where(cols[i], panel, 0.0), axis=1, keepdims=True) for i in range(4)]
            rv = [jnp.sum(jnp.where(rows[i], panel, 0.0), axis=0, keepdims=True) for i in range(4)]
            m = [[None] * 4 for _ in range(4)]
            for i in range(4):
                for j in range(i, 4):
                    m[i][j] = jnp.sum(jnp.where(sub_col == t + i, cv[j], 0.0), axis=0, keepdims=True)
                    m[j][i] = m[i][j]
            mi = _inv4(m)
            nr = [mi[i][0] * rv[0] + mi[i][1] * rv[1] + mi[i][2] * rv[2] + mi[i][3] * rv[3] for i in range(4)]
            nc = [cv[0] * mi[0][j] + cv[1] * mi[1][j] + cv[2] * mi[2][j] + cv[3] * mi[3][j] for j in range(4)]
            rest = panel - cv[0] * nr[0] - cv[1] * nr[1] - cv[2] * nr[2] - cv[3] * nr[3]
            for j in range(4):
                rest = jnp.where(cols[j], nc[j], rest)
            for i in range(4):
                row_val = nr[i]
                for j in range(4):
                    row_val = jnp.where(cols[j], -mi[i][j], row_val)
                rest = jnp.where(rows[i], row_val, rest)
            panel = rest
        full = o_ref[...]
        update = lax.dot_general(orig, panel, (((0,), (0,)), ((), ())), precision=precision,
                                 preferred_element_type=jnp.float32)
        in_blk = (lane_full >= base) & (lane_full < base + PANEL)
        o_ref[...] = jnp.where(in_blk, 0.0, full) - update
        o_ref[base:base + PANEL, :] = panel

def neg_inverse(matrix):
    size = matrix.shape[-1]
    return pl.pallas_call(
        _sweep_kernel,
        out_shape=jax.ShapeDtypeStruct((size, size), jnp.float32),
        in_specs=[pl.BlockSpec(memory_space=pltpu.VMEM)],
        out_specs=pl.BlockSpec(memory_space=pltpu.VMEM),
    )(matrix)


def _filter_kernel(
    count_ref, obs_ref, root_row_ref, root_col_ref, trans_row_ref, trans_col_ref, process_ref,
    prior_ref, mean_ref, cov_ref, pred_ref, normal_ref,
):
    points = obs_ref.shape[1]
    eye = (
        lax.broadcasted_iota(jnp.int32, (points, points), 0)
        == lax.broadcasted_iota(jnp.int32, (points, points), 1)
    ).astype(jnp.float32)
    cov_ref[...] = prior_ref[...]
    a_col, b_col, c_col, d_col = (trans_col_ref[i] for i in range(4))
    a_row, b_row, c_row, d_row = (trans_row_ref[i:i + 1, :] for i in range(4))

    def step(t, mean):
        first = t == 0
        top = cov_ref[:points, :]
        bottom = cov_ref[points:, :]
        for rows, left_w, right_w in ((slice(0, points), a_col, b_col), (slice(points, None), c_col, d_col)):
            forward = left_w * top + right_w * bottom
            f_left = forward[:, :points]
            f_right = forward[:, points:]
            pred_ref[rows, :points] = f_left * a_row + f_right * b_row
            pred_ref[rows, points:] = f_left * c_row + f_right * d_row
        cov_pred = jnp.where(first, prior_ref[...], pred_ref[...] + process_ref[...])
        m_top = mean[:, :points]
        m_bottom = mean[:, points:]
        mean_fwd = jnp.concatenate(
            [a_row * m_top + b_row * m_bottom, c_row * m_top + d_row * m_bottom], axis=1
        )
        mean_pred = jnp.where(first, 0.0, mean_fwd)
        r_col = root_col_ref[t]
        r_row = root_row_ref[pl.ds(t, 1), :]
        obs_row = obs_ref[pl.ds(t, 1), :]
        normal_ref[...] = eye + r_col * cov_pred[:points, :points] * r_row
        _sweep_in_place(normal_ref)
        scaled = r_col * cov_pred[:points, :]
        solved = jnp.dot(normal_ref[...], scaled, precision=KERNEL_PRECISION, preferred_element_type=jnp.float32)
        correction = lax.dot_general(
            scaled, solved, (((0,), (0,)), ((), ())), precision=KERNEL_PRECISION,
            preferred_element_type=jnp.float32,
        )
        cov_ref[...] = cov_pred + correction
        innovation = jnp.broadcast_to(r_row * (obs_row - mean_pred[:, :points]), (8, points))
        mean_shift = jnp.dot(innovation, solved, precision=KERNEL_PRECISION, preferred_element_type=jnp.float32)
        return mean_pred - mean_shift[0:1, :]

    mean_ref[...] = lax.fori_loop(0, count_ref[0], step, jnp.zeros((1, 2 * points), jnp.float32))


def run_filter(count, obs_all, root_all, transit, process, prior):
    total, points = obs_all.shape
    width = 2 * points
    vmem = pl.BlockSpec(memory_space=pltpu.VMEM)
    return pl.pallas_call(
        _filter_kernel,
        out_shape=(
            jax.ShapeDtypeStruct((1, width), jnp.float32),
            jax.ShapeDtypeStruct((width, width), jnp.float32),
        ),
        in_specs=[pl.BlockSpec(memory_space=pltpu.SMEM)] + [vmem] * 7,
        out_specs=(vmem, vmem),
        scratch_shapes=[
            pltpu.VMEM((width, width), jnp.float32),
            pltpu.VMEM((points, points), jnp.float32),
        ],
    )(
        jnp.reshape(count, (1,)).astype(jnp.int32),
        obs_all,
        root_all,
        root_all[:, :, None],
        transit,
        transit[:, :, None],
        process,
        prior,
    )


def matmul_hi(left, right):
    return jnp.matmul(left, right, precision=HIGHEST)


def swap_last(matrix):
    return jnp.swapaxes(matrix, -1, -2)


def apply_trans(transit, matrix):
    points = transit.shape[1]
    upper_half = matrix[..., :points, :]
    lower_half = matrix[..., points:, :]
    return jnp.concatenate(
        [
            transit[0][:, None] * upper_half + transit[1][:, None] * lower_half,
            transit[2][:, None] * upper_half + transit[3][:, None] * lower_half,
        ],
        axis=-2,
    )


def build_model(decay_rates, spatial_cov):
    decay_one = jnp.exp(-decay_rates)
    transit = jnp.stack(
        [
            decay_one * (1.0 + decay_rates),
            decay_one * decay_rates,
            -decay_one * decay_rates,
            decay_one * (1.0 - decay_rates),
        ]
    )
    decay_two = jnp.exp(-2.0 * decay_rates)
    var_ff = 1.0 - decay_two * (1.0 + 2.0 * decay_rates + 2.0 * decay_rates * decay_rates)
    cov_fg = 2.0 * decay_rates * decay_rates * decay_two
    var_gg = 1.0 - decay_two * (1.0 - 2.0 * decay_rates + 2.0 * decay_rates * decay_rates)
    fac_ff = jnp.sqrt(var_ff)
    fac_gf = cov_fg / fac_ff
    fac_gg = jnp.sqrt(var_gg - fac_gf * fac_gf)

    def scaled(left, right):
        return left[:, None] * spatial_cov * right[None, :]

    zero_block = jnp.zeros_like(spatial_cov)
    process = jnp.block(
        [
            [scaled(fac_ff, fac_ff), scaled(fac_ff, fac_gf)],
            [scaled(fac_gf, fac_ff), scaled(fac_gf, fac_gf) + scaled(fac_gg, fac_gg)],
        ]
    )
    process = process + JITTER * jnp.eye(2 * spatial_cov.shape[0], dtype=jnp.float32)
    prior = jnp.block([[spatial_cov, zero_block], [zero_block, spatial_cov]])
    return (transit, process, prior)


def predict(transit, process, mean, cov):
    forward_cov = apply_trans(transit, cov)
    cov_pred = apply_trans(transit, swap_last(forward_cov)) + process
    mean_pred = apply_trans(transit, mean[:, None])[:, 0]
    return mean_pred, cov_pred


def kalman_update(mean_pred, cov_pred, obs, root):
    points = obs.shape[-1]
    normal = jnp.eye(points, dtype=jnp.float32) + root[:, None] * cov_pred[:points, :points] * root[None, :]
    neg_inv = neg_inverse(normal)
    innovation = root * (obs - mean_pred[:points])
    scaled = root[:, None] * cov_pred[:points, :]
    rhs = jnp.concatenate([scaled, innovation[:, None]], axis=1)
    solved = matmul_hi(neg_inv, rhs)
    correction = matmul_hi(swap_last(scaled), solved)
    cov_new = cov_pred + correction[:, :-1]
    mean_new = mean_pred - correction[:, -1]
    return mean_new, cov_new


def smoother_elements(means, covs, last_flag, transit, process):
    forward_cov = apply_trans(transit, covs)
    predicted = apply_trans(transit, swap_last(forward_cov)) + process
    neg_inv = jax.vmap(neg_inverse)(predicted)
    gains = -matmul_hi(swap_last(forward_cov), neg_inv)
    gains = gains * (1.0 - last_flag.astype(jnp.float32))[:, None, None]
    forward_mean = apply_trans(transit, means[..., None])
    shift_means = means - matmul_hi(gains, forward_mean)[..., 0]
    shift_covs = covs - matmul_hi(gains, forward_cov)
    return (gains, shift_means, shift_covs)


def smooth_join(lower_el, higher_el):
    gain_a, mean_a, cov_a = lower_el
    gain_b, mean_b, cov_b = higher_el
    return (
        matmul_hi(gain_a, gain_b),
        matmul_hi(gain_a, mean_b[..., None])[..., 0] + mean_a,
        matmul_hi(matmul_hi(gain_a, cov_b), swap_last(gain_a)) + cov_a,
    )


def send_element(element, pairs):
    gain, mean, cov = element
    width = mean.shape[-1]
    packed = jnp.concatenate([cov, jnp.broadcast_to(mean[None], (8, width))], axis=0)
    recv_gain, recv_packed = lax.ppermute((gain, packed), "tm", pairs)
    return (recv_gain, recv_packed[width], recv_packed[:width])


def shards(observed, obs_masks, decay_rates, noise_var, spatial_cov):
    transit, process, prior = build_model(decay_rates, spatial_cov)
    local_steps, points = observed.shape
    width = 2 * points
    position = lax.axis_index("tm")
    tm_count = lax.axis_size("tm")
    total_steps = tm_count * local_steps

    root_local = jnp.sqrt(obs_masks.astype(jnp.float32) / noise_var)
    packed = jnp.stack([observed, root_local], axis=1)
    gathered = lax.all_gather(packed, "tm", tiled=True)
    obs_all = gathered[:, 0]
    root_all = gathered[:, 1]

    last_local = position * local_steps + (local_steps - 1)

    def filter_step(step, mean, cov):
        mean_pred, cov_pred = predict(transit, process, mean, cov)
        obs_now = lax.dynamic_index_in_dim(obs_all, step, keepdims=False)
        root_now = lax.dynamic_index_in_dim(root_all, step, keepdims=False)
        return kalman_update(mean_pred, cov_pred, obs_now, root_now)

    if local_steps == 1:
        mean_last, cov_last = run_filter(position + 1, obs_all, root_all, transit, process, prior)
        means = mean_last
        covs = cov_last[None]
    else:
        mean_first, cov_first = kalman_update(
            jnp.zeros((width,), jnp.float32), prior, obs_all[0], root_all[0]
        )
        mean_buf = jnp.zeros((local_steps, width), jnp.float32).at[0].set(mean_first)
        cov_buf = jnp.zeros((local_steps, width, width), jnp.float32).at[0].set(cov_first)

        def body(step, carry):
            mean, cov, mean_buf, cov_buf = carry
            mean, cov = filter_step(step, mean, cov)
            slot = step % local_steps
            mean_buf = lax.dynamic_update_index_in_dim(mean_buf, mean, slot, 0)
            cov_buf = lax.dynamic_update_index_in_dim(cov_buf, cov, slot, 0)
            return (mean, cov, mean_buf, cov_buf)

        _, _, means, covs = lax.fori_loop(
            1, last_local + 1, body, (mean_first, cov_first, mean_buf, cov_buf)
        )

    global_step = position * local_steps + jnp.arange(local_steps)
    last_flag = global_step == total_steps - 1
    if local_steps == 1:

        def compute_elements(operand):
            return smoother_elements(operand[0], operand[1], last_flag, transit, process)

        def final_elements(operand):
            return (jnp.zeros_like(operand[1]), operand[0], operand[1])

        smooth = lax.cond(position == tm_count - 1, final_elements, compute_elements, (means, covs))
    else:
        smooth = smoother_elements(means, covs, last_flag, transit, process)

    if local_steps > 1:
        last_el = jax.tree.map(lambda leaf: leaf[-1], smooth)
        front_els = jax.tree.map(lambda leaf: leaf[:-1], smooth)

        def backward(running, element):
            joined = smooth_join(element, running)
            return (joined, joined)

        _, head_els = lax.scan(backward, last_el, front_els, reverse=True)
        suffixes = jax.tree.map(
            lambda head_leaf, last_leaf: jnp.concatenate([head_leaf, last_leaf[None]], axis=0),
            head_els,
            last_el,
        )
        block_total = jax.tree.map(lambda leaf: leaf[0], suffixes)
    else:
        block_total = jax.tree.map(lambda leaf: leaf[0], smooth)

    running = block_total
    shift = 1
    while shift < tm_count:
        pairs = [(source, source - shift) for source in range(shift, tm_count)]
        received = send_element(running, pairs)
        running = smooth_join(running, received)
        shift *= 2

    if local_steps == 1:
        return (running[1][None], running[2][None])
    pairs = [(source, source - 1) for source in range(1, tm_count)]
    after_mine = lax.ppermute(running, "tm", pairs)
    gains, shift_means, shift_covs = suffixes
    smooth_mean = matmul_hi(gains, after_mine[1][:, None])[..., 0] + shift_means
    smooth_cov = matmul_hi(matmul_hi(gains, after_mine[2]), swap_last(gains)) + shift_covs
    return (smooth_mean, smooth_cov)


def solution(mesh):
    placed = (
        P(("groups", "tm"), None),
        P(("groups", "tm"), None),
        P("groups"),
        P("groups"),
        P("groups", None),
    )
    return jax.shard_map(
        shards,
        mesh=mesh,
        in_specs=placed,
        out_specs=(P(("groups", "tm"), None), P(("groups", "tm"), None, None)),
        check_vma=False,
    )
```

```python
import jax
import jax.numpy as jnp
from jax import lax
from jax.experimental import pallas as pl
from jax.experimental.pallas import tpu as pltpu
from jax.sharding import PartitionSpec as P

HIGHEST = lax.Precision.HIGHEST
KERNEL_PRECISION = lax.Precision.HIGH
JITTER = 0.001
PANEL = 32


def _inv2(a, b, d):
    idet = 1.0 / (a * d - b * b)
    return d * idet, -b * idet, a * idet

def _inv4(m):
    a00, a01, a11 = _inv2(m[0][0], m[0][1], m[1][1])
    b = ((m[0][2], m[0][3]), (m[1][2], m[1][3]))
    x = [[a00 * b[0][j] + a01 * b[1][j] for j in range(2)], [a01 * b[0][j] + a11 * b[1][j] for j in range(2)]]
    s00 = m[2][2] - (b[0][0] * x[0][0] + b[1][0] * x[1][0])
    s01 = m[2][3] - (b[0][0] * x[0][1] + b[1][0] * x[1][1])
    s11 = m[3][3] - (b[0][1] * x[0][1] + b[1][1] * x[1][1])
    c00, c01, c11 = _inv2(s00, s01, s11)
    cm = ((c00, c01), (c01, c11))
    y = [[x[i][0] * cm[0][j] + x[i][1] * cm[1][j] for j in range(2)] for i in range(2)]
    am = ((a00, a01), (a01, a11))
    out = [[None] * 4 for _ in range(4)]
    for i in range(2):
        for j in range(2):
            out[i][j] = am[i][j] + y[i][0] * x[j][0] + y[i][1] * x[j][1]
            out[i][2 + j] = -y[i][j]
            out[2 + j][i] = -y[i][j]
            out[2 + i][2 + j] = cm[i][j]
    return out

def _sweep_kernel(a_ref, o_ref):
    o_ref[...] = a_ref[...]
    _sweep_in_place(o_ref)

def _sweep_in_place(o_ref):
    n = o_ref.shape[0]
    PANEL = 64 if n >= 256 else 32
    precision = HIGHEST if n >= 256 else KERNEL_PRECISION
    sub = lax.broadcasted_iota(jnp.int32, (PANEL, n), 0)
    lane = lax.broadcasted_iota(jnp.int32, (PANEL, n), 1)
    sub_col = lax.broadcasted_iota(jnp.int32, (PANEL, 1), 0)
    lane_full = lax.broadcasted_iota(jnp.int32, (n, n), 1)
    for blk in range(n // PANEL):
        base = blk * PANEL
        orig = o_ref[base:base + PANEL, :]
        panel = orig
        for t in range(0, PANEL, 4):
            rows = [sub == t + i for i in range(4)]
            cols = [lane == base + t + i for i in range(4)]
            cv = [jnp.sum(jnp.where(cols[i], panel, 0.0), axis=1, keepdims=True) for i in range(4)]
            rv = [jnp.sum(jnp.where(rows[i], panel, 0.0), axis=0, keepdims=True) for i in range(4)]
            m = [[None] * 4 for _ in range(4)]
            for i in range(4):
                for j in range(i, 4):
                    m[i][j] = jnp.sum(jnp.where(sub_col == t + i, cv[j], 0.0), axis=0, keepdims=True)
                    m[j][i] = m[i][j]
            mi = _inv4(m)
            nr = [mi[i][0] * rv[0] + mi[i][1] * rv[1] + mi[i][2] * rv[2] + mi[i][3] * rv[3] for i in range(4)]
            nc = [cv[0] * mi[0][j] + cv[1] * mi[1][j] + cv[2] * mi[2][j] + cv[3] * mi[3][j] for j in range(4)]
            rest = panel - cv[0] * nr[0] - cv[1] * nr[1] - cv[2] * nr[2] - cv[3] * nr[3]
            for j in range(4):
                rest = jnp.where(cols[j], nc[j], rest)
            for i in range(4):
                row_val = nr[i]
                for j in range(4):
                    row_val = jnp.where(cols[j], -mi[i][j], row_val)
                rest = jnp.where(rows[i], row_val, rest)
            panel = rest
        full = o_ref[...]
        update = lax.dot_general(orig, panel, (((0,), (0,)), ((), ())), precision=precision,
                                 preferred_element_type=jnp.float32)
        in_blk = (lane_full >= base) & (lane_full < base + PANEL)
        o_ref[...] = jnp.where(in_blk, 0.0, full) - update
        o_ref[base:base + PANEL, :] = panel

def neg_inverse(matrix):
    size = matrix.shape[-1]
    return pl.pallas_call(
        _sweep_kernel,
        out_shape=jax.ShapeDtypeStruct((size, size), jnp.float32),
        in_specs=[pl.BlockSpec(memory_space=pltpu.VMEM)],
        out_specs=pl.BlockSpec(memory_space=pltpu.VMEM),
    )(matrix)


def _filter_kernel(
    count_ref, obs_ref, root_row_ref, root_col_ref, trans_row_ref, trans_col_ref, process_ref,
    prior_ref, mean_ref, cov_ref, pred_ref, normal_ref,
):
    points = obs_ref.shape[1]
    eye = (
        lax.broadcasted_iota(jnp.int32, (points, points), 0)
        == lax.broadcasted_iota(jnp.int32, (points, points), 1)
    ).astype(jnp.float32)
    cov_ref[...] = prior_ref[...]
    a_col, b_col, c_col, d_col = (trans_col_ref[i] for i in range(4))
    a_row, b_row, c_row, d_row = (trans_row_ref[i:i + 1, :] for i in range(4))

    def step(t, mean):
        first = t == 0
        top = cov_ref[:points, :]
        bottom = cov_ref[points:, :]
        for rows, left_w, right_w in ((slice(0, points), a_col, b_col), (slice(points, None), c_col, d_col)):
            forward = left_w * top + right_w * bottom
            f_left = forward[:, :points]
            f_right = forward[:, points:]
            pred_ref[rows, :points] = f_left * a_row + f_right * b_row
            pred_ref[rows, points:] = f_left * c_row + f_right * d_row
        cov_pred = jnp.where(first, prior_ref[...], pred_ref[...] + process_ref[...])
        m_top = mean[:, :points]
        m_bottom = mean[:, points:]
        mean_fwd = jnp.concatenate(
            [a_row * m_top + b_row * m_bottom, c_row * m_top + d_row * m_bottom], axis=1
        )
        mean_pred = jnp.where(first, 0.0, mean_fwd)
        r_col = root_col_ref[t]
        r_row = root_row_ref[pl.ds(t, 1), :]
        obs_row = obs_ref[pl.ds(t, 1), :]
        normal_ref[...] = eye + r_col * cov_pred[:points, :points] * r_row
        _sweep_in_place(normal_ref)
        scaled = r_col * cov_pred[:points, :]
        solved = jnp.dot(normal_ref[...], scaled, precision=KERNEL_PRECISION, preferred_element_type=jnp.float32)
        correction = lax.dot_general(
            scaled, solved, (((0,), (0,)), ((), ())), precision=HIGHEST,
            preferred_element_type=jnp.float32,
        )
        cov_ref[...] = cov_pred + correction
        innovation = jnp.broadcast_to(r_row * (obs_row - mean_pred[:, :points]), (8, points))
        mean_shift = jnp.dot(innovation, solved, precision=HIGHEST, preferred_element_type=jnp.float32)
        return mean_pred - mean_shift[0:1, :]

    mean_ref[...] = lax.fori_loop(0, count_ref[0], step, jnp.zeros((1, 2 * points), jnp.float32))


def run_filter(count, obs_all, root_all, transit, process, prior):
    total, points = obs_all.shape
    width = 2 * points
    vmem = pl.BlockSpec(memory_space=pltpu.VMEM)
    return pl.pallas_call(
        _filter_kernel,
        out_shape=(
            jax.ShapeDtypeStruct((1, width), jnp.float32),
            jax.ShapeDtypeStruct((width, width), jnp.float32),
        ),
        in_specs=[pl.BlockSpec(memory_space=pltpu.SMEM)] + [vmem] * 7,
        out_specs=(vmem, vmem),
        scratch_shapes=[
            pltpu.VMEM((width, width), jnp.float32),
            pltpu.VMEM((points, points), jnp.float32),
        ],
    )(
        jnp.reshape(count, (1,)).astype(jnp.int32),
        obs_all,
        root_all,
        root_all[:, :, None],
        transit,
        transit[:, :, None],
        process,
        prior,
    )


def matmul_hi(left, right):
    return jnp.matmul(left, right, precision=HIGHEST)


def swap_last(matrix):
    return jnp.swapaxes(matrix, -1, -2)


def apply_trans(transit, matrix):
    points = transit.shape[1]
    upper_half = matrix[..., :points, :]
    lower_half = matrix[..., points:, :]
    return jnp.concatenate(
        [
            transit[0][:, None] * upper_half + transit[1][:, None] * lower_half,
            transit[2][:, None] * upper_half + transit[3][:, None] * lower_half,
        ],
        axis=-2,
    )


def build_model(decay_rates, spatial_cov):
    decay_one = jnp.exp(-decay_rates)
    transit = jnp.stack(
        [
            decay_one * (1.0 + decay_rates),
            decay_one * decay_rates,
            -decay_one * decay_rates,
            decay_one * (1.0 - decay_rates),
        ]
    )
    decay_two = jnp.exp(-2.0 * decay_rates)
    var_ff = 1.0 - decay_two * (1.0 + 2.0 * decay_rates + 2.0 * decay_rates * decay_rates)
    cov_fg = 2.0 * decay_rates * decay_rates * decay_two
    var_gg = 1.0 - decay_two * (1.0 - 2.0 * decay_rates + 2.0 * decay_rates * decay_rates)
    fac_ff = jnp.sqrt(var_ff)
    fac_gf = cov_fg / fac_ff
    fac_gg = jnp.sqrt(var_gg - fac_gf * fac_gf)

    def scaled(left, right):
        return left[:, None] * spatial_cov * right[None, :]

    zero_block = jnp.zeros_like(spatial_cov)
    process = jnp.block(
        [
            [scaled(fac_ff, fac_ff), scaled(fac_ff, fac_gf)],
            [scaled(fac_gf, fac_ff), scaled(fac_gf, fac_gf) + scaled(fac_gg, fac_gg)],
        ]
    )
    process = process + JITTER * jnp.eye(2 * spatial_cov.shape[0], dtype=jnp.float32)
    prior = jnp.block([[spatial_cov, zero_block], [zero_block, spatial_cov]])
    return (transit, process, prior)


def predict(transit, process, mean, cov):
    forward_cov = apply_trans(transit, cov)
    cov_pred = apply_trans(transit, swap_last(forward_cov)) + process
    mean_pred = apply_trans(transit, mean[:, None])[:, 0]
    return mean_pred, cov_pred


def kalman_update(mean_pred, cov_pred, obs, root):
    points = obs.shape[-1]
    normal = jnp.eye(points, dtype=jnp.float32) + root[:, None] * cov_pred[:points, :points] * root[None, :]
    neg_inv = neg_inverse(normal)
    innovation = root * (obs - mean_pred[:points])
    scaled = root[:, None] * cov_pred[:points, :]
    rhs = jnp.concatenate([scaled, innovation[:, None]], axis=1)
    solved = matmul_hi(neg_inv, rhs)
    correction = matmul_hi(swap_last(scaled), solved)
    cov_new = cov_pred + correction[:, :-1]
    mean_new = mean_pred - correction[:, -1]
    return mean_new, cov_new


def smoother_elements(means, covs, last_flag, transit, process):
    forward_cov = apply_trans(transit, covs)
    predicted = apply_trans(transit, swap_last(forward_cov)) + process
    neg_inv = jax.vmap(neg_inverse)(predicted)
    gains = -matmul_hi(swap_last(forward_cov), neg_inv)
    gains = gains * (1.0 - last_flag.astype(jnp.float32))[:, None, None]
    forward_mean = apply_trans(transit, means[..., None])
    shift_means = means - matmul_hi(gains, forward_mean)[..., 0]
    shift_covs = covs - matmul_hi(gains, forward_cov)
    return (gains, shift_means, shift_covs)


def smooth_join(lower_el, higher_el):
    gain_a, mean_a, cov_a = lower_el
    gain_b, mean_b, cov_b = higher_el
    return (
        matmul_hi(gain_a, gain_b),
        matmul_hi(gain_a, mean_b[..., None])[..., 0] + mean_a,
        matmul_hi(matmul_hi(gain_a, cov_b), swap_last(gain_a)) + cov_a,
    )


def send_element(element, pairs):
    gain, mean, cov = element
    width = mean.shape[-1]
    packed = jnp.concatenate([cov, jnp.broadcast_to(mean[None], (8, width))], axis=0)
    recv_gain, recv_packed = lax.ppermute((gain, packed), "tm", pairs)
    return (recv_gain, recv_packed[width], recv_packed[:width])


def shards(observed, obs_masks, decay_rates, noise_var, spatial_cov):
    transit, process, prior = build_model(decay_rates, spatial_cov)
    local_steps, points = observed.shape
    width = 2 * points
    position = lax.axis_index("tm")
    tm_count = lax.axis_size("tm")
    total_steps = tm_count * local_steps

    root_local = jnp.sqrt(obs_masks.astype(jnp.float32) / noise_var)
    packed = jnp.stack([observed, root_local], axis=1)
    gathered = lax.all_gather(packed, "tm", tiled=True)
    obs_all = gathered[:, 0]
    root_all = gathered[:, 1]

    last_local = position * local_steps + (local_steps - 1)

    def filter_step(step, mean, cov):
        mean_pred, cov_pred = predict(transit, process, mean, cov)
        obs_now = lax.dynamic_index_in_dim(obs_all, step, keepdims=False)
        root_now = lax.dynamic_index_in_dim(root_all, step, keepdims=False)
        return kalman_update(mean_pred, cov_pred, obs_now, root_now)

    if local_steps == 1:
        mean_last, cov_last = run_filter(position + 1, obs_all, root_all, transit, process, prior)
        means = mean_last
        covs = cov_last[None]
    else:
        mean_first, cov_first = kalman_update(
            jnp.zeros((width,), jnp.float32), prior, obs_all[0], root_all[0]
        )
        mean_buf = jnp.zeros((local_steps, width), jnp.float32).at[0].set(mean_first)
        cov_buf = jnp.zeros((local_steps, width, width), jnp.float32).at[0].set(cov_first)

        def body(step, carry):
            mean, cov, mean_buf, cov_buf = carry
            mean, cov = filter_step(step, mean, cov)
            slot = step % local_steps
            mean_buf = lax.dynamic_update_index_in_dim(mean_buf, mean, slot, 0)
            cov_buf = lax.dynamic_update_index_in_dim(cov_buf, cov, slot, 0)
            return (mean, cov, mean_buf, cov_buf)

        _, _, means, covs = lax.fori_loop(
            1, last_local + 1, body, (mean_first, cov_first, mean_buf, cov_buf)
        )

    global_step = position * local_steps + jnp.arange(local_steps)
    last_flag = global_step == total_steps - 1
    if local_steps == 1:

        def compute_elements(operand):
            return smoother_elements(operand[0], operand[1], last_flag, transit, process)

        def final_elements(operand):
            return (jnp.zeros_like(operand[1]), operand[0], operand[1])

        smooth = lax.cond(position == tm_count - 1, final_elements, compute_elements, (means, covs))
    else:
        smooth = smoother_elements(means, covs, last_flag, transit, process)

    if local_steps > 1:
        last_el = jax.tree.map(lambda leaf: leaf[-1], smooth)
        front_els = jax.tree.map(lambda leaf: leaf[:-1], smooth)

        def backward(running, element):
            joined = smooth_join(element, running)
            return (joined, joined)

        _, head_els = lax.scan(backward, last_el, front_els, reverse=True)
        suffixes = jax.tree.map(
            lambda head_leaf, last_leaf: jnp.concatenate([head_leaf, last_leaf[None]], axis=0),
            head_els,
            last_el,
        )
        block_total = jax.tree.map(lambda leaf: leaf[0], suffixes)
    else:
        block_total = jax.tree.map(lambda leaf: leaf[0], smooth)

    running = block_total
    shift = 1
    while shift < tm_count:
        pairs = [(source, source - shift) for source in range(shift, tm_count)]
        received = send_element(running, pairs)
        running = smooth_join(running, received)
        shift *= 2

    if local_steps == 1:
        return (running[1][None], running[2][None])
    pairs = [(source, source - 1) for source in range(1, tm_count)]
    after_mine = lax.ppermute(running, "tm", pairs)
    gains, shift_means, shift_covs = suffixes
    smooth_mean = matmul_hi(gains, after_mine[1][:, None])[..., 0] + shift_means
    smooth_cov = matmul_hi(matmul_hi(gains, after_mine[2]), swap_last(gains)) + shift_covs
    return (smooth_mean, smooth_cov)


def solution(mesh):
    placed = (
        P(("groups", "tm"), None),
        P(("groups", "tm"), None),
        P("groups"),
        P("groups"),
        P("groups", None),
    )
    return jax.shard_map(
        shards,
        mesh=mesh,
        in_specs=placed,
        out_specs=(P(("groups", "tm"), None), P(("groups", "tm"), None, None)),
        check_vma=False,
    )
```

```python
import jax
import jax.numpy as jnp
from jax import lax
from jax.experimental import pallas as pl
from jax.experimental.pallas import tpu as pltpu
from jax.sharding import PartitionSpec as P

HIGHEST = lax.Precision.HIGHEST
JITTER = 0.001
PANEL = 32


def _inv2(a, b, d):
    idet = 1.0 / (a * d - b * b)
    return d * idet, -b * idet, a * idet

def _inv4(m):
    a00, a01, a11 = _inv2(m[0][0], m[0][1], m[1][1])
    b = ((m[0][2], m[0][3]), (m[1][2], m[1][3]))
    x = [[a00 * b[0][j] + a01 * b[1][j] for j in range(2)], [a01 * b[0][j] + a11 * b[1][j] for j in range(2)]]
    s00 = m[2][2] - (b[0][0] * x[0][0] + b[1][0] * x[1][0])
    s01 = m[2][3] - (b[0][0] * x[0][1] + b[1][0] * x[1][1])
    s11 = m[3][3] - (b[0][1] * x[0][1] + b[1][1] * x[1][1])
    c00, c01, c11 = _inv2(s00, s01, s11)
    cm = ((c00, c01), (c01, c11))
    y = [[x[i][0] * cm[0][j] + x[i][1] * cm[1][j] for j in range(2)] for i in range(2)]
    am = ((a00, a01), (a01, a11))
    out = [[None] * 4 for _ in range(4)]
    for i in range(2):
        for j in range(2):
            out[i][j] = am[i][j] + y[i][0] * x[j][0] + y[i][1] * x[j][1]
            out[i][2 + j] = -y[i][j]
            out[2 + j][i] = -y[i][j]
            out[2 + i][2 + j] = cm[i][j]
    return out

def _sweep_kernel(a_ref, o_ref):
    o_ref[...] = a_ref[...]
    _sweep_in_place(o_ref)

def _sweep_in_place(o_ref):
    n = o_ref.shape[0]
    PANEL = 64 if n >= 256 else 32
    sub = lax.broadcasted_iota(jnp.int32, (PANEL, n), 0)
    lane = lax.broadcasted_iota(jnp.int32, (PANEL, n), 1)
    sub_col = lax.broadcasted_iota(jnp.int32, (PANEL, 1), 0)
    lane_full = lax.broadcasted_iota(jnp.int32, (n, n), 1)
    for blk in range(n // PANEL):
        base = blk * PANEL
        orig = o_ref[base:base + PANEL, :]
        panel = orig
        for t in range(0, PANEL, 4):
            rows = [sub == t + i for i in range(4)]
            cols = [lane == base + t + i for i in range(4)]
            cv = [jnp.sum(jnp.where(cols[i], panel, 0.0), axis=1, keepdims=True) for i in range(4)]
            rv = [jnp.sum(jnp.where(rows[i], panel, 0.0), axis=0, keepdims=True) for i in range(4)]
            m = [[None] * 4 for _ in range(4)]
            for i in range(4):
                for j in range(i, 4):
                    m[i][j] = jnp.sum(jnp.where(sub_col == t + i, cv[j], 0.0), axis=0, keepdims=True)
                    m[j][i] = m[i][j]
            mi = _inv4(m)
            nr = [mi[i][0] * rv[0] + mi[i][1] * rv[1] + mi[i][2] * rv[2] + mi[i][3] * rv[3] for i in range(4)]
            nc = [cv[0] * mi[0][j] + cv[1] * mi[1][j] + cv[2] * mi[2][j] + cv[3] * mi[3][j] for j in range(4)]
            rest = panel - cv[0] * nr[0] - cv[1] * nr[1] - cv[2] * nr[2] - cv[3] * nr[3]
            for j in range(4):
                rest = jnp.where(cols[j], nc[j], rest)
            for i in range(4):
                row_val = nr[i]
                for j in range(4):
                    row_val = jnp.where(cols[j], -mi[i][j], row_val)
                rest = jnp.where(rows[i], row_val, rest)
            panel = rest
        full = o_ref[...]
        update = lax.dot_general(orig, panel, (((0,), (0,)), ((), ())), precision=HIGHEST,
                                 preferred_element_type=jnp.float32)
        in_blk = (lane_full >= base) & (lane_full < base + PANEL)
        o_ref[...] = jnp.where(in_blk, 0.0, full) - update
        o_ref[base:base + PANEL, :] = panel

def neg_inverse(matrix):
    size = matrix.shape[-1]
    return pl.pallas_call(
        _sweep_kernel,
        out_shape=jax.ShapeDtypeStruct((size, size), jnp.float32),
        in_specs=[pl.BlockSpec(memory_space=pltpu.VMEM)],
        out_specs=pl.BlockSpec(memory_space=pltpu.VMEM),
    )(matrix)


def _filter_kernel(
    count_ref, obs_ref, root_row_ref, root_col_ref, trans_row_ref, trans_col_ref, process_ref,
    prior_ref, mean_ref, cov_ref, gain_ref, shift_mean_ref, shift_cov_ref, pred_ref, normal_ref,
    forward_ref, wide_ref,
):
    points = obs_ref.shape[1]
    eye = (
        lax.broadcasted_iota(jnp.int32, (points, points), 0)
        == lax.broadcasted_iota(jnp.int32, (points, points), 1)
    ).astype(jnp.float32)
    cov_ref[...] = prior_ref[...]
    a_col, b_col, c_col, d_col = (trans_col_ref[i] for i in range(4))
    a_row, b_row, c_row, d_row = (trans_row_ref[i:i + 1, :] for i in range(4))

    def step(t, mean):
        first = t == 0
        top = cov_ref[:points, :]
        bottom = cov_ref[points:, :]
        for rows, left_w, right_w in ((slice(0, points), a_col, b_col), (slice(points, None), c_col, d_col)):
            forward = left_w * top + right_w * bottom
            f_left = forward[:, :points]
            f_right = forward[:, points:]
            pred_ref[rows, :points] = f_left * a_row + f_right * b_row
            pred_ref[rows, points:] = f_left * c_row + f_right * d_row
        cov_pred = jnp.where(first, prior_ref[...], pred_ref[...] + process_ref[...])
        m_top = mean[:, :points]
        m_bottom = mean[:, points:]
        mean_fwd = jnp.concatenate(
            [a_row * m_top + b_row * m_bottom, c_row * m_top + d_row * m_bottom], axis=1
        )
        mean_pred = jnp.where(first, 0.0, mean_fwd)
        r_col = root_col_ref[t]
        r_row = root_row_ref[pl.ds(t, 1), :]
        obs_row = obs_ref[pl.ds(t, 1), :]
        normal_ref[...] = eye + r_col * cov_pred[:points, :points] * r_row
        _sweep_in_place(normal_ref)
        scaled = r_col * cov_pred[:points, :]
        solved = jnp.dot(normal_ref[...], scaled, precision=HIGHEST, preferred_element_type=jnp.float32)
        correction = lax.dot_general(
            scaled, solved, (((0,), (0,)), ((), ())), precision=HIGHEST,
            preferred_element_type=jnp.float32,
        )
        cov_ref[...] = cov_pred + correction
        innovation = jnp.broadcast_to(r_row * (obs_row - mean_pred[:, :points]), (8, points))
        mean_shift = jnp.dot(innovation, solved, precision=HIGHEST, preferred_element_type=jnp.float32)
        return mean_pred - mean_shift[0:1, :]

    mean_last = lax.fori_loop(0, count_ref[0], step, jnp.zeros((1, 2 * points), jnp.float32))
    mean_ref[...] = mean_last

    @pl.when(count_ref[1] == 0)
    def _final_step():
        gain_ref[...] = jnp.zeros_like(gain_ref)
        shift_mean_ref[...] = mean_last
        shift_cov_ref[...] = cov_ref[...]

    @pl.when(count_ref[1] != 0)
    def _smoother_element():
        top = cov_ref[:points, :]
        bottom = cov_ref[points:, :]
        forward_ref[:points, :] = a_col * top + b_col * bottom
        forward_ref[points:, :] = c_col * top + d_col * bottom
        forward = forward_ref[...]
        f_left = forward[:, :points]
        f_right = forward[:, points:]
        wide_ref[:, :points] = f_left * a_row + f_right * b_row
        wide_ref[:, points:] = f_left * c_row + f_right * d_row
        wide_ref[...] = wide_ref[...] + process_ref[...]
        _sweep_in_place(wide_ref)
        gain = -lax.dot_general(
            forward, wide_ref[...], (((0,), (0,)), ((), ())), precision=HIGHEST,
            preferred_element_type=jnp.float32,
        )
        gain_ref[...] = gain
        m_top = mean_last[:, :points]
        m_bottom = mean_last[:, points:]
        mean_fwd = jnp.broadcast_to(
            jnp.concatenate([a_row * m_top + b_row * m_bottom, c_row * m_top + d_row * m_bottom], axis=1),
            (8, 2 * points),
        )
        mean_shift = lax.dot_general(
            mean_fwd, gain, (((1,), (1,)), ((), ())), precision=HIGHEST,
            preferred_element_type=jnp.float32,
        )
        shift_mean_ref[...] = mean_last - mean_shift[0:1, :]
        shift_cov_ref[...] = cov_ref[...] - jnp.dot(
            gain, forward, precision=HIGHEST, preferred_element_type=jnp.float32
        )


def run_filter(count, not_last, obs_all, root_all, transit, process, prior):
    total, points = obs_all.shape
    width = 2 * points
    vmem = pl.BlockSpec(memory_space=pltpu.VMEM)
    square = jax.ShapeDtypeStruct((width, width), jnp.float32)
    row = jax.ShapeDtypeStruct((1, width), jnp.float32)
    return pl.pallas_call(
        _filter_kernel,
        out_shape=(row, square, square, row, square),
        in_specs=[pl.BlockSpec(memory_space=pltpu.SMEM)] + [vmem] * 7,
        out_specs=(vmem,) * 5,
        scratch_shapes=[
            pltpu.VMEM((width, width), jnp.float32),
            pltpu.VMEM((points, points), jnp.float32),
            pltpu.VMEM((width, width), jnp.float32),
            pltpu.VMEM((width, width), jnp.float32),
        ],
    )(
        jnp.stack([count, not_last]).astype(jnp.int32),
        obs_all,
        root_all,
        root_all[:, :, None],
        transit,
        transit[:, :, None],
        process,
        prior,
    )


def matmul_hi(left, right):
    return jnp.matmul(left, right, precision=HIGHEST)


def swap_last(matrix):
    return jnp.swapaxes(matrix, -1, -2)


def apply_trans(transit, matrix):
    points = transit.shape[1]
    upper_half = matrix[..., :points, :]
    lower_half = matrix[..., points:, :]
    return jnp.concatenate(
        [
            transit[0][:, None] * upper_half + transit[1][:, None] * lower_half,
            transit[2][:, None] * upper_half + transit[3][:, None] * lower_half,
        ],
        axis=-2,
    )


def build_model(decay_rates, spatial_cov):
    decay_one = jnp.exp(-decay_rates)
    transit = jnp.stack(
        [
            decay_one * (1.0 + decay_rates),
            decay_one * decay_rates,
            -decay_one * decay_rates,
            decay_one * (1.0 - decay_rates),
        ]
    )
    decay_two = jnp.exp(-2.0 * decay_rates)
    var_ff = 1.0 - decay_two * (1.0 + 2.0 * decay_rates + 2.0 * decay_rates * decay_rates)
    cov_fg = 2.0 * decay_rates * decay_rates * decay_two
    var_gg = 1.0 - decay_two * (1.0 - 2.0 * decay_rates + 2.0 * decay_rates * decay_rates)
    fac_ff = jnp.sqrt(var_ff)
    fac_gf = cov_fg / fac_ff
    fac_gg = jnp.sqrt(var_gg - fac_gf * fac_gf)

    def scaled(left, right):
        return left[:, None] * spatial_cov * right[None, :]

    zero_block = jnp.zeros_like(spatial_cov)
    process = jnp.block(
        [
            [scaled(fac_ff, fac_ff), scaled(fac_ff, fac_gf)],
            [scaled(fac_gf, fac_ff), scaled(fac_gf, fac_gf) + scaled(fac_gg, fac_gg)],
        ]
    )
    process = process + JITTER * jnp.eye(2 * spatial_cov.shape[0], dtype=jnp.float32)
    prior = jnp.block([[spatial_cov, zero_block], [zero_block, spatial_cov]])
    return (transit, process, prior)


def predict(transit, process, mean, cov):
    forward_cov = apply_trans(transit, cov)
    cov_pred = apply_trans(transit, swap_last(forward_cov)) + process
    mean_pred = apply_trans(transit, mean[:, None])[:, 0]
    return mean_pred, cov_pred


def kalman_update(mean_pred, cov_pred, obs, root):
    points = obs.shape[-1]
    normal = jnp.eye(points, dtype=jnp.float32) + root[:, None] * cov_pred[:points, :points] * root[None, :]
    neg_inv = neg_inverse(normal)
    innovation = root * (obs - mean_pred[:points])
    scaled = root[:, None] * cov_pred[:points, :]
    rhs = jnp.concatenate([scaled, innovation[:, None]], axis=1)
    solved = matmul_hi(neg_inv, rhs)
    correction = matmul_hi(swap_last(scaled), solved)
    cov_new = cov_pred + correction[:, :-1]
    mean_new = mean_pred - correction[:, -1]
    return mean_new, cov_new


def smoother_elements(means, covs, last_flag, transit, process):
    forward_cov = apply_trans(transit, covs)
    predicted = apply_trans(transit, swap_last(forward_cov)) + process
    neg_inv = jax.vmap(neg_inverse)(predicted)
    gains = -matmul_hi(swap_last(forward_cov), neg_inv)
    gains = gains * (1.0 - last_flag.astype(jnp.float32))[:, None, None]
    forward_mean = apply_trans(transit, means[..., None])
    shift_means = means - matmul_hi(gains, forward_mean)[..., 0]
    shift_covs = covs - matmul_hi(gains, forward_cov)
    return (gains, shift_means, shift_covs)


def smooth_join(lower_el, higher_el):
    gain_a, mean_a, cov_a = lower_el
    gain_b, mean_b, cov_b = higher_el
    return (
        matmul_hi(gain_a, gain_b),
        matmul_hi(gain_a, mean_b[..., None])[..., 0] + mean_a,
        matmul_hi(matmul_hi(gain_a, cov_b), swap_last(gain_a)) + cov_a,
    )


def send_element(element, pairs):
    gain, mean, cov = element
    width = mean.shape[-1]
    packed = jnp.concatenate([cov, jnp.broadcast_to(mean[None], (8, width))], axis=0)
    recv_gain, recv_packed = lax.ppermute((gain, packed), "tm", pairs)
    return (recv_gain, recv_packed[width], recv_packed[:width])


def shards(observed, obs_masks, decay_rates, noise_var, spatial_cov):
    transit, process, prior = build_model(decay_rates, spatial_cov)
    local_steps, points = observed.shape
    width = 2 * points
    position = lax.axis_index("tm")
    tm_count = lax.axis_size("tm")
    total_steps = tm_count * local_steps

    root_local = jnp.sqrt(obs_masks.astype(jnp.float32) / noise_var)
    packed = jnp.stack([observed, root_local], axis=1)
    gathered = lax.all_gather(packed, "tm", tiled=True)
    obs_all = gathered[:, 0]
    root_all = gathered[:, 1]

    last_local = position * local_steps + (local_steps - 1)

    def filter_step(step, mean, cov):
        mean_pred, cov_pred = predict(transit, process, mean, cov)
        obs_now = lax.dynamic_index_in_dim(obs_all, step, keepdims=False)
        root_now = lax.dynamic_index_in_dim(root_all, step, keepdims=False)
        return kalman_update(mean_pred, cov_pred, obs_now, root_now)

    if local_steps == 1:
        not_last = (position != tm_count - 1).astype(jnp.int32)
        _, _, gain_k, shift_mean_k, shift_cov_k = run_filter(
            position + 1, not_last, obs_all, root_all, transit, process, prior
        )
    else:
        mean_first, cov_first = kalman_update(
            jnp.zeros((width,), jnp.float32), prior, obs_all[0], root_all[0]
        )
        mean_buf = jnp.zeros((local_steps, width), jnp.float32).at[0].set(mean_first)
        cov_buf = jnp.zeros((local_steps, width, width), jnp.float32).at[0].set(cov_first)

        def body(step, carry):
            mean, cov, mean_buf, cov_buf = carry
            mean, cov = filter_step(step, mean, cov)
            slot = step % local_steps
            mean_buf = lax.dynamic_update_index_in_dim(mean_buf, mean, slot, 0)
            cov_buf = lax.dynamic_update_index_in_dim(cov_buf, cov, slot, 0)
            return (mean, cov, mean_buf, cov_buf)

        _, _, means, covs = lax.fori_loop(
            1, last_local + 1, body, (mean_first, cov_first, mean_buf, cov_buf)
        )

    global_step = position * local_steps + jnp.arange(local_steps)
    last_flag = global_step == total_steps - 1
    if local_steps == 1:
        smooth = (gain_k[None], shift_mean_k, shift_cov_k[None])
    else:
        smooth = smoother_elements(means, covs, last_flag, transit, process)

    if local_steps > 1:
        last_el = jax.tree.map(lambda leaf: leaf[-1], smooth)
        front_els = jax.tree.map(lambda leaf: leaf[:-1], smooth)

        def backward(running, element):
            joined = smooth_join(element, running)
            return (joined, joined)

        _, head_els = lax.scan(backward, last_el, front_els, reverse=True)
        suffixes = jax.tree.map(
            lambda head_leaf, last_leaf: jnp.concatenate([head_leaf, last_leaf[None]], axis=0),
            head_els,
            last_el,
        )
        block_total = jax.tree.map(lambda leaf: leaf[0], suffixes)
    else:
        block_total = jax.tree.map(lambda leaf: leaf[0], smooth)

    running = block_total
    shift = 1
    while shift < tm_count:
        pairs = [(source, source - shift) for source in range(shift, tm_count)]
        received = send_element(running, pairs)
        running = smooth_join(running, received)
        shift *= 2

    if local_steps == 1:
        return (running[1][None], running[2][None])
    pairs = [(source, source - 1) for source in range(1, tm_count)]
    after_mine = lax.ppermute(running, "tm", pairs)
    gains, shift_means, shift_covs = suffixes
    smooth_mean = matmul_hi(gains, after_mine[1][:, None])[..., 0] + shift_means
    smooth_cov = matmul_hi(matmul_hi(gains, after_mine[2]), swap_last(gains)) + shift_covs
    return (smooth_mean, smooth_cov)


def solution(mesh):
    placed = (
        P(("groups", "tm"), None),
        P(("groups", "tm"), None),
        P("groups"),
        P("groups"),
        P("groups", None),
    )
    return jax.shard_map(
        shards,
        mesh=mesh,
        in_specs=placed,
        out_specs=(P(("groups", "tm"), None), P(("groups", "tm"), None, None)),
        check_vma=False,
    )
```

```python
import jax
import jax.numpy as jnp
from jax import lax
from jax.experimental import pallas as pl
from jax.experimental.pallas import tpu as pltpu
from jax.sharding import PartitionSpec as P

HIGHEST = lax.Precision.HIGHEST
JITTER = 0.001
PANEL = 32


def _inv2(a, b, d):
    idet = 1.0 / (a * d - b * b)
    return d * idet, -b * idet, a * idet

def _inv4(m):
    a00, a01, a11 = _inv2(m[0][0], m[0][1], m[1][1])
    b = ((m[0][2], m[0][3]), (m[1][2], m[1][3]))
    x = [[a00 * b[0][j] + a01 * b[1][j] for j in range(2)], [a01 * b[0][j] + a11 * b[1][j] for j in range(2)]]
    s00 = m[2][2] - (b[0][0] * x[0][0] + b[1][0] * x[1][0])
    s01 = m[2][3] - (b[0][0] * x[0][1] + b[1][0] * x[1][1])
    s11 = m[3][3] - (b[0][1] * x[0][1] + b[1][1] * x[1][1])
    c00, c01, c11 = _inv2(s00, s01, s11)
    cm = ((c00, c01), (c01, c11))
    y = [[x[i][0] * cm[0][j] + x[i][1] * cm[1][j] for j in range(2)] for i in range(2)]
    am = ((a00, a01), (a01, a11))
    out = [[None] * 4 for _ in range(4)]
    for i in range(2):
        for j in range(2):
            out[i][j] = am[i][j] + y[i][0] * x[j][0] + y[i][1] * x[j][1]
            out[i][2 + j] = -y[i][j]
            out[2 + j][i] = -y[i][j]
            out[2 + i][2 + j] = cm[i][j]
    return out

def _sweep_kernel(a_ref, o_ref):
    o_ref[...] = a_ref[...]
    _sweep_in_place(o_ref)

def _sweep_in_place(o_ref):
    n = o_ref.shape[0]
    PANEL = 64 if n >= 256 else 32
    sub = lax.broadcasted_iota(jnp.int32, (PANEL, n), 0)
    lane = lax.broadcasted_iota(jnp.int32, (PANEL, n), 1)
    sub_col = lax.broadcasted_iota(jnp.int32, (PANEL, 1), 0)
    lane_full = lax.broadcasted_iota(jnp.int32, (n, n), 1)
    for blk in range(n // PANEL):
        base = blk * PANEL
        orig = o_ref[base:base + PANEL, :]
        panel = orig
        for t in range(0, PANEL, 4):
            rows = [sub == t + i for i in range(4)]
            cols = [lane == base + t + i for i in range(4)]
            cv = [jnp.sum(jnp.where(cols[i], panel, 0.0), axis=1, keepdims=True) for i in range(4)]
            rv = [jnp.sum(jnp.where(rows[i], panel, 0.0), axis=0, keepdims=True) for i in range(4)]
            m = [[None] * 4 for _ in range(4)]
            for i in range(4):
                for j in range(i, 4):
                    m[i][j] = jnp.sum(jnp.where(sub_col == t + i, cv[j], 0.0), axis=0, keepdims=True)
                    m[j][i] = m[i][j]
            mi = _inv4(m)
            nr = [mi[i][0] * rv[0] + mi[i][1] * rv[1] + mi[i][2] * rv[2] + mi[i][3] * rv[3] for i in range(4)]
            nc = [cv[0] * mi[0][j] + cv[1] * mi[1][j] + cv[2] * mi[2][j] + cv[3] * mi[3][j] for j in range(4)]
            rest = panel - cv[0] * nr[0] - cv[1] * nr[1] - cv[2] * nr[2] - cv[3] * nr[3]
            for j in range(4):
                rest = jnp.where(cols[j], nc[j], rest)
            for i in range(4):
                row_val = nr[i]
                for j in range(4):
                    row_val = jnp.where(cols[j], -mi[i][j], row_val)
                rest = jnp.where(rows[i], row_val, rest)
            panel = rest
        full = o_ref[...]
        update = lax.dot_general(orig, panel, (((0,), (0,)), ((), ())), precision=HIGHEST,
                                 preferred_element_type=jnp.float32)
        in_blk = (lane_full >= base) & (lane_full < base + PANEL)
        o_ref[...] = jnp.where(in_blk, 0.0, full) - update
        o_ref[base:base + PANEL, :] = panel

def neg_inverse(matrix):
    size = matrix.shape[-1]
    return pl.pallas_call(
        _sweep_kernel,
        out_shape=jax.ShapeDtypeStruct((size, size), jnp.float32),
        in_specs=[pl.BlockSpec(memory_space=pltpu.VMEM)],
        out_specs=pl.BlockSpec(memory_space=pltpu.VMEM),
    )(matrix)


def _filter_kernel(
    count_ref, obs_ref, root_row_ref, root_col_ref, trans_row_ref, trans_col_ref, process_ref,
    prior_ref, mean_ref, cov_ref, pred_ref, normal_ref,
):
    points = obs_ref.shape[1]
    eye = (
        lax.broadcasted_iota(jnp.int32, (points, points), 0)
        == lax.broadcasted_iota(jnp.int32, (points, points), 1)
    ).astype(jnp.float32)
    cov_ref[...] = prior_ref[...]
    a_col, b_col, c_col, d_col = (trans_col_ref[i] for i in range(4))
    a_row, b_row, c_row, d_row = (trans_row_ref[i:i + 1, :] for i in range(4))

    def step(t, mean):
        first = t == 0
        top = cov_ref[:points, :]
        bottom = cov_ref[points:, :]
        for rows, left_w, right_w in ((slice(0, points), a_col, b_col), (slice(points, None), c_col, d_col)):
            forward = left_w * top + right_w * bottom
            f_left = forward[:, :points]
            f_right = forward[:, points:]
            pred_ref[rows, :points] = f_left * a_row + f_right * b_row
            pred_ref[rows, points:] = f_left * c_row + f_right * d_row
        cov_pred = jnp.where(first, prior_ref[...], pred_ref[...] + process_ref[...])
        m_top = mean[:, :points]
        m_bottom = mean[:, points:]
        mean_fwd = jnp.concatenate(
            [a_row * m_top + b_row * m_bottom, c_row * m_top + d_row * m_bottom], axis=1
        )
        mean_pred = jnp.where(first, 0.0, mean_fwd)
        r_col = root_col_ref[t]
        r_row = root_row_ref[pl.ds(t, 1), :]
        obs_row = obs_ref[pl.ds(t, 1), :]
        normal_ref[...] = eye + r_col * cov_pred[:points, :points] * r_row
        _sweep_in_place(normal_ref)
        scaled = r_col * cov_pred[:points, :]
        solved = jnp.dot(normal_ref[...], scaled, precision=HIGHEST, preferred_element_type=jnp.float32)
        correction = lax.dot_general(
            scaled, solved, (((0,), (0,)), ((), ())), precision=HIGHEST,
            preferred_element_type=jnp.float32,
        )
        cov_ref[...] = cov_pred + correction
        innovation = jnp.broadcast_to(r_row * (obs_row - mean_pred[:, :points]), (8, points))
        mean_shift = jnp.dot(innovation, solved, precision=HIGHEST, preferred_element_type=jnp.float32)
        return mean_pred - mean_shift[0:1, :]

    mean_ref[...] = lax.fori_loop(0, count_ref[0], step, jnp.zeros((1, 2 * points), jnp.float32))


def run_filter(count, obs_all, root_all, transit, process, prior):
    total, points = obs_all.shape
    width = 2 * points
    vmem = pl.BlockSpec(memory_space=pltpu.VMEM)
    return pl.pallas_call(
        _filter_kernel,
        out_shape=(
            jax.ShapeDtypeStruct((1, width), jnp.float32),
            jax.ShapeDtypeStruct((width, width), jnp.float32),
        ),
        in_specs=[pl.BlockSpec(memory_space=pltpu.SMEM)] + [vmem] * 7,
        out_specs=(vmem, vmem),
        scratch_shapes=[
            pltpu.VMEM((width, width), jnp.float32),
            pltpu.VMEM((points, points), jnp.float32),
        ],
    )(
        jnp.reshape(count, (1,)).astype(jnp.int32),
        obs_all,
        root_all,
        root_all[:, :, None],
        transit,
        transit[:, :, None],
        process,
        prior,
    )


def matmul_hi(left, right):
    return jnp.matmul(left, right, precision=HIGHEST)


def swap_last(matrix):
    return jnp.swapaxes(matrix, -1, -2)


def apply_trans(transit, matrix):
    points = transit.shape[1]
    upper_half = matrix[..., :points, :]
    lower_half = matrix[..., points:, :]
    return jnp.concatenate(
        [
            transit[0][:, None] * upper_half + transit[1][:, None] * lower_half,
            transit[2][:, None] * upper_half + transit[3][:, None] * lower_half,
        ],
        axis=-2,
    )


def build_model(decay_rates, spatial_cov):
    decay_one = jnp.exp(-decay_rates)
    transit = jnp.stack(
        [
            decay_one * (1.0 + decay_rates),
            decay_one * decay_rates,
            -decay_one * decay_rates,
            decay_one * (1.0 - decay_rates),
        ]
    )
    decay_two = jnp.exp(-2.0 * decay_rates)
    var_ff = 1.0 - decay_two * (1.0 + 2.0 * decay_rates + 2.0 * decay_rates * decay_rates)
    cov_fg = 2.0 * decay_rates * decay_rates * decay_two
    var_gg = 1.0 - decay_two * (1.0 - 2.0 * decay_rates + 2.0 * decay_rates * decay_rates)
    fac_ff = jnp.sqrt(var_ff)
    fac_gf = cov_fg / fac_ff
    fac_gg = jnp.sqrt(var_gg - fac_gf * fac_gf)

    def scaled(left, right):
        return left[:, None] * spatial_cov * right[None, :]

    zero_block = jnp.zeros_like(spatial_cov)
    process = jnp.block(
        [
            [scaled(fac_ff, fac_ff), scaled(fac_ff, fac_gf)],
            [scaled(fac_gf, fac_ff), scaled(fac_gf, fac_gf) + scaled(fac_gg, fac_gg)],
        ]
    )
    process = process + JITTER * jnp.eye(2 * spatial_cov.shape[0], dtype=jnp.float32)
    prior = jnp.block([[spatial_cov, zero_block], [zero_block, spatial_cov]])
    return (transit, process, prior)


def predict(transit, process, mean, cov):
    forward_cov = apply_trans(transit, cov)
    cov_pred = apply_trans(transit, swap_last(forward_cov)) + process
    mean_pred = apply_trans(transit, mean[:, None])[:, 0]
    return mean_pred, cov_pred


def kalman_update(mean_pred, cov_pred, obs, root):
    points = obs.shape[-1]
    normal = jnp.eye(points, dtype=jnp.float32) + root[:, None] * cov_pred[:points, :points] * root[None, :]
    neg_inv = neg_inverse(normal)
    innovation = root * (obs - mean_pred[:points])
    scaled = root[:, None] * cov_pred[:points, :]
    rhs = jnp.concatenate([scaled, innovation[:, None]], axis=1)
    solved = matmul_hi(neg_inv, rhs)
    correction = matmul_hi(swap_last(scaled), solved)
    cov_new = cov_pred + correction[:, :-1]
    mean_new = mean_pred - correction[:, -1]
    return mean_new, cov_new


def smoother_elements(means, covs, last_flag, transit, process):
    forward_cov = apply_trans(transit, covs)
    predicted = apply_trans(transit, swap_last(forward_cov)) + process
    neg_inv = jax.vmap(neg_inverse)(predicted)
    gains = -matmul_hi(swap_last(forward_cov), neg_inv)
    gains = gains * (1.0 - last_flag.astype(jnp.float32))[:, None, None]
    forward_mean = apply_trans(transit, means[..., None])
    shift_means = means - matmul_hi(gains, forward_mean)[..., 0]
    shift_covs = covs - matmul_hi(gains, forward_cov)
    return (gains, shift_means, shift_covs)


def smooth_join(lower_el, higher_el):
    gain_a, mean_a, cov_a = lower_el
    gain_b, mean_b, cov_b = higher_el
    return (
        matmul_hi(gain_a, gain_b),
        matmul_hi(gain_a, mean_b[..., None])[..., 0] + mean_a,
        matmul_hi(matmul_hi(gain_a, cov_b), swap_last(gain_a)) + cov_a,
    )


def send_element(element, pairs):
    gain, mean, cov = element
    width = mean.shape[-1]
    packed = jnp.concatenate([cov, jnp.broadcast_to(mean[None], (8, width))], axis=0)
    recv_gain, recv_packed = lax.ppermute((gain, packed), "tm", pairs)
    return (recv_gain, recv_packed[width], recv_packed[:width])


def shards(observed, obs_masks, decay_rates, noise_var, spatial_cov):
    transit, process, prior = build_model(decay_rates, spatial_cov)
    local_steps, points = observed.shape
    width = 2 * points
    position = lax.axis_index("tm")
    tm_count = lax.axis_size("tm")
    total_steps = tm_count * local_steps

    root_local = jnp.sqrt(obs_masks.astype(jnp.float32) / noise_var)
    packed = jnp.stack([observed, root_local], axis=1)
    placed = lax.dynamic_update_slice_in_dim(
        jnp.zeros((total_steps,) + packed.shape[1:], jnp.float32), packed, position * local_steps, 0
    )
    gathered = lax.psum(placed, "tm")
    obs_all = gathered[:, 0]
    root_all = gathered[:, 1]

    last_local = position * local_steps + (local_steps - 1)

    def filter_step(step, mean, cov):
        mean_pred, cov_pred = predict(transit, process, mean, cov)
        obs_now = lax.dynamic_index_in_dim(obs_all, step, keepdims=False)
        root_now = lax.dynamic_index_in_dim(root_all, step, keepdims=False)
        return kalman_update(mean_pred, cov_pred, obs_now, root_now)

    if local_steps == 1:
        mean_last, cov_last = run_filter(position + 1, obs_all, root_all, transit, process, prior)
        means = mean_last
        covs = cov_last[None]
    else:
        mean_first, cov_first = kalman_update(
            jnp.zeros((width,), jnp.float32), prior, obs_all[0], root_all[0]
        )
        mean_buf = jnp.zeros((local_steps, width), jnp.float32).at[0].set(mean_first)
        cov_buf = jnp.zeros((local_steps, width, width), jnp.float32).at[0].set(cov_first)

        def body(step, carry):
            mean, cov, mean_buf, cov_buf = carry
            mean, cov = filter_step(step, mean, cov)
            slot = step % local_steps
            mean_buf = lax.dynamic_update_index_in_dim(mean_buf, mean, slot, 0)
            cov_buf = lax.dynamic_update_index_in_dim(cov_buf, cov, slot, 0)
            return (mean, cov, mean_buf, cov_buf)

        _, _, means, covs = lax.fori_loop(
            1, last_local + 1, body, (mean_first, cov_first, mean_buf, cov_buf)
        )

    global_step = position * local_steps + jnp.arange(local_steps)
    last_flag = global_step == total_steps - 1
    if local_steps == 1:

        def compute_elements(operand):
            return smoother_elements(operand[0], operand[1], last_flag, transit, process)

        def final_elements(operand):
            return (jnp.zeros_like(operand[1]), operand[0], operand[1])

        smooth = lax.cond(position == tm_count - 1, final_elements, compute_elements, (means, covs))
    else:
        smooth = smoother_elements(means, covs, last_flag, transit, process)

    if local_steps > 1:
        last_el = jax.tree.map(lambda leaf: leaf[-1], smooth)
        front_els = jax.tree.map(lambda leaf: leaf[:-1], smooth)

        def backward(running, element):
            joined = smooth_join(element, running)
            return (joined, joined)

        _, head_els = lax.scan(backward, last_el, front_els, reverse=True)
        suffixes = jax.tree.map(
            lambda head_leaf, last_leaf: jnp.concatenate([head_leaf, last_leaf[None]], axis=0),
            head_els,
            last_el,
        )
        block_total = jax.tree.map(lambda leaf: leaf[0], suffixes)
    else:
        block_total = jax.tree.map(lambda leaf: leaf[0], smooth)

    running = block_total
    shift = 1
    while shift < tm_count:
        pairs = [(source, source - shift) for source in range(shift, tm_count)]
        received = send_element(running, pairs)
        running = smooth_join(running, received)
        shift *= 2

    if local_steps == 1:
        return (running[1][None], running[2][None])
    pairs = [(source, source - 1) for source in range(1, tm_count)]
    after_mine = lax.ppermute(running, "tm", pairs)
    gains, shift_means, shift_covs = suffixes
    smooth_mean = matmul_hi(gains, after_mine[1][:, None])[..., 0] + shift_means
    smooth_cov = matmul_hi(matmul_hi(gains, after_mine[2]), swap_last(gains)) + shift_covs
    return (smooth_mean, smooth_cov)


def solution(mesh):
    placed = (
        P(("groups", "tm"), None),
        P(("groups", "tm"), None),
        P("groups"),
        P("groups"),
        P("groups", None),
    )
    return jax.shard_map(
        shards,
        mesh=mesh,
        in_specs=placed,
        out_specs=(P(("groups", "tm"), None), P(("groups", "tm"), None, None)),
        check_vma=False,
    )
```

```python
import jax
import jax.numpy as jnp
from jax import lax
from jax.experimental import pallas as pl
from jax.experimental.pallas import tpu as pltpu
from jax.sharding import PartitionSpec as P

HIGHEST = lax.Precision.HIGHEST
JITTER = 0.001
PANEL = 32


def _inv2(a, b, d):
    idet = 1.0 / (a * d - b * b)
    return d * idet, -b * idet, a * idet

def _inv4(m):
    a00, a01, a11 = _inv2(m[0][0], m[0][1], m[1][1])
    b = ((m[0][2], m[0][3]), (m[1][2], m[1][3]))
    x = [[a00 * b[0][j] + a01 * b[1][j] for j in range(2)], [a01 * b[0][j] + a11 * b[1][j] for j in range(2)]]
    s00 = m[2][2] - (b[0][0] * x[0][0] + b[1][0] * x[1][0])
    s01 = m[2][3] - (b[0][0] * x[0][1] + b[1][0] * x[1][1])
    s11 = m[3][3] - (b[0][1] * x[0][1] + b[1][1] * x[1][1])
    c00, c01, c11 = _inv2(s00, s01, s11)
    cm = ((c00, c01), (c01, c11))
    y = [[x[i][0] * cm[0][j] + x[i][1] * cm[1][j] for j in range(2)] for i in range(2)]
    am = ((a00, a01), (a01, a11))
    out = [[None] * 4 for _ in range(4)]
    for i in range(2):
        for j in range(2):
            out[i][j] = am[i][j] + y[i][0] * x[j][0] + y[i][1] * x[j][1]
            out[i][2 + j] = -y[i][j]
            out[2 + j][i] = -y[i][j]
            out[2 + i][2 + j] = cm[i][j]
    return out

def _sweep_kernel(a_ref, o_ref):
    o_ref[...] = a_ref[...]
    _sweep_in_place(o_ref)

def _sweep_in_place(o_ref):
    n = o_ref.shape[0]
    PANEL = 64 if n >= 256 else 32
    sub = lax.broadcasted_iota(jnp.int32, (PANEL, n), 0)
    lane = lax.broadcasted_iota(jnp.int32, (PANEL, n), 1)
    sub_col = lax.broadcasted_iota(jnp.int32, (PANEL, 1), 0)
    lane_full = lax.broadcasted_iota(jnp.int32, (n, n), 1)
    for blk in range(n // PANEL):
        base = blk * PANEL
        orig = o_ref[base:base + PANEL, :]
        panel = orig
        for t in range(0, PANEL, 4):
            rows = [sub == t + i for i in range(4)]
            cols = [lane == base + t + i for i in range(4)]
            cv = [jnp.sum(jnp.where(cols[i], panel, 0.0), axis=1, keepdims=True) for i in range(4)]
            rv = [jnp.sum(jnp.where(rows[i], panel, 0.0), axis=0, keepdims=True) for i in range(4)]
            m = [[None] * 4 for _ in range(4)]
            for i in range(4):
                for j in range(i, 4):
                    m[i][j] = jnp.sum(jnp.where(sub_col == t + i, cv[j], 0.0), axis=0, keepdims=True)
                    m[j][i] = m[i][j]
            mi = _inv4(m)
            nr = [mi[i][0] * rv[0] + mi[i][1] * rv[1] + mi[i][2] * rv[2] + mi[i][3] * rv[3] for i in range(4)]
            nc = [cv[0] * mi[0][j] + cv[1] * mi[1][j] + cv[2] * mi[2][j] + cv[3] * mi[3][j] for j in range(4)]
            rest = panel - cv[0] * nr[0] - cv[1] * nr[1] - cv[2] * nr[2] - cv[3] * nr[3]
            for j in range(4):
                rest = jnp.where(cols[j], nc[j], rest)
            for i in range(4):
                row_val = nr[i]
                for j in range(4):
                    row_val = jnp.where(cols[j], -mi[i][j], row_val)
                rest = jnp.where(rows[i], row_val, rest)
            panel = rest
        full = o_ref[...]
        update = lax.dot_general(orig, panel, (((0,), (0,)), ((), ())), precision=HIGHEST,
                                 preferred_element_type=jnp.float32)
        in_blk = (lane_full >= base) & (lane_full < base + PANEL)
        o_ref[...] = jnp.where(in_blk, 0.0, full) - update
        o_ref[base:base + PANEL, :] = panel

def neg_inverse(matrix):
    size = matrix.shape[-1]
    return pl.pallas_call(
        _sweep_kernel,
        out_shape=jax.ShapeDtypeStruct((size, size), jnp.float32),
        in_specs=[pl.BlockSpec(memory_space=pltpu.VMEM)],
        out_specs=pl.BlockSpec(memory_space=pltpu.VMEM),
    )(matrix)


def _filter_kernel(
    count_ref, obs_ref, root_row_ref, root_col_ref, trans_row_ref, trans_col_ref, process_ref,
    prior_ref, mean_ref, cov_ref, pred_ref, normal_ref,
):
    points = obs_ref.shape[1]
    eye = (
        lax.broadcasted_iota(jnp.int32, (points, points), 0)
        == lax.broadcasted_iota(jnp.int32, (points, points), 1)
    ).astype(jnp.float32)
    cov_ref[...] = prior_ref[...]
    a_col, b_col, c_col, d_col = (trans_col_ref[i] for i in range(4))
    a_row, b_row, c_row, d_row = (trans_row_ref[i:i + 1, :] for i in range(4))

    def step(t, mean):
        first = t == 0
        top = cov_ref[:points, :]
        bottom = cov_ref[points:, :]
        for rows, left_w, right_w in ((slice(0, points), a_col, b_col), (slice(points, None), c_col, d_col)):
            forward = left_w * top + right_w * bottom
            f_left = forward[:, :points]
            f_right = forward[:, points:]
            pred_ref[rows, :points] = f_left * a_row + f_right * b_row
            pred_ref[rows, points:] = f_left * c_row + f_right * d_row
        cov_pred = jnp.where(first, prior_ref[...], pred_ref[...] + process_ref[...])
        m_top = mean[:, :points]
        m_bottom = mean[:, points:]
        mean_fwd = jnp.concatenate(
            [a_row * m_top + b_row * m_bottom, c_row * m_top + d_row * m_bottom], axis=1
        )
        mean_pred = jnp.where(first, 0.0, mean_fwd)
        r_col = root_col_ref[t]
        r_row = root_row_ref[pl.ds(t, 1), :]
        obs_row = obs_ref[pl.ds(t, 1), :]
        normal_ref[...] = eye + r_col * cov_pred[:points, :points] * r_row
        _sweep_in_place(normal_ref)
        scaled = r_col * cov_pred[:points, :]
        solved = jnp.dot(normal_ref[...], scaled, precision=HIGHEST, preferred_element_type=jnp.float32)
        correction = lax.dot_general(
            scaled, solved, (((0,), (0,)), ((), ())), precision=HIGHEST,
            preferred_element_type=jnp.float32,
        )
        cov_ref[...] = cov_pred + correction
        innovation = jnp.broadcast_to(r_row * (obs_row - mean_pred[:, :points]), (8, points))
        mean_shift = jnp.dot(innovation, solved, precision=HIGHEST, preferred_element_type=jnp.float32)
        return mean_pred - mean_shift[0:1, :]

    mean_ref[...] = lax.fori_loop(0, count_ref[0], step, jnp.zeros((1, 2 * points), jnp.float32))


def run_filter(count, obs_all, root_all, transit, process, prior):
    total, points = obs_all.shape
    width = 2 * points
    vmem = pl.BlockSpec(memory_space=pltpu.VMEM)
    return pl.pallas_call(
        _filter_kernel,
        out_shape=(
            jax.ShapeDtypeStruct((1, width), jnp.float32),
            jax.ShapeDtypeStruct((width, width), jnp.float32),
        ),
        in_specs=[pl.BlockSpec(memory_space=pltpu.SMEM)] + [vmem] * 7,
        out_specs=(vmem, vmem),
        scratch_shapes=[
            pltpu.VMEM((width, width), jnp.float32),
            pltpu.VMEM((points, points), jnp.float32),
        ],
    )(
        jnp.reshape(count, (1,)).astype(jnp.int32),
        obs_all,
        root_all,
        root_all[:, :, None],
        transit,
        transit[:, :, None],
        process,
        prior,
    )


def matmul_hi(left, right):
    return jnp.matmul(left, right, precision=HIGHEST)


def swap_last(matrix):
    return jnp.swapaxes(matrix, -1, -2)


def apply_trans(transit, matrix):
    points = transit.shape[1]
    upper_half = matrix[..., :points, :]
    lower_half = matrix[..., points:, :]
    return jnp.concatenate(
        [
            transit[0][:, None] * upper_half + transit[1][:, None] * lower_half,
            transit[2][:, None] * upper_half + transit[3][:, None] * lower_half,
        ],
        axis=-2,
    )


def build_model(decay_rates, spatial_cov):
    decay_one = jnp.exp(-decay_rates)
    transit = jnp.stack(
        [
            decay_one * (1.0 + decay_rates),
            decay_one * decay_rates,
            -decay_one * decay_rates,
            decay_one * (1.0 - decay_rates),
        ]
    )
    decay_two = jnp.exp(-2.0 * decay_rates)
    var_ff = 1.0 - decay_two * (1.0 + 2.0 * decay_rates + 2.0 * decay_rates * decay_rates)
    cov_fg = 2.0 * decay_rates * decay_rates * decay_two
    var_gg = 1.0 - decay_two * (1.0 - 2.0 * decay_rates + 2.0 * decay_rates * decay_rates)
    fac_ff = jnp.sqrt(var_ff)
    fac_gf = cov_fg / fac_ff
    fac_gg = jnp.sqrt(var_gg - fac_gf * fac_gf)

    def scaled(left, right):
        return left[:, None] * spatial_cov * right[None, :]

    zero_block = jnp.zeros_like(spatial_cov)
    process = jnp.block(
        [
            [scaled(fac_ff, fac_ff), scaled(fac_ff, fac_gf)],
            [scaled(fac_gf, fac_ff), scaled(fac_gf, fac_gf) + scaled(fac_gg, fac_gg)],
        ]
    )
    process = process + JITTER * jnp.eye(2 * spatial_cov.shape[0], dtype=jnp.float32)
    prior = jnp.block([[spatial_cov, zero_block], [zero_block, spatial_cov]])
    return (transit, process, prior)


def predict(transit, process, mean, cov):
    forward_cov = apply_trans(transit, cov)
    cov_pred = apply_trans(transit, swap_last(forward_cov)) + process
    mean_pred = apply_trans(transit, mean[:, None])[:, 0]
    return mean_pred, cov_pred


def kalman_update(mean_pred, cov_pred, obs, root):
    points = obs.shape[-1]
    normal = jnp.eye(points, dtype=jnp.float32) + root[:, None] * cov_pred[:points, :points] * root[None, :]
    neg_inv = neg_inverse(normal)
    innovation = root * (obs - mean_pred[:points])
    scaled = root[:, None] * cov_pred[:points, :]
    rhs = jnp.concatenate([scaled, innovation[:, None]], axis=1)
    solved = matmul_hi(neg_inv, rhs)
    correction = matmul_hi(swap_last(scaled), solved)
    cov_new = cov_pred + correction[:, :-1]
    mean_new = mean_pred - correction[:, -1]
    return mean_new, cov_new


def smoother_elements(means, covs, last_flag, transit, process):
    forward_cov = apply_trans(transit, covs)
    predicted = apply_trans(transit, swap_last(forward_cov)) + process
    neg_inv = jax.vmap(neg_inverse)(predicted)
    gains = -matmul_hi(swap_last(forward_cov), neg_inv)
    gains = gains * (1.0 - last_flag.astype(jnp.float32))[:, None, None]
    forward_mean = apply_trans(transit, means[..., None])
    shift_means = means - matmul_hi(gains, forward_mean)[..., 0]
    shift_covs = covs - matmul_hi(gains, forward_cov)
    return (gains, shift_means, shift_covs)


def smooth_join(lower_el, higher_el):
    gain_a, mean_a, cov_a = lower_el
    gain_b, mean_b, cov_b = higher_el
    return (
        matmul_hi(gain_a, gain_b),
        matmul_hi(gain_a, mean_b[..., None])[..., 0] + mean_a,
        matmul_hi(matmul_hi(gain_a, cov_b), swap_last(gain_a)) + cov_a,
    )


def send_element(element, pairs):
    gain, mean, cov = element
    width = mean.shape[-1]
    packed = jnp.concatenate([cov, jnp.broadcast_to(mean[None], (8, width))], axis=0)
    recv_gain, recv_packed = lax.ppermute((gain, packed), "tm", pairs)
    return (recv_gain, recv_packed[width], recv_packed[:width])


def shards(observed, obs_masks, decay_rates, noise_var, spatial_cov):
    transit, process, prior = build_model(decay_rates, spatial_cov)
    local_steps, points = observed.shape
    width = 2 * points
    position = lax.axis_index("tm")
    tm_count = lax.axis_size("tm")
    total_steps = tm_count * local_steps

    root_local = jnp.sqrt(obs_masks.astype(jnp.float32) / noise_var)
    packed = jnp.stack([observed, root_local], axis=1)
    gathered = lax.dynamic_update_slice_in_dim(
        jnp.zeros((total_steps,) + packed.shape[1:], jnp.float32), packed, position * local_steps, 0
    )
    shift = 1
    while shift < tm_count:
        pairs = [(source, source + shift) for source in range(tm_count - shift)]
        gathered = gathered + lax.ppermute(gathered, "tm", pairs)
        shift *= 2
    obs_all = gathered[:, 0]
    root_all = gathered[:, 1]

    last_local = position * local_steps + (local_steps - 1)

    def filter_step(step, mean, cov):
        mean_pred, cov_pred = predict(transit, process, mean, cov)
        obs_now = lax.dynamic_index_in_dim(obs_all, step, keepdims=False)
        root_now = lax.dynamic_index_in_dim(root_all, step, keepdims=False)
        return kalman_update(mean_pred, cov_pred, obs_now, root_now)

    if local_steps == 1:
        mean_last, cov_last = run_filter(position + 1, obs_all, root_all, transit, process, prior)
        means = mean_last
        covs = cov_last[None]
    else:
        mean_first, cov_first = kalman_update(
            jnp.zeros((width,), jnp.float32), prior, obs_all[0], root_all[0]
        )
        mean_buf = jnp.zeros((local_steps, width), jnp.float32).at[0].set(mean_first)
        cov_buf = jnp.zeros((local_steps, width, width), jnp.float32).at[0].set(cov_first)

        def body(step, carry):
            mean, cov, mean_buf, cov_buf = carry
            mean, cov = filter_step(step, mean, cov)
            slot = step % local_steps
            mean_buf = lax.dynamic_update_index_in_dim(mean_buf, mean, slot, 0)
            cov_buf = lax.dynamic_update_index_in_dim(cov_buf, cov, slot, 0)
            return (mean, cov, mean_buf, cov_buf)

        _, _, means, covs = lax.fori_loop(
            1, last_local + 1, body, (mean_first, cov_first, mean_buf, cov_buf)
        )

    global_step = position * local_steps + jnp.arange(local_steps)
    last_flag = global_step == total_steps - 1
    if local_steps == 1:

        def compute_elements(operand):
            return smoother_elements(operand[0], operand[1], last_flag, transit, process)

        def final_elements(operand):
            return (jnp.zeros_like(operand[1]), operand[0], operand[1])

        smooth = lax.cond(position == tm_count - 1, final_elements, compute_elements, (means, covs))
    else:
        smooth = smoother_elements(means, covs, last_flag, transit, process)

    if local_steps > 1:
        last_el = jax.tree.map(lambda leaf: leaf[-1], smooth)
        front_els = jax.tree.map(lambda leaf: leaf[:-1], smooth)

        def backward(running, element):
            joined = smooth_join(element, running)
            return (joined, joined)

        _, head_els = lax.scan(backward, last_el, front_els, reverse=True)
        suffixes = jax.tree.map(
            lambda head_leaf, last_leaf: jnp.concatenate([head_leaf, last_leaf[None]], axis=0),
            head_els,
            last_el,
        )
        block_total = jax.tree.map(lambda leaf: leaf[0], suffixes)
    else:
        block_total = jax.tree.map(lambda leaf: leaf[0], smooth)

    running = block_total
    shift = 1
    while shift < tm_count:
        pairs = [(source, source - shift) for source in range(shift, tm_count)]
        received = send_element(running, pairs)
        running = smooth_join(running, received)
        shift *= 2

    if local_steps == 1:
        return (running[1][None], running[2][None])
    pairs = [(source, source - 1) for source in range(1, tm_count)]
    after_mine = lax.ppermute(running, "tm", pairs)
    gains, shift_means, shift_covs = suffixes
    smooth_mean = matmul_hi(gains, after_mine[1][:, None])[..., 0] + shift_means
    smooth_cov = matmul_hi(matmul_hi(gains, after_mine[2]), swap_last(gains)) + shift_covs
    return (smooth_mean, smooth_cov)


def solution(mesh):
    placed = (
        P(("groups", "tm"), None),
        P(("groups", "tm"), None),
        P("groups"),
        P("groups"),
        P("groups", None),
    )
    return jax.shard_map(
        shards,
        mesh=mesh,
        in_specs=placed,
        out_specs=(P(("groups", "tm"), None), P(("groups", "tm"), None, None)),
        check_vma=False,
    )
```

```python
import jax
import jax.numpy as jnp
from jax import lax
from jax.experimental import pallas as pl
from jax.experimental.pallas import tpu as pltpu
from jax.sharding import PartitionSpec as P

HIGHEST = lax.Precision.HIGHEST
JITTER = 0.001
PANEL = 32


def _inv2(a, b, d):
    idet = 1.0 / (a * d - b * b)
    return d * idet, -b * idet, a * idet

def _inv4(m):
    a00, a01, a11 = _inv2(m[0][0], m[0][1], m[1][1])
    b = ((m[0][2], m[0][3]), (m[1][2], m[1][3]))
    x = [[a00 * b[0][j] + a01 * b[1][j] for j in range(2)], [a01 * b[0][j] + a11 * b[1][j] for j in range(2)]]
    s00 = m[2][2] - (b[0][0] * x[0][0] + b[1][0] * x[1][0])
    s01 = m[2][3] - (b[0][0] * x[0][1] + b[1][0] * x[1][1])
    s11 = m[3][3] - (b[0][1] * x[0][1] + b[1][1] * x[1][1])
    c00, c01, c11 = _inv2(s00, s01, s11)
    cm = ((c00, c01), (c01, c11))
    y = [[x[i][0] * cm[0][j] + x[i][1] * cm[1][j] for j in range(2)] for i in range(2)]
    am = ((a00, a01), (a01, a11))
    out = [[None] * 4 for _ in range(4)]
    for i in range(2):
        for j in range(2):
            out[i][j] = am[i][j] + y[i][0] * x[j][0] + y[i][1] * x[j][1]
            out[i][2 + j] = -y[i][j]
            out[2 + j][i] = -y[i][j]
            out[2 + i][2 + j] = cm[i][j]
    return out

def _sweep_kernel(a_ref, o_ref):
    o_ref[...] = a_ref[...]
    _sweep_in_place(o_ref)

def _sweep_in_place(o_ref):
    n = o_ref.shape[0]
    PANEL = 64 if n >= 256 else 32
    sub = lax.broadcasted_iota(jnp.int32, (PANEL, n), 0)
    lane = lax.broadcasted_iota(jnp.int32, (PANEL, n), 1)
    sub_col = lax.broadcasted_iota(jnp.int32, (PANEL, 1), 0)
    lane_full = lax.broadcasted_iota(jnp.int32, (n, n), 1)
    for blk in range(n // PANEL):
        base = blk * PANEL
        orig = o_ref[base:base + PANEL, :]
        panel = orig
        for t in range(0, PANEL, 4):
            rows = [sub == t + i for i in range(4)]
            cols = [lane == base + t + i for i in range(4)]
            cv = [jnp.sum(jnp.where(cols[i], panel, 0.0), axis=1, keepdims=True) for i in range(4)]
            rv = [jnp.sum(jnp.where(rows[i], panel, 0.0), axis=0, keepdims=True) for i in range(4)]
            m = [[None] * 4 for _ in range(4)]
            for i in range(4):
                for j in range(i, 4):
                    m[i][j] = jnp.sum(jnp.where(sub_col == t + i, cv[j], 0.0), axis=0, keepdims=True)
                    m[j][i] = m[i][j]
            mi = _inv4(m)
            nr = [mi[i][0] * rv[0] + mi[i][1] * rv[1] + mi[i][2] * rv[2] + mi[i][3] * rv[3] for i in range(4)]
            nc = [cv[0] * mi[0][j] + cv[1] * mi[1][j] + cv[2] * mi[2][j] + cv[3] * mi[3][j] for j in range(4)]
            rest = panel - cv[0] * nr[0] - cv[1] * nr[1] - cv[2] * nr[2] - cv[3] * nr[3]
            for j in range(4):
                rest = jnp.where(cols[j], nc[j], rest)
            for i in range(4):
                row_val = nr[i]
                for j in range(4):
                    row_val = jnp.where(cols[j], -mi[i][j], row_val)
                rest = jnp.where(rows[i], row_val, rest)
            panel = rest
        full = o_ref[...]
        update = lax.dot_general(orig, panel, (((0,), (0,)), ((), ())), precision=HIGHEST,
                                 preferred_element_type=jnp.float32)
        in_blk = (lane_full >= base) & (lane_full < base + PANEL)
        o_ref[...] = jnp.where(in_blk, 0.0, full) - update
        o_ref[base:base + PANEL, :] = panel

def neg_inverse(matrix):
    size = matrix.shape[-1]
    return pl.pallas_call(
        _sweep_kernel,
        out_shape=jax.ShapeDtypeStruct((size, size), jnp.float32),
        in_specs=[pl.BlockSpec(memory_space=pltpu.VMEM)],
        out_specs=pl.BlockSpec(memory_space=pltpu.VMEM),
    )(matrix)


def _filter_kernel(
    count_ref, obs_ref, root_row_ref, root_col_ref, trans_row_ref, trans_col_ref, process_ref,
    prior_ref, mean_ref, cov_ref, pred_ref, normal_ref,
):
    points = obs_ref.shape[1]
    eye = (
        lax.broadcasted_iota(jnp.int32, (points, points), 0)
        == lax.broadcasted_iota(jnp.int32, (points, points), 1)
    ).astype(jnp.float32)
    cov_ref[...] = prior_ref[...]
    a_col, b_col, c_col, d_col = (trans_col_ref[i] for i in range(4))
    a_row, b_row, c_row, d_row = (trans_row_ref[i:i + 1, :] for i in range(4))

    def step(t, mean):
        first = t == 0
        top = cov_ref[:points, :]
        bottom = cov_ref[points:, :]
        r_col = root_col_ref[t]
        r_row = root_row_ref[pl.ds(t, 1), :]
        forward_top = a_col * top + b_col * bottom
        pred_vv = forward_top[:, :points] * a_row + forward_top[:, points:] * b_row
        pred_vv = jnp.where(first, prior_ref[:points, :points], pred_vv + process_ref[:points, :points])
        normal_ref[...] = eye + r_col * pred_vv * r_row
        _sweep_in_place(normal_ref)
        for rows, left_w, right_w in ((slice(0, points), a_col, b_col), (slice(points, None), c_col, d_col)):
            forward = left_w * top + right_w * bottom
            f_left = forward[:, :points]
            f_right = forward[:, points:]
            pred_ref[rows, :points] = f_left * a_row + f_right * b_row
            pred_ref[rows, points:] = f_left * c_row + f_right * d_row
        cov_pred = jnp.where(first, prior_ref[...], pred_ref[...] + process_ref[...])
        m_top = mean[:, :points]
        m_bottom = mean[:, points:]
        mean_fwd = jnp.concatenate(
            [a_row * m_top + b_row * m_bottom, c_row * m_top + d_row * m_bottom], axis=1
        )
        mean_pred = jnp.where(first, 0.0, mean_fwd)
        obs_row = obs_ref[pl.ds(t, 1), :]
        scaled = r_col * cov_pred[:points, :]
        solved = jnp.dot(normal_ref[...], scaled, precision=HIGHEST, preferred_element_type=jnp.float32)
        correction = lax.dot_general(
            scaled, solved, (((0,), (0,)), ((), ())), precision=HIGHEST,
            preferred_element_type=jnp.float32,
        )
        cov_ref[...] = cov_pred + correction
        innovation = jnp.broadcast_to(r_row * (obs_row - mean_pred[:, :points]), (8, points))
        mean_shift = jnp.dot(innovation, solved, precision=HIGHEST, preferred_element_type=jnp.float32)
        return mean_pred - mean_shift[0:1, :]

    mean_ref[...] = lax.fori_loop(0, count_ref[0], step, jnp.zeros((1, 2 * points), jnp.float32))


def run_filter(count, obs_all, root_all, transit, process, prior):
    total, points = obs_all.shape
    width = 2 * points
    vmem = pl.BlockSpec(memory_space=pltpu.VMEM)
    return pl.pallas_call(
        _filter_kernel,
        out_shape=(
            jax.ShapeDtypeStruct((1, width), jnp.float32),
            jax.ShapeDtypeStruct((width, width), jnp.float32),
        ),
        in_specs=[pl.BlockSpec(memory_space=pltpu.SMEM)] + [vmem] * 7,
        out_specs=(vmem, vmem),
        scratch_shapes=[
            pltpu.VMEM((width, width), jnp.float32),
            pltpu.VMEM((points, points), jnp.float32),
        ],
    )(
        jnp.reshape(count, (1,)).astype(jnp.int32),
        obs_all,
        root_all,
        root_all[:, :, None],
        transit,
        transit[:, :, None],
        process,
        prior,
    )


def matmul_hi(left, right):
    return jnp.matmul(left, right, precision=HIGHEST)


def swap_last(matrix):
    return jnp.swapaxes(matrix, -1, -2)


def apply_trans(transit, matrix):
    points = transit.shape[1]
    upper_half = matrix[..., :points, :]
    lower_half = matrix[..., points:, :]
    return jnp.concatenate(
        [
            transit[0][:, None] * upper_half + transit[1][:, None] * lower_half,
            transit[2][:, None] * upper_half + transit[3][:, None] * lower_half,
        ],
        axis=-2,
    )


def build_model(decay_rates, spatial_cov):
    decay_one = jnp.exp(-decay_rates)
    transit = jnp.stack(
        [
            decay_one * (1.0 + decay_rates),
            decay_one * decay_rates,
            -decay_one * decay_rates,
            decay_one * (1.0 - decay_rates),
        ]
    )
    decay_two = jnp.exp(-2.0 * decay_rates)
    var_ff = 1.0 - decay_two * (1.0 + 2.0 * decay_rates + 2.0 * decay_rates * decay_rates)
    cov_fg = 2.0 * decay_rates * decay_rates * decay_two
    var_gg = 1.0 - decay_two * (1.0 - 2.0 * decay_rates + 2.0 * decay_rates * decay_rates)
    fac_ff = jnp.sqrt(var_ff)
    fac_gf = cov_fg / fac_ff
    fac_gg = jnp.sqrt(var_gg - fac_gf * fac_gf)

    def scaled(left, right):
        return left[:, None] * spatial_cov * right[None, :]

    zero_block = jnp.zeros_like(spatial_cov)
    process = jnp.block(
        [
            [scaled(fac_ff, fac_ff), scaled(fac_ff, fac_gf)],
            [scaled(fac_gf, fac_ff), scaled(fac_gf, fac_gf) + scaled(fac_gg, fac_gg)],
        ]
    )
    process = process + JITTER * jnp.eye(2 * spatial_cov.shape[0], dtype=jnp.float32)
    prior = jnp.block([[spatial_cov, zero_block], [zero_block, spatial_cov]])
    return (transit, process, prior)


def predict(transit, process, mean, cov):
    forward_cov = apply_trans(transit, cov)
    cov_pred = apply_trans(transit, swap_last(forward_cov)) + process
    mean_pred = apply_trans(transit, mean[:, None])[:, 0]
    return mean_pred, cov_pred


def kalman_update(mean_pred, cov_pred, obs, root):
    points = obs.shape[-1]
    normal = jnp.eye(points, dtype=jnp.float32) + root[:, None] * cov_pred[:points, :points] * root[None, :]
    neg_inv = neg_inverse(normal)
    innovation = root * (obs - mean_pred[:points])
    scaled = root[:, None] * cov_pred[:points, :]
    rhs = jnp.concatenate([scaled, innovation[:, None]], axis=1)
    solved = matmul_hi(neg_inv, rhs)
    correction = matmul_hi(swap_last(scaled), solved)
    cov_new = cov_pred + correction[:, :-1]
    mean_new = mean_pred - correction[:, -1]
    return mean_new, cov_new


def smoother_elements(means, covs, last_flag, transit, process):
    forward_cov = apply_trans(transit, covs)
    predicted = apply_trans(transit, swap_last(forward_cov)) + process
    neg_inv = jax.vmap(neg_inverse)(predicted)
    gains = -matmul_hi(swap_last(forward_cov), neg_inv)
    gains = gains * (1.0 - last_flag.astype(jnp.float32))[:, None, None]
    forward_mean = apply_trans(transit, means[..., None])
    shift_means = means - matmul_hi(gains, forward_mean)[..., 0]
    shift_covs = covs - matmul_hi(gains, forward_cov)
    return (gains, shift_means, shift_covs)


def smooth_join(lower_el, higher_el):
    gain_a, mean_a, cov_a = lower_el
    gain_b, mean_b, cov_b = higher_el
    return (
        matmul_hi(gain_a, gain_b),
        matmul_hi(gain_a, mean_b[..., None])[..., 0] + mean_a,
        matmul_hi(matmul_hi(gain_a, cov_b), swap_last(gain_a)) + cov_a,
    )


def send_element(element, pairs):
    gain, mean, cov = element
    width = mean.shape[-1]
    packed = jnp.concatenate([cov, jnp.broadcast_to(mean[None], (8, width))], axis=0)
    recv_gain, recv_packed = lax.ppermute((gain, packed), "tm", pairs)
    return (recv_gain, recv_packed[width], recv_packed[:width])


def shards(observed, obs_masks, decay_rates, noise_var, spatial_cov):
    transit, process, prior = build_model(decay_rates, spatial_cov)
    local_steps, points = observed.shape
    width = 2 * points
    position = lax.axis_index("tm")
    tm_count = lax.axis_size("tm")
    total_steps = tm_count * local_steps

    root_local = jnp.sqrt(obs_masks.astype(jnp.float32) / noise_var)
    packed = jnp.stack([observed, root_local], axis=1)
    gathered = lax.all_gather(packed, "tm", tiled=True)
    obs_all = gathered[:, 0]
    root_all = gathered[:, 1]

    last_local = position * local_steps + (local_steps - 1)

    def filter_step(step, mean, cov):
        mean_pred, cov_pred = predict(transit, process, mean, cov)
        obs_now = lax.dynamic_index_in_dim(obs_all, step, keepdims=False)
        root_now = lax.dynamic_index_in_dim(root_all, step, keepdims=False)
        return kalman_update(mean_pred, cov_pred, obs_now, root_now)

    if local_steps == 1:
        mean_last, cov_last = run_filter(position + 1, obs_all, root_all, transit, process, prior)
        means = mean_last
        covs = cov_last[None]
    else:
        mean_first, cov_first = kalman_update(
            jnp.zeros((width,), jnp.float32), prior, obs_all[0], root_all[0]
        )
        mean_buf = jnp.zeros((local_steps, width), jnp.float32).at[0].set(mean_first)
        cov_buf = jnp.zeros((local_steps, width, width), jnp.float32).at[0].set(cov_first)

        def body(step, carry):
            mean, cov, mean_buf, cov_buf = carry
            mean, cov = filter_step(step, mean, cov)
            slot = step % local_steps
            mean_buf = lax.dynamic_update_index_in_dim(mean_buf, mean, slot, 0)
            cov_buf = lax.dynamic_update_index_in_dim(cov_buf, cov, slot, 0)
            return (mean, cov, mean_buf, cov_buf)

        _, _, means, covs = lax.fori_loop(
            1, last_local + 1, body, (mean_first, cov_first, mean_buf, cov_buf)
        )

    global_step = position * local_steps + jnp.arange(local_steps)
    last_flag = global_step == total_steps - 1
    if local_steps == 1:

        def compute_elements(operand):
            return smoother_elements(operand[0], operand[1], last_flag, transit, process)

        def final_elements(operand):
            return (jnp.zeros_like(operand[1]), operand[0], operand[1])

        smooth = lax.cond(position == tm_count - 1, final_elements, compute_elements, (means, covs))
    else:
        smooth = smoother_elements(means, covs, last_flag, transit, process)

    if local_steps > 1:
        last_el = jax.tree.map(lambda leaf: leaf[-1], smooth)
        front_els = jax.tree.map(lambda leaf: leaf[:-1], smooth)

        def backward(running, element):
            joined = smooth_join(element, running)
            return (joined, joined)

        _, head_els = lax.scan(backward, last_el, front_els, reverse=True)
        suffixes = jax.tree.map(
            lambda head_leaf, last_leaf: jnp.concatenate([head_leaf, last_leaf[None]], axis=0),
            head_els,
            last_el,
        )
        block_total = jax.tree.map(lambda leaf: leaf[0], suffixes)
    else:
        block_total = jax.tree.map(lambda leaf: leaf[0], smooth)

    running = block_total
    shift = 1
    while shift < tm_count:
        pairs = [(source, source - shift) for source in range(shift, tm_count)]
        received = send_element(running, pairs)
        running = smooth_join(running, received)
        shift *= 2

    if local_steps == 1:
        return (running[1][None], running[2][None])
    pairs = [(source, source - 1) for source in range(1, tm_count)]
    after_mine = lax.ppermute(running, "tm", pairs)
    gains, shift_means, shift_covs = suffixes
    smooth_mean = matmul_hi(gains, after_mine[1][:, None])[..., 0] + shift_means
    smooth_cov = matmul_hi(matmul_hi(gains, after_mine[2]), swap_last(gains)) + shift_covs
    return (smooth_mean, smooth_cov)


def solution(mesh):
    placed = (
        P(("groups", "tm"), None),
        P(("groups", "tm"), None),
        P("groups"),
        P("groups"),
        P("groups", None),
    )
    return jax.shard_map(
        shards,
        mesh=mesh,
        in_specs=placed,
        out_specs=(P(("groups", "tm"), None), P(("groups", "tm"), None, None)),
        check_vma=False,
    )
```
